32 devices in a mesh: groups: 2 (over y), tensor: 8 (over z, x), dp: 2 (over core).
Axes of the slice: x: 2, y: 2, z: 4, core: 2. Of those that a mesh axis runs over, the one named last changes fastest.
Arguments:
- hidden: bfloat16 [2400, 8192], P(('groups', 'dp'), 'tensor'), parts along dimension 0, may hold values from -6 to 6
- norm_gain: float32 [8192], replicated, may hold values from 0.1 to 1.9
- query_weight: bfloat16 [8192, 8192], P('dp', 'tensor'), may hold values from -0.09375 to 0.09375
- query_keep: int32 [128, 128], P('dp', 'tensor'), may hold values 0 or 1
- kv_weight: bfloat16 [2048, 8192], P('tensor', 'dp'), may hold values from -0.0625 to 0.0625
- out_weight: bfloat16 [8192, 8192], P('tensor', 'dp'), may hold values from -0.5 to 0.5
- out_keep: int32 [128, 128], P('tensor', 'dp'), may hold values 0 or 1
- pair_lengths: int32 [4, 4], P(('groups', 'dp')), parts along dimension 0, may hold values from 1 to 300, 600 in all within a row
- premise_lengths: int32 [4, 4], P(('groups', 'dp')), parts along dimension 0, may hold values from 1 to 299
Outputs:
- attn_out: bfloat16 [2400, 8192], P(('groups', 'dp'), 'tensor'), parts along dimension 0
The draws below stay inside these ranges and needn't reach their ends.
There are 2 independent parts, one for each index of `groups`. The reference program is written for one: setup_inputs(seed, part) draws one part's arguments, and reference() takes and returns one part's arrays. A program takes and returns all parts, laid end to end along the dimension named above; an argument that names none is the same for every part. Nothing has to cross between parts.
Inputs may be any that keep to these rules, and one draw needn't show every extreme that they name: `pair_lengths`: each row lists the 4 pair lengths of one batch in order; they sum to 600.
All inputs are finite; a program needn't handle non-finite values. No bound on the sum of `query_keep` or of `out_keep` on one device may be relied on, other than what follows from the above.
Results may differ from the reference program's by a relative error of at most 0.01.
Values may be sent and summed in bfloat16 or wider, within the bound.
No kernel may reach another device: no remote copies, remote signals or barrier semaphores. Data moves between devices by JAX's collectives and lax.ppermute only.
A program may use at most 192 MiB of HBM per device.

```python
import math
import jax
import jax.numpy as jnp
import numpy as np
from jax import lax

D = 8192
HEADS = 64
KVH = 8
HD = 128
BLOCK = 64
PAIRS = 4
ROWS = 600
TOKENS = 1200
MAXLEN = 300
N_DP = 2


def set_ends(drawn, stream_key, smallest, top_value):
    dims = drawn.shape
    index_at = [jax.random.randint(jax.random.fold_in(stream_key, axis), (), 0, dims[axis]) for axis in range(len(dims))]
    drawn = drawn.at[tuple(index_at)].set(smallest)
    longest = dims.index(max(dims))
    index_at[longest] = (index_at[longest] + 1) % dims[longest]
    return drawn.at[tuple(index_at)].set(top_value)


def spiked(array, stream_key, source, target, shards_of, factor):
    owner, partner = [(jnp.arange(array.shape[dim]) // (array.shape[dim] // shards_of)).reshape([-1 if axis == dim else 1 for axis in range(array.ndim)]) for dim in (source, target)]
    chosen = jax.random.permutation(stream_key, shards_of)[partner]
    strong = (owner == chosen) | (owner == (partner + shards_of // 2) % shards_of)
    return jnp.where(strong, factor * array, array)


def block_levels(key, dims, split, least, high):
    factor_of = 1.0
    for dim, parts in split:
        heights = jax.random.uniform(jax.random.fold_in(jax.random.fold_in(key, 6), dim), (parts,), jnp.float32, least / len(split), high / len(split))
        factor_of = factor_of * jnp.repeat(jnp.exp(heights), dims[dim] // parts).reshape((-1,) + (1,) * (len(dims) - 1 - dim))
    return factor_of


def length_profile(amount, total, limit, lean):
    loads = [(1 << 20) // math.isqrt(standing ** lean) + 1 for standing in range(2, amount + 1)]
    rest, holding = total - limit - (amount - 1), [1] * (amount - 1)
    while rest > 0:
        candidates = [i for i in range(amount - 1) if holding[i] < limit]
        pool, remaining = sum([loads[i] for i in candidates]), rest
        for i in candidates:
            more = min(limit - holding[i], max(1, remaining * loads[i] // pool), rest)
            holding[i] = holding[i] + more
            rest = rest - more
    return np.array([limit] + holding)


def uneven_parts(stream_key, number_of, total, bound, slope):
    if number_of == 2:
        one = jax.random.randint(stream_key, (), max(1, total - bound), min(bound, total - 1) + 1)
        return jnp.stack([one, total - one])
    sizes = jnp.asarray(length_profile(number_of, total, bound, slope), jnp.int32)
    twos = (number_of - 1) // 2
    donor, sink = sizes[1:1 + 2 * twos:2], sizes[2:2 + 2 * twos:2]
    room = jnp.minimum(donor - 1, bound - sink)
    moved = jax.random.randint(jax.random.fold_in(stream_key, 1), (twos,), 0, 1 << 20) % (room + 1)
    sizes = sizes.at[1:1 + 2 * twos:2].set(donor - moved).at[2:2 + 2 * twos:2].set(sink + moved)
    return sizes[jax.random.permutation(jax.random.fold_in(stream_key, 2), number_of)]


def scatter_about(stream_key, dims, spread, bound, shards=(), kind=jnp.bfloat16):
    array = jax.random.normal(stream_key, dims, jnp.float32) * spread
    if len(shards) > 0:
        array = block_levels(stream_key, dims, shards, -0.22, 0.18) * array
    return jnp.clip(array, min=-bound, max=bound).astype(kind)


def noise_with(own_key, extent, spread, limit, pieces, heavy, held_as=jnp.bfloat16):
    drawn = spread * jax.random.normal(own_key, extent, jnp.float32)
    if pieces:
        drawn = drawn * block_levels(own_key, extent, pieces, -0.22, 0.18)
    return jnp.clip(spiked(drawn, jax.random.fold_in(own_key, 3), *heavy), -limit, limit).astype(held_as)


def setup_inputs(seed: int = 0, part: int = 0) -> dict:
    splits = jax.random.split(jax.random.key(seed), 10)
    own_keys = jax.random.split(jax.random.fold_in(splits[9], part), 10)
    return {
        "hidden": scatter_about(own_keys[0], (TOKENS, D), 1.0, 6.0, ((0, 2), (1, 8))),
        "norm_gain": jnp.clip(1.0 + 0.18 * jax.random.normal(splits[1], (D,), jnp.float32), 0.1, 1.9),
        "query_weight": scatter_about(splits[2], (D, D), (D // 2) ** -0.5, 0.09375, ((0, 2), (1, 8))),
        "query_keep": set_ends((jax.random.randint(splits[3], (D // BLOCK, D // BLOCK), 0, 2) < 1).astype(jnp.int32), jax.random.fold_in(splits[3], 1), 0, 1),
        "kv_weight": scatter_about(splits[4], (2 * KVH * HD, D), D ** -0.5, 0.0625, ((0, 8), (1, 2))),
        "out_weight": noise_with(splits[5], (D, D), (D // 32) ** -0.5, 0.5, ((0, 8), (1, 2)), (0, 1, 8, 2.0)),
        "out_keep": set_ends((jax.random.randint(splits[6], (D // BLOCK, D // BLOCK), 0, 2) < 1).astype(jnp.int32), jax.random.fold_in(splits[6], 1), 0, 1),
        "pair_lengths": jax.vmap(lambda own: uneven_parts(own, PAIRS, ROWS, MAXLEN, 2))(jax.random.split(own_keys[7], N_DP)).reshape((N_DP, PAIRS)).astype(jnp.int32),
        "premise_lengths": set_ends(jax.random.randint(own_keys[8], (N_DP, PAIRS), 1, MAXLEN), jax.random.fold_in(own_keys[8], 1), 1, MAXLEN - 1).astype(jnp.int32),
    }


def rotate_pairs(values, positions):
    half_width = values.shape[-1] // 2
    inverse = 500000.0 ** (-(jnp.arange(half_width, dtype=jnp.float32) * 2.0 / values.shape[-1]))
    angles = positions[:, None] * inverse[None, :]
    cosine = jnp.cos(angles)[:, None, :]
    sine_part = jnp.sin(angles)[:, None, :]
    first_half = values[..., :half_width]
    second_half = values[..., half_width:]
    return jnp.concatenate([first_half * cosine - second_half * sine_part, second_half * cosine + first_half * sine_part], axis=-1)

def pair_layout(lengths, premise, count):
    pair_ends = jnp.cumsum(lengths).astype(jnp.int32)
    pair_starts = pair_ends - lengths
    position = jnp.arange(count, dtype=jnp.int32)
    pair_index = lax.optimization_barrier(jnp.sum((position[:, None] >= pair_ends[None, :]).astype(jnp.int32), axis=1))
    one_hot = (pair_index[:, None] == jnp.arange(lengths.shape[0], dtype=jnp.int32)[None, :]).astype(jnp.int32)
    offset = position - lax.optimization_barrier(jnp.sum(one_hot * pair_starts[None, :], axis=1))
    premise_used = jnp.minimum(premise, lengths - 1)
    in_premise = offset < lax.optimization_barrier(jnp.sum(one_hot * premise_used[None, :], axis=1))
    allowed = (pair_index[:, None] == pair_index[None, :]) & (in_premise[None, :] | jnp.logical_not(in_premise)[:, None])
    return (offset.astype(jnp.float32), allowed)

def prune(weight, keep):
    blocks = weight.reshape(keep.shape[0], weight.shape[0] // keep.shape[0], keep.shape[1], weight.shape[1] // keep.shape[1])
    blocks = blocks * keep.astype(weight.dtype)[:, None, :, None]
    return blocks.reshape(weight.shape)

def reference(hidden, norm_gain, query_weight, query_keep, kv_weight, out_weight, out_keep, pair_lengths, premise_lengths):
    query_full = prune(query_weight, query_keep)
    out_full = prune(out_weight, out_keep)
    group_size = HEADS // KVH
    scale = HD ** (-0.5)
    results = []
    for member in range(N_DP):
        rows_here = hidden[member * ROWS:(member + 1) * ROWS].astype(jnp.float32)
        mean_square = lax.optimization_barrier(jnp.mean(rows_here * rows_here, axis=-1, keepdims=True))
        normed = (rows_here * lax.rsqrt(mean_square + 1e-05) * norm_gain).astype(jnp.bfloat16)
        offsets, allowed = pair_layout(pair_lengths[member], premise_lengths[member], ROWS)
        queries = jnp.dot(normed, query_full, preferred_element_type=jnp.float32).reshape(ROWS, HEADS, HD)
        queries = rotate_pairs(queries, offsets).astype(jnp.bfloat16)
        keys_values = jnp.dot(normed, kv_weight.T, preferred_element_type=jnp.float32).astype(jnp.bfloat16)
        keys = keys_values[:, :KVH * HD].reshape(ROWS, KVH, HD).astype(jnp.float32)
        keys = rotate_pairs(keys, offsets).astype(jnp.bfloat16)
        values_all = keys_values[:, KVH * HD:].reshape(ROWS, KVH, HD)
        keys = jnp.transpose(jnp.repeat(keys, group_size, axis=1), (1, 0, 2))
        values_all = jnp.transpose(jnp.repeat(values_all, group_size, axis=1), (1, 0, 2))
        queries = jnp.transpose(queries, (1, 0, 2))

        def one_head(operands):
            query_head, key_head, value_head = operands
            scores = jnp.dot(query_head.astype(jnp.float32), key_head.astype(jnp.float32).T) * scale
            weighted = jnp.where(allowed, jnp.exp(scores), 0.0)
            probs = (weighted / lax.optimization_barrier(jnp.sum(weighted, axis=-1, keepdims=True))).astype(jnp.bfloat16)
            return jnp.dot(probs.astype(jnp.float32), value_head.astype(jnp.float32)).astype(jnp.bfloat16)
        context = lax.map(one_head, (queries, keys, values_all))
        context = jnp.transpose(context, (1, 0, 2)).reshape(ROWS, D)
        results.append(jnp.dot(context, out_full, preferred_element_type=jnp.float32).astype(jnp.bfloat16))
    return jnp.concatenate(results, axis=0)
```

```python
import jax
import jax.numpy as jnp
import numpy as np
from jax import lax
from jax.sharding import PartitionSpec as P

HEADS = 64
KVH = 8
HD = 128


def rotate_pairs(values, positions):
    half_width = values.shape[-1] // 2
    inverse = 500000.0 ** (-(jnp.arange(half_width, dtype=jnp.float32) * 2.0 / values.shape[-1]))
    angles = positions[:, None] * inverse[None, :]
    cosine = jnp.cos(angles)[:, None, :]
    sine_part = jnp.sin(angles)[:, None, :]
    first_half = values[..., :half_width]
    second_half = values[..., half_width:]
    return jnp.concatenate(
        [
            first_half * cosine - second_half * sine_part,
            second_half * cosine + first_half * sine_part,
        ],
        axis=-1,
    )


def pair_layout(lengths, premise, count):
    pair_ends = jnp.cumsum(lengths)
    pair_starts = pair_ends - lengths
    position = jnp.arange(count, dtype=jnp.int32)
    pair_index = jnp.sum((position[:, None] >= pair_ends[None, :]).astype(jnp.int32), axis=1)
    one_hot = (
        pair_index[:, None] == jnp.arange(lengths.shape[0], dtype=jnp.int32)[None, :]
    ).astype(jnp.int32)
    offset = position - jnp.sum(one_hot * pair_starts[None, :], axis=1)
    premise_used = jnp.minimum(premise, lengths - 1)
    in_premise = offset < jnp.sum(one_hot * premise_used[None, :], axis=1)
    allowed = (pair_index[:, None] == pair_index[None, :]) & (
        in_premise[None, :] | jnp.logical_not(in_premise)[:, None]
    )
    return (offset.astype(jnp.float32), allowed)


def prune(weight, keep):
    blocks = weight.reshape(
        keep.shape[0],
        weight.shape[0] // keep.shape[0],
        keep.shape[1],
        weight.shape[1] // keep.shape[1],
    )
    blocks = blocks * keep.astype(weight.dtype)[:, None, :, None]
    return blocks.reshape(weight.shape)


def ring_order(z_size, x_size):
    if x_size == 1 or z_size == 1:
        return list(range(z_size * x_size))
    cycle = [(z, 0) for z in range(z_size)]
    for step, z in enumerate(range(z_size - 1, -1, -1)):
        xs = list(range(1, x_size))
        cycle += [(z, x) for x in (xs if step % 2 == 0 else xs[::-1])]
    return [z * x_size + x for z, x in cycle]


def make_fast(n, order):
    position_of = np.zeros(n, np.int32)
    for p, t in enumerate(order):
        position_of[t] = p
    order_arr = np.asarray(order, np.int32)
    to_next = [(order[i], order[(i + 1) % n]) for i in range(n)]
    to_prev = [(order[i], order[(i - 1) % n]) for i in range(n)]
    n_cw = n // 2
    n_ccw = (n - 1) // 2

    def on_device(
        hidden,
        norm_gain,
        query_weight,
        query_keep,
        kv_weight,
        out_weight,
        out_keep,
        pair_lengths,
        premise_lengths,
    ):
        tensor_rank = lax.axis_index("tensor")
        dp_rank = lax.axis_index("dp")
        pos = jnp.asarray(position_of)[tensor_rank]
        ring = jnp.asarray(order_arr)
        total_rows, feat = hidden.shape
        head_local = query_weight.shape[1] // HD
        half_rows = query_weight.shape[0]

        query_mine = prune(query_weight, query_keep)
        out_mine = prune(out_weight, out_keep)
        swap = [(0, 1), (1, 0)]
        query_other = lax.ppermute(query_mine, "dp", swap)
        kv_other = lax.ppermute(kv_weight, "dp", swap)
        out_other = lax.ppermute(out_mine, "dp", swap)

        whole = jnp.zeros((total_rows, n * feat), hidden.dtype)
        whole = lax.dynamic_update_slice(whole, hidden, (0, tensor_rank * feat))
        fwd = hidden
        for s in range(n_cw):
            fwd = lax.ppermute(fwd, "tensor", to_next)
            src = ring[(pos - s - 1) % n]
            whole = lax.dynamic_update_slice(whole, fwd, (0, src * feat))
        bwd = hidden
        for s in range(n_ccw):
            bwd = lax.ppermute(bwd, "tensor", to_prev)
            src = ring[(pos + s + 1) % n]
            whole = lax.dynamic_update_slice(whole, bwd, (0, src * feat))

        rows_float = whole.astype(jnp.float32)
        mean_square = jnp.mean(rows_float * rows_float, axis=-1, keepdims=True)
        normed = (rows_float * lax.rsqrt(mean_square + 1e-05) * norm_gain).astype(jnp.bfloat16)
        mine_cols = lax.dynamic_slice_in_dim(normed, dp_rank * half_rows, half_rows, axis=1)
        other_cols = lax.dynamic_slice_in_dim(normed, (1 - dp_rank) * half_rows, half_rows, axis=1)

        queries_raw = jnp.dot(mine_cols, query_mine, preferred_element_type=jnp.float32) + jnp.dot(
            other_cols, query_other, preferred_element_type=jnp.float32
        )
        contract = (((1,), (1,)), ((), ()))
        kv_piece = (
            lax.dot_general(mine_cols, kv_weight, contract, preferred_element_type=jnp.float32)
            + lax.dot_general(other_cols, kv_other, contract, preferred_element_type=jnp.float32)
        ).astype(jnp.bfloat16)

        low = tensor_rank < n // 2
        first = kv_piece[:, :HD]
        second = kv_piece[:, HD:]
        pairs_a = [(s, 2 * s) if s < n // 2 else (s, 2 * (s - n // 2) + 1) for s in range(n)]
        pairs_b = [(s, 2 * s + 1) if s < n // 2 else (s, 2 * (s - n // 2)) for s in range(n)]
        got_a = lax.ppermute(jnp.where(low, first, second), "tensor", pairs_a)
        got_b = lax.ppermute(jnp.where(low, second, first), "tensor", pairs_b)
        even = tensor_rank % 2 == 0
        key_head = jnp.where(even, got_a, got_b)
        value_head = jnp.where(even, got_b, got_a)

        offsets, allowed = pair_layout(pair_lengths[0], premise_lengths[0], total_rows)
        queries = rotate_pairs(queries_raw.reshape(total_rows, head_local, HD), offsets).astype(
            jnp.bfloat16
        )
        keys = rotate_pairs(key_head.astype(jnp.float32)[:, None, :], offsets)[:, 0, :].astype(
            jnp.bfloat16
        )
        scale = HD ** (-0.5)
        scores = jnp.einsum("qhd,kd->hqk", queries, keys, preferred_element_type=jnp.float32) * scale
        weighted = jnp.where(allowed[None, :, :], jnp.exp(scores), 0.0)
        probs = (weighted / jnp.sum(weighted, axis=-1, keepdims=True)).astype(jnp.bfloat16)
        context = jnp.einsum(
            "hqk,kd->qhd", probs, value_head, preferred_element_type=jnp.float32
        ).astype(jnp.bfloat16)
        context = context.reshape(total_rows, head_local * HD)

        terms_mine = jnp.dot(context, out_mine, preferred_element_type=jnp.float32)
        terms_other = jnp.dot(context, out_other, preferred_element_type=jnp.float32)
        terms = jnp.where(
            dp_rank == 0,
            jnp.concatenate([terms_mine, terms_other], axis=1),
            jnp.concatenate([terms_other, terms_mine], axis=1),
        )

        def chunk(dest_pos):
            return lax.dynamic_slice_in_dim(terms, ring[dest_pos % n] * feat, feat, axis=1)

        total = chunk(pos)
        acc = None
        for s in range(n_cw):
            part = chunk(pos + n_cw - s)
            send = part if acc is None else part + acc.astype(jnp.float32)
            acc = lax.ppermute(send.astype(jnp.bfloat16), "tensor", to_next)
        if acc is not None:
            total = total + acc.astype(jnp.float32)
        acc = None
        for s in range(n_ccw):
            part = chunk(pos - (n_ccw - s))
            send = part if acc is None else part + acc.astype(jnp.float32)
            acc = lax.ppermute(send.astype(jnp.bfloat16), "tensor", to_prev)
        if acc is not None:
            total = total + acc.astype(jnp.float32)
        return total.astype(jnp.bfloat16)

    return on_device


def generic(
    hidden,
    norm_gain,
    query_weight,
    query_keep,
    kv_weight,
    out_weight,
    out_keep,
    pair_lengths,
    premise_lengths,
):
    tensor_rank = lax.axis_index("tensor")
    total_rows = hidden.shape[0]
    head_local = query_weight.shape[1] // HD
    query_pruned = prune(query_weight, query_keep)
    out_pruned = prune(out_weight, out_keep)
    query_full = lax.all_gather(query_pruned, "dp", axis=0, tiled=True)
    kv_full, out_full = (
        lax.all_gather(kv_weight, "dp", axis=1, tiled=True),
        lax.all_gather(out_pruned, "dp", axis=1, tiled=True),
    )
    whole = lax.all_gather(hidden, "tensor", axis=1, tiled=True)
    rows_float = whole.astype(jnp.float32)
    mean_square = jnp.mean(rows_float * rows_float, axis=-1, keepdims=True)
    normed = (rows_float * lax.rsqrt(mean_square + 1e-05) * norm_gain).astype(jnp.bfloat16)
    queries_raw = jnp.dot(normed, query_full, preferred_element_type=jnp.float32)
    kv_piece = lax.dot_general(
        normed, kv_full, (((1,), (1,)), ((), ())), preferred_element_type=jnp.float32
    ).astype(jnp.bfloat16)
    kv_whole = lax.all_gather(kv_piece, "tensor", axis=1, tiled=True)
    offsets, allowed = pair_layout(pair_lengths[0], premise_lengths[0], total_rows)
    queries = rotate_pairs(queries_raw.reshape(total_rows, head_local, HD), offsets).astype(
        jnp.bfloat16
    )
    keys_all = rotate_pairs(
        kv_whole[:, : KVH * HD].reshape(total_rows, KVH, HD).astype(jnp.float32), offsets
    ).astype(jnp.bfloat16)
    values_all = kv_whole[:, KVH * HD :].reshape(total_rows, KVH, HD)
    chosen = (tensor_rank * head_local + jnp.arange(head_local, dtype=jnp.int32)) // (HEADS // KVH)
    keys_used = jnp.take(keys_all, chosen, axis=1)
    values_used = jnp.take(values_all, chosen, axis=1)
    scale = HD ** (-0.5)
    scores = (
        jnp.einsum("qhd,khd->hqk", queries, keys_used, preferred_element_type=jnp.float32) * scale
    )
    weighted = jnp.where(allowed[None, :, :], jnp.exp(scores), 0.0)
    probs = (weighted / jnp.sum(weighted, axis=-1, keepdims=True)).astype(jnp.bfloat16)
    context = jnp.einsum(
        "hqk,khd->qhd", probs, values_used, preferred_element_type=jnp.float32
    ).astype(jnp.bfloat16)
    context = context.reshape(total_rows, head_local * HD)
    terms = jnp.dot(context, out_full, preferred_element_type=jnp.float32)
    mixed = lax.psum_scatter(terms, "tensor", scatter_dimension=1, tiled=True)
    return mixed.astype(jnp.bfloat16)


def solution(mesh):
    placed = (
        P(("groups", "dp"), "tensor"),
        P(),
        P("dp", "tensor"),
        P("dp", "tensor"),
        P("tensor", "dp"),
        P("tensor", "dp"),
        P("tensor", "dp"),
        P(("groups", "dp"), None),
        P(("groups", "dp"), None),
    )
    n = mesh.shape["tensor"]
    if n == KVH and mesh.shape["dp"] == 2:
        coords = [getattr(d, "coords", None) for d in mesh.devices.reshape(-1)]
        z_size, x_size = n, 1
        if all(c is not None for c in coords):
            xs = sorted({c[0] for c in coords})
            zs = sorted({c[2] for c in coords})
            if len(xs) * len(zs) == n:
                z_size, x_size = len(zs), len(xs)
        body = make_fast(n, ring_order(z_size, x_size))
    else:
        body = generic
    return jax.shard_map(
        body,
        mesh=mesh,
        in_specs=placed,
        out_specs=P(("groups", "dp"), "tensor"),
        check_vma=False,
    )
```

```python
import jax
import jax.numpy as jnp
import numpy as np
from jax import lax
from jax.sharding import PartitionSpec as P

HEADS = 64
KVH = 8
HD = 128


def rotate_pairs(values, positions):
    half_width = values.shape[-1] // 2
    inverse = 500000.0 ** (-(jnp.arange(half_width, dtype=jnp.float32) * 2.0 / values.shape[-1]))
    angles = positions[:, None] * inverse[None, :]
    cosine = jnp.cos(angles)[:, None, :]
    sine_part = jnp.sin(angles)[:, None, :]
    first_half = values[..., :half_width]
    second_half = values[..., half_width:]
    return jnp.concatenate(
        [
            first_half * cosine - second_half * sine_part,
            second_half * cosine + first_half * sine_part,
        ],
        axis=-1,
    )


def pair_layout(lengths, premise, count):
    pair_ends = jnp.cumsum(lengths)
    pair_starts = pair_ends - lengths
    position = jnp.arange(count, dtype=jnp.int32)
    pair_index = jnp.sum((position[:, None] >= pair_ends[None, :]).astype(jnp.int32), axis=1)
    one_hot = (
        pair_index[:, None] == jnp.arange(lengths.shape[0], dtype=jnp.int32)[None, :]
    ).astype(jnp.int32)
    offset = position - jnp.sum(one_hot * pair_starts[None, :], axis=1)
    premise_used = jnp.minimum(premise, lengths - 1)
    in_premise = offset < jnp.sum(one_hot * premise_used[None, :], axis=1)
    allowed = (pair_index[:, None] == pair_index[None, :]) & (
        in_premise[None, :] | jnp.logical_not(in_premise)[:, None]
    )
    return (offset.astype(jnp.float32), allowed)


def prune(weight, keep):
    blocks = weight.reshape(
        keep.shape[0],
        weight.shape[0] // keep.shape[0],
        keep.shape[1],
        weight.shape[1] // keep.shape[1],
    )
    blocks = blocks * keep.astype(weight.dtype)[:, None, :, None]
    return blocks.reshape(weight.shape)


def ring_order(z_size, x_size):
    if x_size == 1 or z_size == 1:
        return list(range(z_size * x_size))
    cycle = [(z, 0) for z in range(z_size)]
    for step, z in enumerate(range(z_size - 1, -1, -1)):
        xs = list(range(1, x_size))
        cycle += [(z, x) for x in (xs if step % 2 == 0 else xs[::-1])]
    return [z * x_size + x for z, x in cycle]


def fast_prune(weight, keep):
    rows, cols = weight.shape
    step_r, step_c = rows // keep.shape[0], cols // keep.shape[1]
    mask = jnp.repeat(keep.astype(weight.dtype), step_c, axis=1)
    return (weight.reshape(keep.shape[0], step_r, cols) * mask[:, None, :]).reshape(rows, cols)


def make_fast(n, order):
    position_of = np.zeros(n, np.int32)
    for p, t in enumerate(order):
        position_of[t] = p
    order_arr = np.asarray(order, np.int32)
    both = ("tensor", "dp")
    ring_pairs = [(order[i] * 2, order[(i + 1) % n] * 2) for i in range(n)] + [
        (order[i] * 2 + 1, order[(i - 1) % n] * 2 + 1) for i in range(n)
    ]

    def on_device(
        hidden,
        norm_gain,
        query_weight,
        query_keep,
        kv_weight,
        out_weight,
        out_keep,
        pair_lengths,
        premise_lengths,
    ):
        tensor_rank = lax.axis_index("tensor")
        dp_rank = lax.axis_index("dp")
        pos = jnp.asarray(position_of)[tensor_rank]
        ring = jnp.asarray(order_arr)
        sign = 1 - 2 * dp_rank
        total_rows, feat = hidden.shape
        head_local = query_weight.shape[1] // HD

        swap = [(0, 1), (1, 0)]
        first = dp_rank == 0

        def full_over_dp(local, axis):
            other = lax.ppermute(local, "dp", swap)
            return jnp.where(
                first,
                jnp.concatenate([local, other], axis=axis),
                jnp.concatenate([other, local], axis=axis),
            )

        query_full = fast_prune(full_over_dp(query_weight, 0), full_over_dp(query_keep, 0))
        kv_full = full_over_dp(kv_weight, 1)
        out_full = fast_prune(full_over_dp(out_weight, 1), full_over_dp(out_keep, 1))

        whole = jnp.zeros((total_rows, n * feat), hidden.dtype)
        whole = lax.dynamic_update_slice(whole, hidden, (0, tensor_rank * feat))
        moving = hidden
        for s in range(n - 1):
            moving = lax.ppermute(moving, both, ring_pairs)
            src = ring[(pos - sign * (s + 1)) % n]
            whole = lax.dynamic_update_slice(whole, moving, (0, src * feat))

        rows_float = whole.astype(jnp.float32)
        mean_square = jnp.mean(rows_float * rows_float, axis=-1, keepdims=True)
        normed = (rows_float * lax.rsqrt(mean_square + 1e-05) * norm_gain).astype(jnp.bfloat16)
        queries_raw = jnp.dot(normed, query_full, preferred_element_type=jnp.float32)
        kv_piece = lax.dot_general(
            normed, kv_full, (((1,), (1,)), ((), ())), preferred_element_type=jnp.float32
        ).astype(jnp.bfloat16)

        low = tensor_rank < n // 2
        lo_cols = kv_piece[:, :HD]
        hi_cols = kv_piece[:, HD:]
        pairs_a = [(s, 2 * s) if s < n // 2 else (s, 2 * (s - n // 2) + 1) for s in range(n)]
        pairs_b = [(s, 2 * s + 1) if s < n // 2 else (s, 2 * (s - n // 2)) for s in range(n)]
        got_a = lax.ppermute(jnp.where(low, lo_cols, hi_cols), "tensor", pairs_a)
        got_b = lax.ppermute(jnp.where(low, hi_cols, lo_cols), "tensor", pairs_b)
        even = tensor_rank % 2 == 0
        key_head = jnp.where(even, got_a, got_b)
        value_head = jnp.where(even, got_b, got_a)

        offsets, allowed = pair_layout(pair_lengths[0], premise_lengths[0], total_rows)
        queries = rotate_pairs(queries_raw.reshape(total_rows, head_local, HD), offsets).astype(
            jnp.bfloat16
        )
        keys = rotate_pairs(key_head.astype(jnp.float32)[:, None, :], offsets)[:, 0, :].astype(
            jnp.bfloat16
        )
        scale = HD ** (-0.5)
        scores = jnp.einsum("qhd,kd->hqk", queries, keys, preferred_element_type=jnp.float32) * scale
        weighted = jnp.where(allowed[None, :, :], jnp.exp(scores), 0.0)
        probs = (weighted / jnp.sum(weighted, axis=-1, keepdims=True)).astype(jnp.bfloat16)
        context = jnp.einsum(
            "hqk,kd->qhd", probs, value_head, preferred_element_type=jnp.float32
        ).astype(jnp.bfloat16)
        context = context.reshape(total_rows, head_local * HD)

        def chunk(dest_pos):
            cols = lax.dynamic_slice_in_dim(out_full, ring[dest_pos % n] * feat, feat, axis=1)
            return jnp.dot(context, cols, preferred_element_type=jnp.float32)

        acc = None
        for s in range(n - 1):
            part = chunk(pos + sign * (n - 1 - s))
            send = part if acc is None else part + acc.astype(jnp.float32)
            acc = lax.ppermute(send.astype(jnp.bfloat16), both, ring_pairs)
        total = chunk(pos)
        if acc is not None:
            total = total + acc.astype(jnp.float32)
        return total.astype(jnp.bfloat16)

    return on_device


def generic(
    hidden,
    norm_gain,
    query_weight,
    query_keep,
    kv_weight,
    out_weight,
    out_keep,
    pair_lengths,
    premise_lengths,
):
    tensor_rank = lax.axis_index("tensor")
    total_rows = hidden.shape[0]
    head_local = query_weight.shape[1] // HD
    query_pruned = prune(query_weight, query_keep)
    out_pruned = prune(out_weight, out_keep)
    query_full = lax.all_gather(query_pruned, "dp", axis=0, tiled=True)
    kv_full, out_full = (
        lax.all_gather(kv_weight, "dp", axis=1, tiled=True),
        lax.all_gather(out_pruned, "dp", axis=1, tiled=True),
    )
    whole = lax.all_gather(hidden, "tensor", axis=1, tiled=True)
    rows_float = whole.astype(jnp.float32)
    mean_square = jnp.mean(rows_float * rows_float, axis=-1, keepdims=True)
    normed = (rows_float * lax.rsqrt(mean_square + 1e-05) * norm_gain).astype(jnp.bfloat16)
    queries_raw = jnp.dot(normed, query_full, preferred_element_type=jnp.float32)
    kv_piece = lax.dot_general(
        normed, kv_full, (((1,), (1,)), ((), ())), preferred_element_type=jnp.float32
    ).astype(jnp.bfloat16)
    kv_whole = lax.all_gather(kv_piece, "tensor", axis=1, tiled=True)
    offsets, allowed = pair_layout(pair_lengths[0], premise_lengths[0], total_rows)
    queries = rotate_pairs(queries_raw.reshape(total_rows, head_local, HD), offsets).astype(
        jnp.bfloat16
    )
    keys_all = rotate_pairs(
        kv_whole[:, : KVH * HD].reshape(total_rows, KVH, HD).astype(jnp.float32), offsets
    ).astype(jnp.bfloat16)
    values_all = kv_whole[:, KVH * HD :].reshape(total_rows, KVH, HD)
    chosen = (tensor_rank * head_local + jnp.arange(head_local, dtype=jnp.int32)) // (HEADS // KVH)
    keys_used = jnp.take(keys_all, chosen, axis=1)
    values_used = jnp.take(values_all, chosen, axis=1)
    scale = HD ** (-0.5)
    scores = (
        jnp.einsum("qhd,khd->hqk", queries, keys_used, preferred_element_type=jnp.float32) * scale
    )
    weighted = jnp.where(allowed[None, :, :], jnp.exp(scores), 0.0)
    probs = (weighted / jnp.sum(weighted, axis=-1, keepdims=True)).astype(jnp.bfloat16)
    context = jnp.einsum(
        "hqk,khd->qhd", probs, values_used, preferred_element_type=jnp.float32
    ).astype(jnp.bfloat16)
    context = context.reshape(total_rows, head_local * HD)
    terms = jnp.dot(context, out_full, preferred_element_type=jnp.float32)
    mixed = lax.psum_scatter(terms, "tensor", scatter_dimension=1, tiled=True)
    return mixed.astype(jnp.bfloat16)


def solution(mesh):
    placed = (
        P(("groups", "dp"), "tensor"),
        P(),
        P("dp", "tensor"),
        P("dp", "tensor"),
        P("tensor", "dp"),
        P("tensor", "dp"),
        P("tensor", "dp"),
        P(("groups", "dp"), None),
        P(("groups", "dp"), None),
    )
    n = mesh.shape["tensor"]
    if n == KVH and mesh.shape["dp"] == 2:
        coords = [getattr(d, "coords", None) for d in mesh.devices.reshape(-1)]
        z_size, x_size = n, 1
        if all(c is not None for c in coords):
            xs = sorted({c[0] for c in coords})
            zs = sorted({c[2] for c in coords})
            if len(xs) * len(zs) == n:
                z_size, x_size = len(zs), len(xs)
        body = make_fast(n, ring_order(z_size, x_size))
    else:
        body = generic
    return jax.shard_map(
        body,
        mesh=mesh,
        in_specs=placed,
        out_specs=P(("groups", "dp"), "tensor"),
        check_vma=False,
    )
```

```python
import jax
import jax.numpy as jnp
import numpy as np
from jax import lax
from jax.sharding import PartitionSpec as P

HEADS = 64
KVH = 8
HD = 128


def rotate_pairs(values, positions):
    half_width = values.shape[-1] // 2
    inverse = 500000.0 ** (-(jnp.arange(half_width, dtype=jnp.float32) * 2.0 / values.shape[-1]))
    angles = positions[:, None] * inverse[None, :]
    cosine = jnp.cos(angles)[:, None, :]
    sine_part = jnp.sin(angles)[:, None, :]
    first_half = values[..., :half_width]
    second_half = values[..., half_width:]
    return jnp.concatenate(
        [
            first_half * cosine - second_half * sine_part,
            second_half * cosine + first_half * sine_part,
        ],
        axis=-1,
    )


def pair_layout(lengths, premise, count):
    pair_ends = jnp.cumsum(lengths)
    pair_starts = pair_ends - lengths
    position = jnp.arange(count, dtype=jnp.int32)
    pair_index = jnp.sum((position[:, None] >= pair_ends[None, :]).astype(jnp.int32), axis=1)
    one_hot = (
        pair_index[:, None] == jnp.arange(lengths.shape[0], dtype=jnp.int32)[None, :]
    ).astype(jnp.int32)
    offset = position - jnp.sum(one_hot * pair_starts[None, :], axis=1)
    premise_used = jnp.minimum(premise, lengths - 1)
    in_premise = offset < jnp.sum(one_hot * premise_used[None, :], axis=1)
    allowed = (pair_index[:, None] == pair_index[None, :]) & (
        in_premise[None, :] | jnp.logical_not(in_premise)[:, None]
    )
    return (offset.astype(jnp.float32), allowed)


def prune(weight, keep):
    blocks = weight.reshape(
        keep.shape[0],
        weight.shape[0] // keep.shape[0],
        keep.shape[1],
        weight.shape[1] // keep.shape[1],
    )
    blocks = blocks * keep.astype(weight.dtype)[:, None, :, None]
    return blocks.reshape(weight.shape)


def ring_order(z_size, x_size):
    if x_size == 1 or z_size == 1:
        return list(range(z_size * x_size))
    cycle = [(z, 0) for z in range(z_size)]
    for step, z in enumerate(range(z_size - 1, -1, -1)):
        xs = list(range(1, x_size))
        cycle += [(z, x) for x in (xs if step % 2 == 0 else xs[::-1])]
    return [z * x_size + x for z, x in cycle]


def fast_prune(weight, keep):
    rows, cols = weight.shape
    step_r, step_c = rows // keep.shape[0], cols // keep.shape[1]
    mask = jnp.repeat(keep.astype(weight.dtype), step_c, axis=1)
    return (weight.reshape(keep.shape[0], step_r, cols) * mask[:, None, :]).reshape(rows, cols)


def make_fast(n, order):
    position_of = np.zeros(n, np.int32)
    for p, t in enumerate(order):
        position_of[t] = p
    order_arr = np.asarray(order, np.int32)
    both = ("tensor", "dp")
    ring_pairs = [(order[i] * 2, order[(i + 1) % n] * 2) for i in range(n)] + [
        (order[i] * 2 + 1, order[(i - 1) % n] * 2 + 1) for i in range(n)
    ]

    def on_device(
        hidden,
        norm_gain,
        query_weight,
        query_keep,
        kv_weight,
        out_weight,
        out_keep,
        pair_lengths,
        premise_lengths,
    ):
        tensor_rank = lax.axis_index("tensor")
        dp_rank = lax.axis_index("dp")
        pos = jnp.asarray(position_of)[tensor_rank]
        ring = jnp.asarray(order_arr)
        sign = 1 - 2 * dp_rank
        total_rows, feat = hidden.shape
        head_local = query_weight.shape[1] // HD

        query_full = lax.all_gather(fast_prune(query_weight, query_keep), "dp", axis=0, tiled=True)
        kv_full = lax.all_gather(kv_weight, "dp", axis=1, tiled=True)
        out_full = lax.all_gather(fast_prune(out_weight, out_keep), "dp", axis=1, tiled=True)

        whole = jnp.zeros((total_rows, n * feat), hidden.dtype)
        whole = lax.dynamic_update_slice(whole, hidden, (0, tensor_rank * feat))
        moving = hidden
        for s in range(n - 1):
            moving = lax.ppermute(moving, both, ring_pairs)
            src = ring[(pos - sign * (s + 1)) % n]
            whole = lax.dynamic_update_slice(whole, moving, (0, src * feat))

        rows_float = whole.astype(jnp.float32)
        mean_square = jnp.mean(rows_float * rows_float, axis=-1, keepdims=True)
        normed = (rows_float * lax.rsqrt(mean_square + 1e-05) * norm_gain).astype(jnp.bfloat16)
        queries_raw = jnp.dot(normed, query_full, preferred_element_type=jnp.float32)
        kv_piece = lax.dot_general(
            normed, kv_full, (((1,), (1,)), ((), ())), preferred_element_type=jnp.float32
        ).astype(jnp.bfloat16)

        low = tensor_rank < n // 2
        lo_cols = kv_piece[:, :HD]
        hi_cols = kv_piece[:, HD:]
        pairs_a = [(s, 2 * s) if s < n // 2 else (s, 2 * (s - n // 2) + 1) for s in range(n)]
        pairs_b = [(s, 2 * s + 1) if s < n // 2 else (s, 2 * (s - n // 2)) for s in range(n)]
        got_a = lax.ppermute(jnp.where(low, lo_cols, hi_cols), "tensor", pairs_a)
        got_b = lax.ppermute(jnp.where(low, hi_cols, lo_cols), "tensor", pairs_b)
        even = tensor_rank % 2 == 0
        key_head = jnp.where(even, got_a, got_b)
        value_head = jnp.where(even, got_b, got_a)

        offsets, allowed = pair_layout(pair_lengths[0], premise_lengths[0], total_rows)
        queries = rotate_pairs(queries_raw.reshape(total_rows, head_local, HD), offsets).astype(
            jnp.bfloat16
        )
        keys = rotate_pairs(key_head.astype(jnp.float32)[:, None, :], offsets)[:, 0, :].astype(
            jnp.bfloat16
        )
        scale = HD ** (-0.5)
        scores = jnp.einsum("qhd,kd->hqk", queries, keys, preferred_element_type=jnp.float32) * scale
        weighted = jnp.where(allowed[None, :, :], jnp.exp(scores), 0.0)
        probs = (weighted / jnp.sum(weighted, axis=-1, keepdims=True)).astype(jnp.bfloat16)
        context = jnp.einsum(
            "hqk,kd->qhd", probs, value_head, preferred_element_type=jnp.float32
        ).astype(jnp.bfloat16)
        context = context.reshape(total_rows, head_local * HD)

        def chunk(dest_pos):
            cols = lax.dynamic_slice_in_dim(out_full, ring[dest_pos % n] * feat, feat, axis=1)
            return jnp.dot(context, cols, preferred_element_type=jnp.float32)

        parts = [chunk(pos + sign * (n - 1 - s)) for s in range(n)]
        parts = [parts[0].astype(jnp.bfloat16)] + lax.optimization_barrier(parts[1:])
        acc = None
        for s in range(n - 1):
            send = parts[0] if acc is None else (parts[s] + acc.astype(jnp.float32)).astype(jnp.bfloat16)
            acc = lax.ppermute(send, both, ring_pairs)
        total = parts[n - 1]
        if acc is not None:
            total = total + acc.astype(jnp.float32)
        return total.astype(jnp.bfloat16)

    return on_device


def generic(
    hidden,
    norm_gain,
    query_weight,
    query_keep,
    kv_weight,
    out_weight,
    out_keep,
    pair_lengths,
    premise_lengths,
):
    tensor_rank = lax.axis_index("tensor")
    total_rows = hidden.shape[0]
    head_local = query_weight.shape[1] // HD
    query_pruned = prune(query_weight, query_keep)
    out_pruned = prune(out_weight, out_keep)
    query_full = lax.all_gather(query_pruned, "dp", axis=0, tiled=True)
    kv_full, out_full = (
        lax.all_gather(kv_weight, "dp", axis=1, tiled=True),
        lax.all_gather(out_pruned, "dp", axis=1, tiled=True),
    )
    whole = lax.all_gather(hidden, "tensor", axis=1, tiled=True)
    rows_float = whole.astype(jnp.float32)
    mean_square = jnp.mean(rows_float * rows_float, axis=-1, keepdims=True)
    normed = (rows_float * lax.rsqrt(mean_square + 1e-05) * norm_gain).astype(jnp.bfloat16)
    queries_raw = jnp.dot(normed, query_full, preferred_element_type=jnp.float32)
    kv_piece = lax.dot_general(
        normed, kv_full, (((1,), (1,)), ((), ())), preferred_element_type=jnp.float32
    ).astype(jnp.bfloat16)
    kv_whole = lax.all_gather(kv_piece, "tensor", axis=1, tiled=True)
    offsets, allowed = pair_layout(pair_lengths[0], premise_lengths[0], total_rows)
    queries = rotate_pairs(queries_raw.reshape(total_rows, head_local, HD), offsets).astype(
        jnp.bfloat16
    )
    keys_all = rotate_pairs(
        kv_whole[:, : KVH * HD].reshape(total_rows, KVH, HD).astype(jnp.float32), offsets
    ).astype(jnp.bfloat16)
    values_all = kv_whole[:, KVH * HD :].reshape(total_rows, KVH, HD)
    chosen = (tensor_rank * head_local + jnp.arange(head_local, dtype=jnp.int32)) // (HEADS // KVH)
    keys_used = jnp.take(keys_all, chosen, axis=1)
    values_used = jnp.take(values_all, chosen, axis=1)
    scale = HD ** (-0.5)
    scores = (
        jnp.einsum("qhd,khd->hqk", queries, keys_used, preferred_element_type=jnp.float32) * scale
    )
    weighted = jnp.where(allowed[None, :, :], jnp.exp(scores), 0.0)
    probs = (weighted / jnp.sum(weighted, axis=-1, keepdims=True)).astype(jnp.bfloat16)
    context = jnp.einsum(
        "hqk,khd->qhd", probs, values_used, preferred_element_type=jnp.float32
    ).astype(jnp.bfloat16)
    context = context.reshape(total_rows, head_local * HD)
    terms = jnp.dot(context, out_full, preferred_element_type=jnp.float32)
    mixed = lax.psum_scatter(terms, "tensor", scatter_dimension=1, tiled=True)
    return mixed.astype(jnp.bfloat16)


def solution(mesh):
    placed = (
        P(("groups", "dp"), "tensor"),
        P(),
        P("dp", "tensor"),
        P("dp", "tensor"),
        P("tensor", "dp"),
        P("tensor", "dp"),
        P("tensor", "dp"),
        P(("groups", "dp"), None),
        P(("groups", "dp"), None),
    )
    n = mesh.shape["tensor"]
    if n == KVH and mesh.shape["dp"] == 2:
        coords = [getattr(d, "coords", None) for d in mesh.devices.reshape(-1)]
        z_size, x_size = n, 1
        if all(c is not None for c in coords):
            xs = sorted({c[0] for c in coords})
            zs = sorted({c[2] for c in coords})
            if len(xs) * len(zs) == n:
                z_size, x_size = len(zs), len(xs)
        body = make_fast(n, ring_order(z_size, x_size))
    else:
        body = generic
    return jax.shard_map(
        body,
        mesh=mesh,
        in_specs=placed,
        out_specs=P(("groups", "dp"), "tensor"),
        check_vma=False,
    )
```

```python
import jax
import jax.numpy as jnp
import numpy as np
from jax import lax
from jax.sharding import PartitionSpec as P

HEADS = 64
KVH = 8
HD = 128


def rotate_pairs(values, positions):
    half_width = values.shape[-1] // 2
    inverse = 500000.0 ** (-(jnp.arange(half_width, dtype=jnp.float32) * 2.0 / values.shape[-1]))
    angles = positions[:, None] * inverse[None, :]
    cosine = jnp.cos(angles)[:, None, :]
    sine_part = jnp.sin(angles)[:, None, :]
    first_half = values[..., :half_width]
    second_half = values[..., half_width:]
    return jnp.concatenate(
        [
            first_half * cosine - second_half * sine_part,
            second_half * cosine + first_half * sine_part,
        ],
        axis=-1,
    )


def pair_layout(lengths, premise, count):
    pair_ends = jnp.cumsum(lengths)
    pair_starts = pair_ends - lengths
    position = jnp.arange(count, dtype=jnp.int32)
    pair_index = jnp.sum((position[:, None] >= pair_ends[None, :]).astype(jnp.int32), axis=1)
    one_hot = (
        pair_index[:, None] == jnp.arange(lengths.shape[0], dtype=jnp.int32)[None, :]
    ).astype(jnp.int32)
    offset = position - jnp.sum(one_hot * pair_starts[None, :], axis=1)
    premise_used = jnp.minimum(premise, lengths - 1)
    in_premise = offset < jnp.sum(one_hot * premise_used[None, :], axis=1)
    allowed = (pair_index[:, None] == pair_index[None, :]) & (
        in_premise[None, :] | jnp.logical_not(in_premise)[:, None]
    )
    return (offset.astype(jnp.float32), allowed)


def prune(weight, keep):
    blocks = weight.reshape(
        keep.shape[0],
        weight.shape[0] // keep.shape[0],
        keep.shape[1],
        weight.shape[1] // keep.shape[1],
    )
    blocks = blocks * keep.astype(weight.dtype)[:, None, :, None]
    return blocks.reshape(weight.shape)


def ring_order(z_size, x_size):
    if x_size == 1 or z_size == 1:
        return list(range(z_size * x_size))
    cycle = [(z, 0) for z in range(z_size)]
    for step, z in enumerate(range(z_size - 1, -1, -1)):
        xs = list(range(1, x_size))
        cycle += [(z, x) for x in (xs if step % 2 == 0 else xs[::-1])]
    return [z * x_size + x for z, x in cycle]


def fast_prune(weight, keep):
    rows, cols = weight.shape
    step_r, step_c = rows // keep.shape[0], cols // keep.shape[1]
    mask = jnp.repeat(keep.astype(weight.dtype), step_c, axis=1)
    return (weight.reshape(keep.shape[0], step_r, cols) * mask[:, None, :]).reshape(rows, cols)


def make_fast(n, order):
    position_of = np.zeros(n, np.int32)
    for p, t in enumerate(order):
        position_of[t] = p
    order_arr = np.asarray(order, np.int32)
    both = ("tensor", "dp")
    ring_pairs = [(order[i] * 2, order[(i + 1) % n] * 2) for i in range(n)] + [
        (order[i] * 2 + 1, order[(i - 1) % n] * 2 + 1) for i in range(n)
    ]

    def on_device(
        hidden,
        norm_gain,
        query_weight,
        query_keep,
        kv_weight,
        out_weight,
        out_keep,
        pair_lengths,
        premise_lengths,
    ):
        tensor_rank = lax.axis_index("tensor")
        dp_rank = lax.axis_index("dp")
        pos = jnp.asarray(position_of)[tensor_rank]
        ring = jnp.asarray(order_arr)
        sign = 1 - 2 * dp_rank
        total_rows, feat = hidden.shape
        head_local = query_weight.shape[1] // HD

        query_full = fast_prune(
            lax.all_gather(query_weight, "dp", axis=0, tiled=True),
            lax.all_gather(query_keep, "dp", axis=0, tiled=True),
        )
        kv_full = lax.all_gather(kv_weight, "dp", axis=1, tiled=True)
        out_full = lax.all_gather(fast_prune(out_weight, out_keep), "dp", axis=1, tiled=True)

        contract = (((1,), (1,)), ((), ()))

        def take_block(block, src, sums, q_acc, kv_acc):
            block_f = block.astype(jnp.float32)
            sums = sums + jnp.sum(block_f * block_f, axis=1, keepdims=True)
            gain = lax.dynamic_slice_in_dim(norm_gain, src * feat, feat)
            scaled = (block_f * gain).astype(jnp.bfloat16)
            q_rows = lax.dynamic_slice_in_dim(query_full, src * feat, feat, axis=0)
            kv_cols = lax.dynamic_slice_in_dim(kv_full, src * feat, feat, axis=1)
            q_acc = q_acc + jnp.dot(scaled, q_rows, preferred_element_type=jnp.float32)
            kv_acc = kv_acc + lax.dot_general(
                scaled, kv_cols, contract, preferred_element_type=jnp.float32
            )
            return sums, q_acc, kv_acc

        sums = jnp.zeros((total_rows, 1), jnp.float32)
        q_acc = jnp.zeros((total_rows, query_full.shape[1]), jnp.float32)
        kv_acc = jnp.zeros((total_rows, kv_full.shape[0]), jnp.float32)
        sums, q_acc, kv_acc = take_block(hidden, tensor_rank, sums, q_acc, kv_acc)
        moving = hidden
        for s in range(n - 1):
            moving = lax.ppermute(moving, both, ring_pairs)
            src = ring[(pos - sign * (s + 1)) % n]
            sums, q_acc, kv_acc = take_block(moving, src, sums, q_acc, kv_acc)

        inv_rms = lax.rsqrt(sums / (n * feat) + 1e-05)
        queries_raw = q_acc * inv_rms
        kv_piece = (kv_acc * inv_rms).astype(jnp.bfloat16)

        low = tensor_rank < n // 2
        lo_cols = kv_piece[:, :HD]
        hi_cols = kv_piece[:, HD:]
        pairs_a = [(s, 2 * s) if s < n // 2 else (s, 2 * (s - n // 2) + 1) for s in range(n)]
        pairs_b = [(s, 2 * s + 1) if s < n // 2 else (s, 2 * (s - n // 2)) for s in range(n)]
        got_a = lax.ppermute(jnp.where(low, lo_cols, hi_cols), "tensor", pairs_a)
        got_b = lax.ppermute(jnp.where(low, hi_cols, lo_cols), "tensor", pairs_b)
        even = tensor_rank % 2 == 0
        key_head = jnp.where(even, got_a, got_b)
        value_head = jnp.where(even, got_b, got_a)

        offsets, allowed = pair_layout(pair_lengths[0], premise_lengths[0], total_rows)
        queries = rotate_pairs(queries_raw.reshape(total_rows, head_local, HD), offsets).astype(
            jnp.bfloat16
        )
        keys = rotate_pairs(key_head.astype(jnp.float32)[:, None, :], offsets)[:, 0, :].astype(
            jnp.bfloat16
        )
        scale = HD ** (-0.5)
        scores = jnp.einsum("qhd,kd->hqk", queries, keys, preferred_element_type=jnp.float32) * scale
        weighted = jnp.where(allowed[None, :, :], jnp.exp(scores), 0.0)
        probs = (weighted / jnp.sum(weighted, axis=-1, keepdims=True)).astype(jnp.bfloat16)
        context = jnp.einsum(
            "hqk,kd->qhd", probs, value_head, preferred_element_type=jnp.float32
        ).astype(jnp.bfloat16)
        context = context.reshape(total_rows, head_local * HD)

        def chunk(dest_pos):
            cols = lax.dynamic_slice_in_dim(out_full, ring[dest_pos % n] * feat, feat, axis=1)
            return jnp.dot(context, cols, preferred_element_type=jnp.float32)

        parts = [lax.optimization_barrier(chunk(pos + sign * (n - 1 - s))) for s in range(n)]
        parts[0] = parts[0].astype(jnp.bfloat16)
        acc = None
        for s in range(n - 1):
            send = parts[0] if acc is None else (parts[s] + acc.astype(jnp.float32)).astype(jnp.bfloat16)
            acc = lax.ppermute(send, both, ring_pairs)
        total = parts[n - 1]
        if acc is not None:
            total = total + acc.astype(jnp.float32)
        return total.astype(jnp.bfloat16)

    return on_device


def generic(
    hidden,
    norm_gain,
    query_weight,
    query_keep,
    kv_weight,
    out_weight,
    out_keep,
    pair_lengths,
    premise_lengths,
):
    tensor_rank = lax.axis_index("tensor")
    total_rows = hidden.shape[0]
    head_local = query_weight.shape[1] // HD
    query_pruned = prune(query_weight, query_keep)
    out_pruned = prune(out_weight, out_keep)
    query_full = lax.all_gather(query_pruned, "dp", axis=0, tiled=True)
    kv_full, out_full = (
        lax.all_gather(kv_weight, "dp", axis=1, tiled=True),
        lax.all_gather(out_pruned, "dp", axis=1, tiled=True),
    )
    whole = lax.all_gather(hidden, "tensor", axis=1, tiled=True)
    rows_float = whole.astype(jnp.float32)
    mean_square = jnp.mean(rows_float * rows_float, axis=-1, keepdims=True)
    normed = (rows_float * lax.rsqrt(mean_square + 1e-05) * norm_gain).astype(jnp.bfloat16)
    queries_raw = jnp.dot(normed, query_full, preferred_element_type=jnp.float32)
    kv_piece = lax.dot_general(
        normed, kv_full, (((1,), (1,)), ((), ())), preferred_element_type=jnp.float32
    ).astype(jnp.bfloat16)
    kv_whole = lax.all_gather(kv_piece, "tensor", axis=1, tiled=True)
    offsets, allowed = pair_layout(pair_lengths[0], premise_lengths[0], total_rows)
    queries = rotate_pairs(queries_raw.reshape(total_rows, head_local, HD), offsets).astype(
        jnp.bfloat16
    )
    keys_all = rotate_pairs(
        kv_whole[:, : KVH * HD].reshape(total_rows, KVH, HD).astype(jnp.float32), offsets
    ).astype(jnp.bfloat16)
    values_all = kv_whole[:, KVH * HD :].reshape(total_rows, KVH, HD)
    chosen = (tensor_rank * head_local + jnp.arange(head_local, dtype=jnp.int32)) // (HEADS // KVH)
    keys_used = jnp.take(keys_all, chosen, axis=1)
    values_used = jnp.take(values_all, chosen, axis=1)
    scale = HD ** (-0.5)
    scores = (
        jnp.einsum("qhd,khd->hqk", queries, keys_used, preferred_element_type=jnp.float32) * scale
    )
    weighted = jnp.where(allowed[None, :, :], jnp.exp(scores), 0.0)
    probs = (weighted / jnp.sum(weighted, axis=-1, keepdims=True)).astype(jnp.bfloat16)
    context = jnp.einsum(
        "hqk,khd->qhd", probs, values_used, preferred_element_type=jnp.float32
    ).astype(jnp.bfloat16)
    context = context.reshape(total_rows, head_local * HD)
    terms = jnp.dot(context, out_full, preferred_element_type=jnp.float32)
    mixed = lax.psum_scatter(terms, "tensor", scatter_dimension=1, tiled=True)
    return mixed.astype(jnp.bfloat16)


def solution(mesh):
    placed = (
        P(("groups", "dp"), "tensor"),
        P(),
        P("dp", "tensor"),
        P("dp", "tensor"),
        P("tensor", "dp"),
        P("tensor", "dp"),
        P("tensor", "dp"),
        P(("groups", "dp"), None),
        P(("groups", "dp"), None),
    )
    n = mesh.shape["tensor"]
    if n == KVH and mesh.shape["dp"] == 2:
        coords = [getattr(d, "coords", None) for d in mesh.devices.reshape(-1)]
        z_size, x_size = n, 1
        if all(c is not None for c in coords):
            xs = sorted({c[0] for c in coords})
            zs = sorted({c[2] for c in coords})
            if len(xs) * len(zs) == n:
                z_size, x_size = len(zs), len(xs)
        body = make_fast(n, ring_order(z_size, x_size))
    else:
        body = generic
    return jax.shard_map(
        body,
        mesh=mesh,
        in_specs=placed,
        out_specs=P(("groups", "dp"), "tensor"),
        check_vma=False,
    )
```

```python
import jax
import jax.numpy as jnp
import numpy as np
from jax import lax
from jax.sharding import PartitionSpec as P

HEADS = 64
KVH = 8
HD = 128


def rotate_pairs(values, positions):
    half_width = values.shape[-1] // 2
    inverse = 500000.0 ** (-(jnp.arange(half_width, dtype=jnp.float32) * 2.0 / values.shape[-1]))
    angles = positions[:, None] * inverse[None, :]
    cosine = jnp.cos(angles)[:, None, :]
    sine_part = jnp.sin(angles)[:, None, :]
    first_half = values[..., :half_width]
    second_half = values[..., half_width:]
    return jnp.concatenate(
        [
            first_half * cosine - second_half * sine_part,
            second_half * cosine + first_half * sine_part,
        ],
        axis=-1,
    )


def pair_layout(lengths, premise, count):
    pair_ends = jnp.cumsum(lengths)
    pair_starts = pair_ends - lengths
    position = jnp.arange(count, dtype=jnp.int32)
    pair_index = jnp.sum((position[:, None] >= pair_ends[None, :]).astype(jnp.int32), axis=1)
    one_hot = (
        pair_index[:, None] == jnp.arange(lengths.shape[0], dtype=jnp.int32)[None, :]
    ).astype(jnp.int32)
    offset = position - jnp.sum(one_hot * pair_starts[None, :], axis=1)
    premise_used = jnp.minimum(premise, lengths - 1)
    in_premise = offset < jnp.sum(one_hot * premise_used[None, :], axis=1)
    allowed = (pair_index[:, None] == pair_index[None, :]) & (
        in_premise[None, :] | jnp.logical_not(in_premise)[:, None]
    )
    return (offset.astype(jnp.float32), allowed)


def prune(weight, keep):
    blocks = weight.reshape(
        keep.shape[0],
        weight.shape[0] // keep.shape[0],
        keep.shape[1],
        weight.shape[1] // keep.shape[1],
    )
    blocks = blocks * keep.astype(weight.dtype)[:, None, :, None]
    return blocks.reshape(weight.shape)


def ring_order(z_size, x_size):
    if x_size == 1 or z_size == 1:
        return list(range(z_size * x_size))
    cycle = [(z, 0) for z in range(z_size)]
    for step, z in enumerate(range(z_size - 1, -1, -1)):
        xs = list(range(1, x_size))
        cycle += [(z, x) for x in (xs if step % 2 == 0 else xs[::-1])]
    return [z * x_size + x for z, x in cycle]


def fast_prune(weight, keep):
    rows, cols = weight.shape
    step_r, step_c = rows // keep.shape[0], cols // keep.shape[1]
    mask = jnp.repeat(keep.astype(weight.dtype), step_c, axis=1)
    return (weight.reshape(keep.shape[0], step_r, cols) * mask[:, None, :]).reshape(rows, cols)


def make_fast(n, order):
    position_of = np.zeros(n, np.int32)
    for p, t in enumerate(order):
        position_of[t] = p
    order_arr = np.asarray(order, np.int32)
    both = ("tensor", "dp")
    ring_pairs = [(order[i] * 2, order[(i + 1) % n] * 2) for i in range(n)] + [
        (order[i] * 2 + 1, order[(i - 1) % n] * 2 + 1) for i in range(n)
    ]

    def on_device(
        hidden,
        norm_gain,
        query_weight,
        query_keep,
        kv_weight,
        out_weight,
        out_keep,
        pair_lengths,
        premise_lengths,
    ):
        tensor_rank = lax.axis_index("tensor")
        dp_rank = lax.axis_index("dp")
        pos = jnp.asarray(position_of)[tensor_rank]
        ring = jnp.asarray(order_arr)
        sign = 1 - 2 * dp_rank
        total_rows, feat = hidden.shape
        head_local = query_weight.shape[1] // HD

        query_full = lax.all_gather(fast_prune(query_weight, query_keep), "dp", axis=0, tiled=True)
        kv_full = lax.all_gather(kv_weight, "dp", axis=1, tiled=True)
        out_full = lax.all_gather(fast_prune(out_weight, out_keep), "dp", axis=1, tiled=True)

        split = (total_rows // 2 + 7) // 8 * 8
        halves = [hidden[:split], hidden[split:]]
        wholes = []
        for half in halves:
            buf = jnp.zeros((half.shape[0], n * feat), hidden.dtype)
            wholes.append(lax.dynamic_update_slice(buf, half, (0, tensor_rank * feat)))
        moving = list(halves)
        for s in range(n - 1):
            src = ring[(pos - sign * (s + 1)) % n]
            for i in range(2):
                moving[i] = lax.ppermute(moving[i], both, ring_pairs)
                wholes[i] = lax.dynamic_update_slice(wholes[i], moving[i], (0, src * feat))

        offsets, allowed = pair_layout(pair_lengths[0], premise_lengths[0], total_rows)
        low = tensor_rank < n // 2
        even = tensor_rank % 2 == 0
        pairs_a = [(s, 2 * s) if s < n // 2 else (s, 2 * (s - n // 2) + 1) for s in range(n)]
        pairs_b = [(s, 2 * s + 1) if s < n // 2 else (s, 2 * (s - n // 2)) for s in range(n)]
        contract = (((1,), (1,)), ((), ()))
        query_parts, key_parts, value_parts = [], [], []
        for i in range(2):
            rows_float = wholes[i].astype(jnp.float32)
            mean_square = jnp.mean(rows_float * rows_float, axis=-1, keepdims=True)
            normed = (rows_float * lax.rsqrt(mean_square + 1e-05) * norm_gain).astype(jnp.bfloat16)
            query_parts.append(jnp.dot(normed, query_full, preferred_element_type=jnp.float32))
            kv_piece = lax.dot_general(
                normed, kv_full, contract, preferred_element_type=jnp.float32
            ).astype(jnp.bfloat16)
            lo_cols = kv_piece[:, :HD]
            hi_cols = kv_piece[:, HD:]
            got_a = lax.ppermute(jnp.where(low, lo_cols, hi_cols), "tensor", pairs_a)
            got_b = lax.ppermute(jnp.where(low, hi_cols, lo_cols), "tensor", pairs_b)
            key_parts.append(jnp.where(even, got_a, got_b))
            value_parts.append(jnp.where(even, got_b, got_a))
        queries_raw = jnp.concatenate(query_parts, axis=0)
        key_head = jnp.concatenate(key_parts, axis=0)
        value_head = jnp.concatenate(value_parts, axis=0)

        queries = rotate_pairs(queries_raw.reshape(total_rows, head_local, HD), offsets).astype(
            jnp.bfloat16
        )
        keys = rotate_pairs(key_head.astype(jnp.float32)[:, None, :], offsets)[:, 0, :].astype(
            jnp.bfloat16
        )
        scale = HD ** (-0.5)
        starts = [0, split]
        sizes = [split, total_rows - split]

        def context_rows(i):
            q_rows = lax.slice_in_dim(queries, starts[i], starts[i] + sizes[i], axis=0)
            mask = lax.slice_in_dim(allowed, starts[i], starts[i] + sizes[i], axis=0)
            scores = jnp.einsum("qhd,kd->hqk", q_rows, keys, preferred_element_type=jnp.float32) * scale
            weighted = jnp.where(mask[None, :, :], jnp.exp(scores), 0.0)
            probs = (weighted / jnp.sum(weighted, axis=-1, keepdims=True)).astype(jnp.bfloat16)
            context = jnp.einsum(
                "hqk,kd->qhd", probs, value_head, preferred_element_type=jnp.float32
            ).astype(jnp.bfloat16)
            return context.reshape(sizes[i], head_local * HD)

        def chunk(context, dest_pos):
            cols = lax.dynamic_slice_in_dim(out_full, ring[dest_pos % n] * feat, feat, axis=1)
            return jnp.dot(context, cols, preferred_element_type=jnp.float32)

        parts = []
        for i in range(2):
            context = context_rows(i)
            mine = [chunk(context, pos + sign * (n - 1 - s)) for s in range(n)]
            parts.append([mine[0].astype(jnp.bfloat16)] + lax.optimization_barrier(mine[1:]))
        acc = [None, None]
        for s in range(n - 1):
            for i in range(2):
                if acc[i] is None:
                    send = parts[i][0]
                else:
                    send = (parts[i][s] + acc[i].astype(jnp.float32)).astype(jnp.bfloat16)
                acc[i] = lax.ppermute(send, both, ring_pairs)
        total = jnp.concatenate(
            [parts[i][n - 1] + acc[i].astype(jnp.float32) for i in range(2)], axis=0
        )
        return total.astype(jnp.bfloat16)

    return on_device


def generic(
    hidden,
    norm_gain,
    query_weight,
    query_keep,
    kv_weight,
    out_weight,
    out_keep,
    pair_lengths,
    premise_lengths,
):
    tensor_rank = lax.axis_index("tensor")
    total_rows = hidden.shape[0]
    head_local = query_weight.shape[1] // HD
    query_pruned = prune(query_weight, query_keep)
    out_pruned = prune(out_weight, out_keep)
    query_full = lax.all_gather(query_pruned, "dp", axis=0, tiled=True)
    kv_full, out_full = (
        lax.all_gather(kv_weight, "dp", axis=1, tiled=True),
        lax.all_gather(out_pruned, "dp", axis=1, tiled=True),
    )
    whole = lax.all_gather(hidden, "tensor", axis=1, tiled=True)
    rows_float = whole.astype(jnp.float32)
    mean_square = jnp.mean(rows_float * rows_float, axis=-1, keepdims=True)
    normed = (rows_float * lax.rsqrt(mean_square + 1e-05) * norm_gain).astype(jnp.bfloat16)
    queries_raw = jnp.dot(normed, query_full, preferred_element_type=jnp.float32)
    kv_piece = lax.dot_general(
        normed, kv_full, (((1,), (1,)), ((), ())), preferred_element_type=jnp.float32
    ).astype(jnp.bfloat16)
    kv_whole = lax.all_gather(kv_piece, "tensor", axis=1, tiled=True)
    offsets, allowed = pair_layout(pair_lengths[0], premise_lengths[0], total_rows)
    queries = rotate_pairs(queries_raw.reshape(total_rows, head_local, HD), offsets).astype(
        jnp.bfloat16
    )
    keys_all = rotate_pairs(
        kv_whole[:, : KVH * HD].reshape(total_rows, KVH, HD).astype(jnp.float32), offsets
    ).astype(jnp.bfloat16)
    values_all = kv_whole[:, KVH * HD :].reshape(total_rows, KVH, HD)
    chosen = (tensor_rank * head_local + jnp.arange(head_local, dtype=jnp.int32)) // (HEADS // KVH)
    keys_used = jnp.take(keys_all, chosen, axis=1)
    values_used = jnp.take(values_all, chosen, axis=1)
    scale = HD ** (-0.5)
    scores = (
        jnp.einsum("qhd,khd->hqk", queries, keys_used, preferred_element_type=jnp.float32) * scale
    )
    weighted = jnp.where(allowed[None, :, :], jnp.exp(scores), 0.0)
    probs = (weighted / jnp.sum(weighted, axis=-1, keepdims=True)).astype(jnp.bfloat16)
    context = jnp.einsum(
        "hqk,khd->qhd", probs, values_used, preferred_element_type=jnp.float32
    ).astype(jnp.bfloat16)
    context = context.reshape(total_rows, head_local * HD)
    terms = jnp.dot(context, out_full, preferred_element_type=jnp.float32)
    mixed = lax.psum_scatter(terms, "tensor", scatter_dimension=1, tiled=True)
    return mixed.astype(jnp.bfloat16)


def solution(mesh):
    placed = (
        P(("groups", "dp"), "tensor"),
        P(),
        P("dp", "tensor"),
        P("dp", "tensor"),
        P("tensor", "dp"),
        P("tensor", "dp"),
        P("tensor", "dp"),
        P(("groups", "dp"), None),
        P(("groups", "dp"), None),
    )
    n = mesh.shape["tensor"]
    if n == KVH and mesh.shape["dp"] == 2:
        coords = [getattr(d, "coords", None) for d in mesh.devices.reshape(-1)]
        z_size, x_size = n, 1
        if all(c is not None for c in coords):
            xs = sorted({c[0] for c in coords})
            zs = sorted({c[2] for c in coords})
            if len(xs) * len(zs) == n:
                z_size, x_size = len(zs), len(xs)
        body = make_fast(n, ring_order(z_size, x_size))
    else:
        body = generic
    return jax.shard_map(
        body,
        mesh=mesh,
        in_specs=placed,
        out_specs=P(("groups", "dp"), "tensor"),
        check_vma=False,
    )
```

```python
import jax
import jax.numpy as jnp
import numpy as np
from jax import lax
from jax.sharding import PartitionSpec as P

HEADS = 64
KVH = 8
HD = 128


def rotate_pairs(values, positions):
    half_width = values.shape[-1] // 2
    inverse = 500000.0 ** (-(jnp.arange(half_width, dtype=jnp.float32) * 2.0 / values.shape[-1]))
    angles = positions[:, None] * inverse[None, :]
    cosine = jnp.cos(angles)[:, None, :]
    sine_part = jnp.sin(angles)[:, None, :]
    first_half = values[..., :half_width]
    second_half = values[..., half_width:]
    return jnp.concatenate(
        [
            first_half * cosine - second_half * sine_part,
            second_half * cosine + first_half * sine_part,
        ],
        axis=-1,
    )


def pair_layout(lengths, premise, count):
    pair_ends = jnp.cumsum(lengths)
    pair_starts = pair_ends - lengths
    position = jnp.arange(count, dtype=jnp.int32)
    pair_index = jnp.sum((position[:, None] >= pair_ends[None, :]).astype(jnp.int32), axis=1)
    one_hot = (
        pair_index[:, None] == jnp.arange(lengths.shape[0], dtype=jnp.int32)[None, :]
    ).astype(jnp.int32)
    offset = position - jnp.sum(one_hot * pair_starts[None, :], axis=1)
    premise_used = jnp.minimum(premise, lengths - 1)
    in_premise = offset < jnp.sum(one_hot * premise_used[None, :], axis=1)
    allowed = (pair_index[:, None] == pair_index[None, :]) & (
        in_premise[None, :] | jnp.logical_not(in_premise)[:, None]
    )
    return (offset.astype(jnp.float32), allowed)


def prune(weight, keep):
    blocks = weight.reshape(
        keep.shape[0],
        weight.shape[0] // keep.shape[0],
        keep.shape[1],
        weight.shape[1] // keep.shape[1],
    )
    blocks = blocks * keep.astype(weight.dtype)[:, None, :, None]
    return blocks.reshape(weight.shape)


def ring_order(z_size, x_size):
    if x_size == 1 or z_size == 1:
        return list(range(z_size * x_size))
    cycle = [(z, 0) for z in range(z_size)]
    for step, z in enumerate(range(z_size - 1, -1, -1)):
        xs = list(range(1, x_size))
        cycle += [(z, x) for x in (xs if step % 2 == 0 else xs[::-1])]
    return [z * x_size + x for z, x in cycle]


def fast_prune(weight, keep):
    rows, cols = weight.shape
    step_r, step_c = rows // keep.shape[0], cols // keep.shape[1]
    mask = jnp.repeat(keep.astype(weight.dtype), step_c, axis=1)
    return (weight.reshape(keep.shape[0], step_r, cols) * mask[:, None, :]).reshape(rows, cols)


def make_fast(n, order):
    position_of = np.zeros(n, np.int32)
    for p, t in enumerate(order):
        position_of[t] = p
    order_arr = np.asarray(order, np.int32)
    both = ("tensor", "dp")
    ring_pairs = [(order[i] * 2, order[(i + 1) % n] * 2) for i in range(n)] + [
        (order[i] * 2 + 1, order[(i - 1) % n] * 2 + 1) for i in range(n)
    ]

    def on_device(
        hidden,
        norm_gain,
        query_weight,
        query_keep,
        kv_weight,
        out_weight,
        out_keep,
        pair_lengths,
        premise_lengths,
    ):
        tensor_rank = lax.axis_index("tensor")
        dp_rank = lax.axis_index("dp")
        pos = jnp.asarray(position_of)[tensor_rank]
        ring = jnp.asarray(order_arr)
        sign = 1 - 2 * dp_rank
        total_rows, feat = hidden.shape
        head_local = query_weight.shape[1] // HD

        local_f = hidden.astype(jnp.float32)
        square_sum = lax.psum(jnp.sum(local_f * local_f, axis=-1, keepdims=True), "tensor")
        inv_rms = lax.rsqrt(square_sum / (n * feat) + 1e-05)

        query_full = fast_prune(
            lax.all_gather(query_weight, "dp", axis=0, tiled=True),
            lax.all_gather(query_keep, "dp", axis=0, tiled=True),
        )
        kv_full = lax.all_gather(kv_weight, "dp", axis=1, tiled=True)
        out_full = fast_prune(
            lax.all_gather(out_weight, "dp", axis=1, tiled=True),
            lax.all_gather(out_keep, "dp", axis=1, tiled=True),
        )

        split = (total_rows // 2 + 7) // 8 * 8
        starts = [0, split]
        sizes = [split, total_rows - split]
        contract = (((1,), (1,)), ((), ()))
        q_acc, kv_acc, moving = [], [], []

        def project(i, block, src):
            scale_rows = lax.slice_in_dim(inv_rms, starts[i], starts[i] + sizes[i], axis=0)
            gain = lax.dynamic_slice_in_dim(norm_gain, src * feat, feat)
            normed = (block.astype(jnp.float32) * scale_rows * gain).astype(jnp.bfloat16)
            q_rows = lax.dynamic_slice_in_dim(query_full, src * feat, feat, axis=0)
            kv_cols = lax.dynamic_slice_in_dim(kv_full, src * feat, feat, axis=1)
            return (
                jnp.dot(normed, q_rows, preferred_element_type=jnp.float32),
                lax.dot_general(normed, kv_cols, contract, preferred_element_type=jnp.float32),
            )

        for i in range(2):
            moving.append(lax.slice_in_dim(hidden, starts[i], starts[i] + sizes[i], axis=0))
            q_part, kv_part = project(i, moving[i], tensor_rank)
            q_acc.append(q_part)
            kv_acc.append(kv_part)
        for s in range(n - 1):
            src = ring[(pos - sign * (s + 1)) % n]
            for i in range(2):
                moving[i] = lax.ppermute(moving[i], both, ring_pairs)
                q_part, kv_part = project(i, moving[i], src)
                q_acc[i] = q_acc[i] + q_part
                kv_acc[i] = kv_acc[i] + kv_part

        offsets, allowed = pair_layout(pair_lengths[0], premise_lengths[0], total_rows)
        low = tensor_rank < n // 2
        even = tensor_rank % 2 == 0
        pairs_a = [(s, 2 * s) if s < n // 2 else (s, 2 * (s - n // 2) + 1) for s in range(n)]
        pairs_b = [(s, 2 * s + 1) if s < n // 2 else (s, 2 * (s - n // 2)) for s in range(n)]
        query_parts, key_parts, value_parts = [], [], []
        for i in range(2):
            query_parts.append(q_acc[i])
            kv_piece = kv_acc[i].astype(jnp.bfloat16)
            lo_cols = kv_piece[:, :HD]
            hi_cols = kv_piece[:, HD:]
            got_a = lax.ppermute(jnp.where(low, lo_cols, hi_cols), "tensor", pairs_a)
            got_b = lax.ppermute(jnp.where(low, hi_cols, lo_cols), "tensor", pairs_b)
            key_parts.append(jnp.where(even, got_a, got_b))
            value_parts.append(jnp.where(even, got_b, got_a))
        queries_raw = jnp.concatenate(query_parts, axis=0)
        key_head = jnp.concatenate(key_parts, axis=0)
        value_head = jnp.concatenate(value_parts, axis=0)

        queries = rotate_pairs(queries_raw.reshape(total_rows, head_local, HD), offsets).astype(
            jnp.bfloat16
        )
        keys = rotate_pairs(key_head.astype(jnp.float32)[:, None, :], offsets)[:, 0, :].astype(
            jnp.bfloat16
        )
        scale = HD ** (-0.5)

        def context_rows(i):
            q_rows = lax.slice_in_dim(queries, starts[i], starts[i] + sizes[i], axis=0)
            mask = lax.slice_in_dim(allowed, starts[i], starts[i] + sizes[i], axis=0)
            scores = jnp.einsum("qhd,kd->hqk", q_rows, keys, preferred_element_type=jnp.float32) * scale
            weighted = jnp.where(mask[None, :, :], jnp.exp(scores), 0.0)
            probs = (weighted / jnp.sum(weighted, axis=-1, keepdims=True)).astype(jnp.bfloat16)
            context = jnp.einsum(
                "hqk,kd->qhd", probs, value_head, preferred_element_type=jnp.float32
            ).astype(jnp.bfloat16)
            return context.reshape(sizes[i], head_local * HD)

        def chunk(context, dest_pos):
            cols = lax.dynamic_slice_in_dim(out_full, ring[dest_pos % n] * feat, feat, axis=1)
            return jnp.dot(context, cols, preferred_element_type=jnp.float32)

        parts = []
        for i in range(2):
            context = context_rows(i)
            mine = [chunk(context, pos + sign * (n - 1 - s)) for s in range(n)]
            parts.append([mine[0].astype(jnp.bfloat16)] + lax.optimization_barrier(mine[1:]))
        acc = [None, None]
        for s in range(n - 1):
            for i in range(2):
                if acc[i] is None:
                    send = parts[i][0]
                else:
                    send = (parts[i][s] + acc[i].astype(jnp.float32)).astype(jnp.bfloat16)
                acc[i] = lax.ppermute(send, both, ring_pairs)
        total = jnp.concatenate(
            [parts[i][n - 1] + acc[i].astype(jnp.float32) for i in range(2)], axis=0
        )
        return total.astype(jnp.bfloat16)

    return on_device


def generic(
    hidden,
    norm_gain,
    query_weight,
    query_keep,
    kv_weight,
    out_weight,
    out_keep,
    pair_lengths,
    premise_lengths,
):
    tensor_rank = lax.axis_index("tensor")
    total_rows = hidden.shape[0]
    head_local = query_weight.shape[1] // HD
    query_pruned = prune(query_weight, query_keep)
    out_pruned = prune(out_weight, out_keep)
    query_full = lax.all_gather(query_pruned, "dp", axis=0, tiled=True)
    kv_full, out_full = (
        lax.all_gather(kv_weight, "dp", axis=1, tiled=True),
        lax.all_gather(out_pruned, "dp", axis=1, tiled=True),
    )
    whole = lax.all_gather(hidden, "tensor", axis=1, tiled=True)
    rows_float = whole.astype(jnp.float32)
    mean_square = jnp.mean(rows_float * rows_float, axis=-1, keepdims=True)
    normed = (rows_float * lax.rsqrt(mean_square + 1e-05) * norm_gain).astype(jnp.bfloat16)
    queries_raw = jnp.dot(normed, query_full, preferred_element_type=jnp.float32)
    kv_piece = lax.dot_general(
        normed, kv_full, (((1,), (1,)), ((), ())), preferred_element_type=jnp.float32
    ).astype(jnp.bfloat16)
    kv_whole = lax.all_gather(kv_piece, "tensor", axis=1, tiled=True)
    offsets, allowed = pair_layout(pair_lengths[0], premise_lengths[0], total_rows)
    queries = rotate_pairs(queries_raw.reshape(total_rows, head_local, HD), offsets).astype(
        jnp.bfloat16
    )
    keys_all = rotate_pairs(
        kv_whole[:, : KVH * HD].reshape(total_rows, KVH, HD).astype(jnp.float32), offsets
    ).astype(jnp.bfloat16)
    values_all = kv_whole[:, KVH * HD :].reshape(total_rows, KVH, HD)
    chosen = (tensor_rank * head_local + jnp.arange(head_local, dtype=jnp.int32)) // (HEADS // KVH)
    keys_used = jnp.take(keys_all, chosen, axis=1)
    values_used = jnp.take(values_all, chosen, axis=1)
    scale = HD ** (-0.5)
    scores = (
        jnp.einsum("qhd,khd->hqk", queries, keys_used, preferred_element_type=jnp.float32) * scale
    )
    weighted = jnp.where(allowed[None, :, :], jnp.exp(scores), 0.0)
    probs = (weighted / jnp.sum(weighted, axis=-1, keepdims=True)).astype(jnp.bfloat16)
    context = jnp.einsum(
        "hqk,khd->qhd", probs, values_used, preferred_element_type=jnp.float32
    ).astype(jnp.bfloat16)
    context = context.reshape(total_rows, head_local * HD)
    terms = jnp.dot(context, out_full, preferred_element_type=jnp.float32)
    mixed = lax.psum_scatter(terms, "tensor", scatter_dimension=1, tiled=True)
    return mixed.astype(jnp.bfloat16)


def solution(mesh):
    placed = (
        P(("groups", "dp"), "tensor"),
        P(),
        P("dp", "tensor"),
        P("dp", "tensor"),
        P("tensor", "dp"),
        P("tensor", "dp"),
        P("tensor", "dp"),
        P(("groups", "dp"), None),
        P(("groups", "dp"), None),
    )
    n = mesh.shape["tensor"]
    if n == KVH and mesh.shape["dp"] == 2:
        coords = [getattr(d, "coords", None) for d in mesh.devices.reshape(-1)]
        z_size, x_size = n, 1
        if all(c is not None for c in coords):
            xs = sorted({c[0] for c in coords})
            zs = sorted({c[2] for c in coords})
            if len(xs) * len(zs) == n:
                z_size, x_size = len(zs), len(xs)
        body = make_fast(n, ring_order(z_size, x_size))
    else:
        body = generic
    return jax.shard_map(
        body,
        mesh=mesh,
        in_specs=placed,
        out_specs=P(("groups", "dp"), "tensor"),
        check_vma=False,
    )
```

```python
import jax
import jax.numpy as jnp
import numpy as np
from jax import lax
from jax.sharding import PartitionSpec as P

HEADS = 64
KVH = 8
HD = 128


def rotate_pairs(values, positions):
    half_width = values.shape[-1] // 2
    inverse = 500000.0 ** (-(jnp.arange(half_width, dtype=jnp.float32) * 2.0 / values.shape[-1]))
    angles = positions[:, None] * inverse[None, :]
    cosine = jnp.cos(angles)[:, None, :]
    sine_part = jnp.sin(angles)[:, None, :]
    first_half = values[..., :half_width]
    second_half = values[..., half_width:]
    return jnp.concatenate(
        [
            first_half * cosine - second_half * sine_part,
            second_half * cosine + first_half * sine_part,
        ],
        axis=-1,
    )


def pair_layout(lengths, premise, count):
    pair_ends = jnp.cumsum(lengths)
    pair_starts = pair_ends - lengths
    position = jnp.arange(count, dtype=jnp.int32)
    pair_index = jnp.sum((position[:, None] >= pair_ends[None, :]).astype(jnp.int32), axis=1)
    one_hot = (
        pair_index[:, None] == jnp.arange(lengths.shape[0], dtype=jnp.int32)[None, :]
    ).astype(jnp.int32)
    offset = position - jnp.sum(one_hot * pair_starts[None, :], axis=1)
    premise_used = jnp.minimum(premise, lengths - 1)
    in_premise = offset < jnp.sum(one_hot * premise_used[None, :], axis=1)
    allowed = (pair_index[:, None] == pair_index[None, :]) & (
        in_premise[None, :] | jnp.logical_not(in_premise)[:, None]
    )
    return (offset.astype(jnp.float32), allowed)


def prune(weight, keep):
    blocks = weight.reshape(
        keep.shape[0],
        weight.shape[0] // keep.shape[0],
        keep.shape[1],
        weight.shape[1] // keep.shape[1],
    )
    blocks = blocks * keep.astype(weight.dtype)[:, None, :, None]
    return blocks.reshape(weight.shape)


def ring_order(z_size, x_size):
    if x_size == 1 or z_size == 1:
        return list(range(z_size * x_size))
    cycle = [(z, 0) for z in range(z_size)]
    for step, z in enumerate(range(z_size - 1, -1, -1)):
        xs = list(range(1, x_size))
        cycle += [(z, x) for x in (xs if step % 2 == 0 else xs[::-1])]
    return [z * x_size + x for z, x in cycle]


def fast_prune(weight, keep):
    rows, cols = weight.shape
    step_r, step_c = rows // keep.shape[0], cols // keep.shape[1]
    mask = jnp.repeat(keep.astype(weight.dtype), step_c, axis=1)
    return (weight.reshape(keep.shape[0], step_r, cols) * mask[:, None, :]).reshape(rows, cols)


def make_fast(n, order):
    position_of = np.zeros(n, np.int32)
    for p, t in enumerate(order):
        position_of[t] = p
    order_arr = np.asarray(order, np.int32)
    both = ("tensor", "dp")
    ring_pairs = [(order[i] * 2, order[(i + 1) % n] * 2) for i in range(n)] + [
        (order[i] * 2 + 1, order[(i - 1) % n] * 2 + 1) for i in range(n)
    ]

    def on_device(
        hidden,
        norm_gain,
        query_weight,
        query_keep,
        kv_weight,
        out_weight,
        out_keep,
        pair_lengths,
        premise_lengths,
    ):
        tensor_rank = lax.axis_index("tensor")
        dp_rank = lax.axis_index("dp")
        pos = jnp.asarray(position_of)[tensor_rank]
        ring = jnp.asarray(order_arr)
        sign = 1 - 2 * dp_rank
        total_rows, feat = hidden.shape
        head_local = query_weight.shape[1] // HD

        split = (total_rows // 2 + 7) // 8 * 8
        moving = [hidden[:split], hidden[split:]]
        arrived = [[], []]
        for s in range(n - 1):
            for i in range(2):
                moving[i] = lax.ppermute(moving[i], both, ring_pairs)
                arrived[i].append(moving[i])
            if s == 0:
                query_weight, out_weight, arrived[0][0], arrived[1][0] = lax.optimization_barrier(
                    (query_weight, out_weight, arrived[0][0], arrived[1][0])
                )
                query_full = lax.all_gather(
                    fast_prune(query_weight, query_keep), "dp", axis=0, tiled=True
                )
                kv_full = lax.all_gather(kv_weight, "dp", axis=1, tiled=True)
                out_full = lax.all_gather(fast_prune(out_weight, out_keep), "dp", axis=1, tiled=True)
        wholes = []
        for i, half in enumerate([hidden[:split], hidden[split:]]):
            buf = jnp.zeros((half.shape[0], n * feat), hidden.dtype)
            buf = lax.dynamic_update_slice(buf, half, (0, tensor_rank * feat))
            for s in range(n - 1):
                src = ring[(pos - sign * (s + 1)) % n]
                buf = lax.dynamic_update_slice(buf, arrived[i][s], (0, src * feat))
            wholes.append(buf)

        offsets, allowed = pair_layout(pair_lengths[0], premise_lengths[0], total_rows)
        low = tensor_rank < n // 2
        even = tensor_rank % 2 == 0
        pairs_a = [(s, 2 * s) if s < n // 2 else (s, 2 * (s - n // 2) + 1) for s in range(n)]
        pairs_b = [(s, 2 * s + 1) if s < n // 2 else (s, 2 * (s - n // 2)) for s in range(n)]
        contract = (((1,), (1,)), ((), ()))
        query_parts, key_parts, value_parts = [], [], []
        for i in range(2):
            rows_float = wholes[i].astype(jnp.float32)
            mean_square = jnp.mean(rows_float * rows_float, axis=-1, keepdims=True)
            normed = (rows_float * lax.rsqrt(mean_square + 1e-05) * norm_gain).astype(jnp.bfloat16)
            query_parts.append(jnp.dot(normed, query_full, preferred_element_type=jnp.float32))
            kv_piece = lax.dot_general(
                normed, kv_full, contract, preferred_element_type=jnp.float32
            ).astype(jnp.bfloat16)
            lo_cols = kv_piece[:, :HD]
            hi_cols = kv_piece[:, HD:]
            got_a = lax.ppermute(jnp.where(low, lo_cols, hi_cols), "tensor", pairs_a)
            got_b = lax.ppermute(jnp.where(low, hi_cols, lo_cols), "tensor", pairs_b)
            key_parts.append(jnp.where(even, got_a, got_b))
            value_parts.append(jnp.where(even, got_b, got_a))
        queries_raw = jnp.concatenate(query_parts, axis=0)
        key_head = jnp.concatenate(key_parts, axis=0)
        value_head = jnp.concatenate(value_parts, axis=0)

        queries = rotate_pairs(queries_raw.reshape(total_rows, head_local, HD), offsets).astype(
            jnp.bfloat16
        )
        keys = rotate_pairs(key_head.astype(jnp.float32)[:, None, :], offsets)[:, 0, :].astype(
            jnp.bfloat16
        )
        scale = HD ** (-0.5)
        starts = [0, split]
        sizes = [split, total_rows - split]

        def context_rows(i):
            q_rows = lax.slice_in_dim(queries, starts[i], starts[i] + sizes[i], axis=0)
            mask = lax.slice_in_dim(allowed, starts[i], starts[i] + sizes[i], axis=0)
            scores = jnp.einsum("qhd,kd->hqk", q_rows, keys, preferred_element_type=jnp.float32) * scale
            weighted = jnp.where(mask[None, :, :], jnp.exp(scores), 0.0)
            probs = (weighted / jnp.sum(weighted, axis=-1, keepdims=True)).astype(jnp.bfloat16)
            context = jnp.einsum(
                "hqk,kd->qhd", probs, value_head, preferred_element_type=jnp.float32
            ).astype(jnp.bfloat16)
            return context.reshape(sizes[i], head_local * HD)

        def chunk(context, dest_pos):
            cols = lax.dynamic_slice_in_dim(out_full, ring[dest_pos % n] * feat, feat, axis=1)
            return jnp.dot(context, cols, preferred_element_type=jnp.float32)

        parts = []
        for i in range(2):
            context = context_rows(i)
            mine = [chunk(context, pos + sign * (n - 1 - s)) for s in range(n)]
            parts.append([mine[0].astype(jnp.bfloat16)] + lax.optimization_barrier(mine[1:]))
        acc = [None, None]
        for s in range(n - 1):
            for i in range(2):
                if acc[i] is None:
                    send = parts[i][0]
                else:
                    send = (parts[i][s] + acc[i].astype(jnp.float32)).astype(jnp.bfloat16)
                acc[i] = lax.ppermute(send, both, ring_pairs)
        total = jnp.concatenate(
            [parts[i][n - 1] + acc[i].astype(jnp.float32) for i in range(2)], axis=0
        )
        return total.astype(jnp.bfloat16)

    return on_device


def generic(
    hidden,
    norm_gain,
    query_weight,
    query_keep,
    kv_weight,
    out_weight,
    out_keep,
    pair_lengths,
    premise_lengths,
):
    tensor_rank = lax.axis_index("tensor")
    total_rows = hidden.shape[0]
    head_local = query_weight.shape[1] // HD
    query_pruned = prune(query_weight, query_keep)
    out_pruned = prune(out_weight, out_keep)
    query_full = lax.all_gather(query_pruned, "dp", axis=0, tiled=True)
    kv_full, out_full = (
        lax.all_gather(kv_weight, "dp", axis=1, tiled=True),
        lax.all_gather(out_pruned, "dp", axis=1, tiled=True),
    )
    whole = lax.all_gather(hidden, "tensor", axis=1, tiled=True)
    rows_float = whole.astype(jnp.float32)
    mean_square = jnp.mean(rows_float * rows_float, axis=-1, keepdims=True)
    normed = (rows_float * lax.rsqrt(mean_square + 1e-05) * norm_gain).astype(jnp.bfloat16)
    queries_raw = jnp.dot(normed, query_full, preferred_element_type=jnp.float32)
    kv_piece = lax.dot_general(
        normed, kv_full, (((1,), (1,)), ((), ())), preferred_element_type=jnp.float32
    ).astype(jnp.bfloat16)
    kv_whole = lax.all_gather(kv_piece, "tensor", axis=1, tiled=True)
    offsets, allowed = pair_layout(pair_lengths[0], premise_lengths[0], total_rows)
    queries = rotate_pairs(queries_raw.reshape(total_rows, head_local, HD), offsets).astype(
        jnp.bfloat16
    )
    keys_all = rotate_pairs(
        kv_whole[:, : KVH * HD].reshape(total_rows, KVH, HD).astype(jnp.float32), offsets
    ).astype(jnp.bfloat16)
    values_all = kv_whole[:, KVH * HD :].reshape(total_rows, KVH, HD)
    chosen = (tensor_rank * head_local + jnp.arange(head_local, dtype=jnp.int32)) // (HEADS // KVH)
    keys_used = jnp.take(keys_all, chosen, axis=1)
    values_used = jnp.take(values_all, chosen, axis=1)
    scale = HD ** (-0.5)
    scores = (
        jnp.einsum("qhd,khd->hqk", queries, keys_used, preferred_element_type=jnp.float32) * scale
    )
    weighted = jnp.where(allowed[None, :, :], jnp.exp(scores), 0.0)
    probs = (weighted / jnp.sum(weighted, axis=-1, keepdims=True)).astype(jnp.bfloat16)
    context = jnp.einsum(
        "hqk,khd->qhd", probs, values_used, preferred_element_type=jnp.float32
    ).astype(jnp.bfloat16)
    context = context.reshape(total_rows, head_local * HD)
    terms = jnp.dot(context, out_full, preferred_element_type=jnp.float32)
    mixed = lax.psum_scatter(terms, "tensor", scatter_dimension=1, tiled=True)
    return mixed.astype(jnp.bfloat16)


def solution(mesh):
    placed = (
        P(("groups", "dp"), "tensor"),
        P(),
        P("dp", "tensor"),
        P("dp", "tensor"),
        P("tensor", "dp"),
        P("tensor", "dp"),
        P("tensor", "dp"),
        P(("groups", "dp"), None),
        P(("groups", "dp"), None),
    )
    n = mesh.shape["tensor"]
    if n == KVH and mesh.shape["dp"] == 2:
        coords = [getattr(d, "coords", None) for d in mesh.devices.reshape(-1)]
        z_size, x_size = n, 1
        if all(c is not None for c in coords):
            xs = sorted({c[0] for c in coords})
            zs = sorted({c[2] for c in coords})
            if len(xs) * len(zs) == n:
                z_size, x_size = len(zs), len(xs)
        body = make_fast(n, ring_order(z_size, x_size))
    else:
        body = generic
    return jax.shard_map(
        body,
        mesh=mesh,
        in_specs=placed,
        out_specs=P(("groups", "dp"), "tensor"),
        check_vma=False,
    )
```

```python
import jax
import jax.numpy as jnp
import numpy as np
from jax import lax
from jax.sharding import PartitionSpec as P

HEADS = 64
KVH = 8
HD = 128


def rotate_pairs(values, positions):
    half_width = values.shape[-1] // 2
    inverse = 500000.0 ** (-(jnp.arange(half_width, dtype=jnp.float32) * 2.0 / values.shape[-1]))
    angles = positions[:, None] * inverse[None, :]
    cosine = jnp.cos(angles)[:, None, :]
    sine_part = jnp.sin(angles)[:, None, :]
    first_half = values[..., :half_width]
    second_half = values[..., half_width:]
    return jnp.concatenate(
        [
            first_half * cosine - second_half * sine_part,
            second_half * cosine + first_half * sine_part,
        ],
        axis=-1,
    )


def pair_layout(lengths, premise, count):
    pair_ends = jnp.cumsum(lengths)
    pair_starts = pair_ends - lengths
    position = jnp.arange(count, dtype=jnp.int32)
    pair_index = jnp.sum((position[:, None] >= pair_ends[None, :]).astype(jnp.int32), axis=1)
    one_hot = (
        pair_index[:, None] == jnp.arange(lengths.shape[0], dtype=jnp.int32)[None, :]
    ).astype(jnp.int32)
    offset = position - jnp.sum(one_hot * pair_starts[None, :], axis=1)
    premise_used = jnp.minimum(premise, lengths - 1)
    in_premise = offset < jnp.sum(one_hot * premise_used[None, :], axis=1)
    allowed = (pair_index[:, None] == pair_index[None, :]) & (
        in_premise[None, :] | jnp.logical_not(in_premise)[:, None]
    )
    return (offset.astype(jnp.float32), allowed)


def prune(weight, keep):
    blocks = weight.reshape(
        keep.shape[0],
        weight.shape[0] // keep.shape[0],
        keep.shape[1],
        weight.shape[1] // keep.shape[1],
    )
    blocks = blocks * keep.astype(weight.dtype)[:, None, :, None]
    return blocks.reshape(weight.shape)


def ring_order(z_size, x_size):
    if x_size == 1 or z_size == 1:
        return list(range(z_size * x_size))
    cycle = [(z, 0) for z in range(z_size)]
    for step, z in enumerate(range(z_size - 1, -1, -1)):
        xs = list(range(1, x_size))
        cycle += [(z, x) for x in (xs if step % 2 == 0 else xs[::-1])]
    return [z * x_size + x for z, x in cycle]


def fast_prune(weight, keep):
    rows, cols = weight.shape
    step_r, step_c = rows // keep.shape[0], cols // keep.shape[1]
    mask = jnp.repeat(keep.astype(weight.dtype), step_c, axis=1)
    return (weight.reshape(keep.shape[0], step_r, cols) * mask[:, None, :]).reshape(rows, cols)


def make_fast(n, order):
    position_of = np.zeros(n, np.int32)
    for p, t in enumerate(order):
        position_of[t] = p
    order_arr = np.asarray(order, np.int32)
    both = ("tensor", "dp")
    ring_pairs = [(order[i] * 2, order[(i + 1) % n] * 2) for i in range(n)] + [
        (order[i] * 2 + 1, order[(i - 1) % n] * 2 + 1) for i in range(n)
    ]

    def on_device(
        hidden,
        norm_gain,
        query_weight,
        query_keep,
        kv_weight,
        out_weight,
        out_keep,
        pair_lengths,
        premise_lengths,
    ):
        tensor_rank = lax.axis_index("tensor")
        dp_rank = lax.axis_index("dp")
        pos = jnp.asarray(position_of)[tensor_rank]
        ring = jnp.asarray(order_arr)
        sign = 1 - 2 * dp_rank
        total_rows, feat = hidden.shape
        head_local = query_weight.shape[1] // HD

        query_full = fast_prune(
            lax.all_gather(query_weight, "dp", axis=0, tiled=True),
            lax.all_gather(query_keep, "dp", axis=0, tiled=True),
        )
        kv_full = lax.all_gather(kv_weight, "dp", axis=1, tiled=True)
        out_full = fast_prune(
            lax.all_gather(out_weight, "dp", axis=1, tiled=True),
            lax.all_gather(out_keep, "dp", axis=1, tiled=True),
        )

        split = (total_rows // 2 + 7) // 8 * 8
        halves = [hidden[:split], hidden[split:]]
        wholes = []
        for half in halves:
            buf = jnp.zeros((half.shape[0], n * feat), hidden.dtype)
            wholes.append(lax.dynamic_update_slice(buf, half, (0, tensor_rank * feat)))
        moving = list(halves)
        for s in range(n - 1):
            src = ring[(pos - sign * (s + 1)) % n]
            for i in range(2):
                moving[i] = lax.ppermute(moving[i], both, ring_pairs)
                wholes[i] = lax.dynamic_update_slice(wholes[i], moving[i], (0, src * feat))

        offsets, allowed = pair_layout(pair_lengths[0], premise_lengths[0], total_rows)
        low = tensor_rank < n // 2
        even = tensor_rank % 2 == 0
        pairs_a = [(s, 2 * s) if s < n // 2 else (s, 2 * (s - n // 2) + 1) for s in range(n)]
        pairs_b = [(s, 2 * s + 1) if s < n // 2 else (s, 2 * (s - n // 2)) for s in range(n)]
        contract = (((1,), (1,)), ((), ()))
        query_parts, key_parts, value_parts = [], [], []
        for i in range(2):
            rows_float = wholes[i].astype(jnp.float32)
            mean_square = jnp.mean(rows_float * rows_float, axis=-1, keepdims=True)
            normed = (rows_float * lax.rsqrt(mean_square + 1e-05) * norm_gain).astype(jnp.bfloat16)
            query_parts.append(jnp.dot(normed, query_full, preferred_element_type=jnp.float32))
            kv_piece = lax.dot_general(
                normed, kv_full, contract, preferred_element_type=jnp.float32
            ).astype(jnp.bfloat16)
            lo_cols = kv_piece[:, :HD]
            hi_cols = kv_piece[:, HD:]
            got_a = lax.ppermute(jnp.where(low, lo_cols, hi_cols), "tensor", pairs_a)
            got_b = lax.ppermute(jnp.where(low, hi_cols, lo_cols), "tensor", pairs_b)
            key_parts.append(jnp.where(even, got_a, got_b))
            value_parts.append(jnp.where(even, got_b, got_a))
        queries_raw = jnp.concatenate(query_parts, axis=0)
        key_head = jnp.concatenate(key_parts, axis=0)
        value_head = jnp.concatenate(value_parts, axis=0)

        queries = rotate_pairs(queries_raw.reshape(total_rows, head_local, HD), offsets).astype(
            jnp.bfloat16
        )
        keys = rotate_pairs(key_head.astype(jnp.float32)[:, None, :], offsets)[:, 0, :].astype(
            jnp.bfloat16
        )
        scale = HD ** (-0.5)
        starts = [0, split]
        sizes = [split, total_rows - split]

        def context_rows(i):
            q_rows = lax.slice_in_dim(queries, starts[i], starts[i] + sizes[i], axis=0)
            mask = lax.slice_in_dim(allowed, starts[i], starts[i] + sizes[i], axis=0)
            scores = jnp.einsum("qhd,kd->hqk", q_rows, keys, preferred_element_type=jnp.float32) * scale
            weighted = jnp.where(mask[None, :, :], jnp.exp(scores), 0.0)
            probs = (weighted / jnp.sum(weighted, axis=-1, keepdims=True)).astype(jnp.bfloat16)
            context = jnp.einsum(
                "hqk,kd->qhd", probs, value_head, preferred_element_type=jnp.float32
            ).astype(jnp.bfloat16)
            return context.reshape(sizes[i], head_local * HD)

        def chunk(context, dest_pos):
            cols = lax.dynamic_slice_in_dim(out_full, ring[dest_pos % n] * feat, feat, axis=1)
            return jnp.dot(context, cols, preferred_element_type=jnp.float32)

        parts = []
        for i in range(2):
            context = context_rows(i)
            mine = [chunk(context, pos + sign * (n - 1 - s)) for s in range(n)]
            parts.append([mine[0].astype(jnp.bfloat16)] + lax.optimization_barrier(mine[1:]))
        acc = [None, None]
        for s in range(n - 1):
            for i in range(2):
                if acc[i] is None:
                    send = parts[i][0]
                else:
                    send = (parts[i][s] + acc[i].astype(jnp.float32)).astype(jnp.bfloat16)
                acc[i] = lax.ppermute(send, both, ring_pairs)
        total = jnp.concatenate(
            [parts[i][n - 1] + acc[i].astype(jnp.float32) for i in range(2)], axis=0
        )
        return total.astype(jnp.bfloat16)

    return on_device


def generic(
    hidden,
    norm_gain,
    query_weight,
    query_keep,
    kv_weight,
    out_weight,
    out_keep,
    pair_lengths,
    premise_lengths,
):
    tensor_rank = lax.axis_index("tensor")
    total_rows = hidden.shape[0]
    head_local = query_weight.shape[1] // HD
    query_pruned = prune(query_weight, query_keep)
    out_pruned = prune(out_weight, out_keep)
    query_full = lax.all_gather(query_pruned, "dp", axis=0, tiled=True)
    kv_full, out_full = (
        lax.all_gather(kv_weight, "dp", axis=1, tiled=True),
        lax.all_gather(out_pruned, "dp", axis=1, tiled=True),
    )
    whole = lax.all_gather(hidden, "tensor", axis=1, tiled=True)
    rows_float = whole.astype(jnp.float32)
    mean_square = jnp.mean(rows_float * rows_float, axis=-1, keepdims=True)
    normed = (rows_float * lax.rsqrt(mean_square + 1e-05) * norm_gain).astype(jnp.bfloat16)
    queries_raw = jnp.dot(normed, query_full, preferred_element_type=jnp.float32)
    kv_piece = lax.dot_general(
        normed, kv_full, (((1,), (1,)), ((), ())), preferred_element_type=jnp.float32
    ).astype(jnp.bfloat16)
    kv_whole = lax.all_gather(kv_piece, "tensor", axis=1, tiled=True)
    offsets, allowed = pair_layout(pair_lengths[0], premise_lengths[0], total_rows)
    queries = rotate_pairs(queries_raw.reshape(total_rows, head_local, HD), offsets).astype(
        jnp.bfloat16
    )
    keys_all = rotate_pairs(
        kv_whole[:, : KVH * HD].reshape(total_rows, KVH, HD).astype(jnp.float32), offsets
    ).astype(jnp.bfloat16)
    values_all = kv_whole[:, KVH * HD :].reshape(total_rows, KVH, HD)
    chosen = (tensor_rank * head_local + jnp.arange(head_local, dtype=jnp.int32)) // (HEADS // KVH)
    keys_used = jnp.take(keys_all, chosen, axis=1)
    values_used = jnp.take(values_all, chosen, axis=1)
    scale = HD ** (-0.5)
    scores = (
        jnp.einsum("qhd,khd->hqk", queries, keys_used, preferred_element_type=jnp.float32) * scale
    )
    weighted = jnp.where(allowed[None, :, :], jnp.exp(scores), 0.0)
    probs = (weighted / jnp.sum(weighted, axis=-1, keepdims=True)).astype(jnp.bfloat16)
    context = jnp.einsum(
        "hqk,khd->qhd", probs, values_used, preferred_element_type=jnp.float32
    ).astype(jnp.bfloat16)
    context = context.reshape(total_rows, head_local * HD)
    terms = jnp.dot(context, out_full, preferred_element_type=jnp.float32)
    mixed = lax.psum_scatter(terms, "tensor", scatter_dimension=1, tiled=True)
    return mixed.astype(jnp.bfloat16)


def solution(mesh):
    placed = (
        P(("groups", "dp"), "tensor"),
        P(),
        P("dp", "tensor"),
        P("dp", "tensor"),
        P("tensor", "dp"),
        P("tensor", "dp"),
        P("tensor", "dp"),
        P(("groups", "dp"), None),
        P(("groups", "dp"), None),
    )
    n = mesh.shape["tensor"]
    if n == KVH and mesh.shape["dp"] == 2:
        coords = [getattr(d, "coords", None) for d in mesh.devices.reshape(-1)]
        z_size, x_size = n, 1
        if all(c is not None for c in coords):
            xs = sorted({c[0] for c in coords})
            zs = sorted({c[2] for c in coords})
            if len(xs) * len(zs) == n:
                z_size, x_size = len(zs), len(xs)
        body = make_fast(n, ring_order(z_size, x_size))
    else:
        body = generic
    return jax.shard_map(
        body,
        mesh=mesh,
        in_specs=placed,
        out_specs=P(("groups", "dp"), "tensor"),
        check_vma=False,
    )
```

```python
import jax
import jax.numpy as jnp
import numpy as np
from jax import lax
from jax.sharding import PartitionSpec as P

HEADS = 64
KVH = 8
HD = 128


def rotate_pairs(values, positions):
    half_width = values.shape[-1] // 2
    inverse = 500000.0 ** (-(jnp.arange(half_width, dtype=jnp.float32) * 2.0 / values.shape[-1]))
    angles = positions[:, None] * inverse[None, :]
    cosine = jnp.cos(angles)[:, None, :]
    sine_part = jnp.sin(angles)[:, None, :]
    first_half = values[..., :half_width]
    second_half = values[..., half_width:]
    return jnp.concatenate(
        [
            first_half * cosine - second_half * sine_part,
            second_half * cosine + first_half * sine_part,
        ],
        axis=-1,
    )


def pair_layout(lengths, premise, count):
    pair_ends = jnp.cumsum(lengths)
    pair_starts = pair_ends - lengths
    position = jnp.arange(count, dtype=jnp.int32)
    pair_index = jnp.sum((position[:, None] >= pair_ends[None, :]).astype(jnp.int32), axis=1)
    one_hot = (
        pair_index[:, None] == jnp.arange(lengths.shape[0], dtype=jnp.int32)[None, :]
    ).astype(jnp.int32)
    offset = position - jnp.sum(one_hot * pair_starts[None, :], axis=1)
    premise_used = jnp.minimum(premise, lengths - 1)
    in_premise = offset < jnp.sum(one_hot * premise_used[None, :], axis=1)
    allowed = (pair_index[:, None] == pair_index[None, :]) & (
        in_premise[None, :] | jnp.logical_not(in_premise)[:, None]
    )
    return (offset.astype(jnp.float32), allowed)


def prune(weight, keep):
    blocks = weight.reshape(
        keep.shape[0],
        weight.shape[0] // keep.shape[0],
        keep.shape[1],
        weight.shape[1] // keep.shape[1],
    )
    blocks = blocks * keep.astype(weight.dtype)[:, None, :, None]
    return blocks.reshape(weight.shape)


def ring_order(z_size, x_size):
    if x_size == 1 or z_size == 1:
        return list(range(z_size * x_size))
    cycle = [(z, 0) for z in range(z_size)]
    for step, z in enumerate(range(z_size - 1, -1, -1)):
        xs = list(range(1, x_size))
        cycle += [(z, x) for x in (xs if step % 2 == 0 else xs[::-1])]
    return [z * x_size + x for z, x in cycle]


def fast_prune(weight, keep):
    rows, cols = weight.shape
    step_r, step_c = rows // keep.shape[0], cols // keep.shape[1]
    mask = jnp.repeat(keep.astype(weight.dtype), step_c, axis=1)
    return (weight.reshape(keep.shape[0], step_r, cols) * mask[:, None, :]).reshape(rows, cols)


def make_fast(n, order):
    position_of = np.zeros(n, np.int32)
    for p, t in enumerate(order):
        position_of[t] = p
    order_arr = np.asarray(order, np.int32)
    both = ("tensor", "dp")
    ring_pairs = [(order[i] * 2, order[(i + 1) % n] * 2) for i in range(n)] + [
        (order[i] * 2 + 1, order[(i - 1) % n] * 2 + 1) for i in range(n)
    ]

    def on_device(
        hidden,
        norm_gain,
        query_weight,
        query_keep,
        kv_weight,
        out_weight,
        out_keep,
        pair_lengths,
        premise_lengths,
    ):
        tensor_rank = lax.axis_index("tensor")
        dp_rank = lax.axis_index("dp")
        pos = jnp.asarray(position_of)[tensor_rank]
        ring = jnp.asarray(order_arr)
        sign = 1 - 2 * dp_rank
        total_rows, feat = hidden.shape
        head_local = query_weight.shape[1] // HD

        query_full = fast_prune(
            lax.all_gather(query_weight, "dp", axis=0, tiled=True),
            lax.all_gather(query_keep, "dp", axis=0, tiled=True),
        )
        kv_full = lax.all_gather(kv_weight, "dp", axis=1, tiled=True)
        out_full = fast_prune(
            lax.all_gather(out_weight, "dp", axis=1, tiled=True),
            lax.all_gather(out_keep, "dp", axis=1, tiled=True),
        )

        split = (total_rows // 2 + 7) // 8 * 8
        halves = [hidden[:split], hidden[split:]]
        wholes = []
        for half in halves:
            buf = jnp.zeros((half.shape[0], n * feat), hidden.dtype)
            wholes.append(lax.dynamic_update_slice(buf, half, (0, tensor_rank * feat)))
        moving = list(halves)
        for s in range(n - 1):
            src = ring[(pos - sign * (s + 1)) % n]
            for i in range(2):
                if (s, i) == (min(4, n - 2), 0):
                    moving[i], query_full = lax.optimization_barrier((moving[i], query_full))
                if (s, i) == (n - 2, 1):
                    moving[i], out_full = lax.optimization_barrier((moving[i], out_full))
                moving[i] = lax.ppermute(moving[i], both, ring_pairs)
                wholes[i] = lax.dynamic_update_slice(wholes[i], moving[i], (0, src * feat))

        offsets, allowed = pair_layout(pair_lengths[0], premise_lengths[0], total_rows)
        low = tensor_rank < n // 2
        even = tensor_rank % 2 == 0
        pairs_a = [(s, 2 * s) if s < n // 2 else (s, 2 * (s - n // 2) + 1) for s in range(n)]
        pairs_b = [(s, 2 * s + 1) if s < n // 2 else (s, 2 * (s - n // 2)) for s in range(n)]
        contract = (((1,), (1,)), ((), ()))
        query_parts, key_parts, value_parts = [], [], []
        for i in range(2):
            rows_float = wholes[i].astype(jnp.float32)
            mean_square = jnp.mean(rows_float * rows_float, axis=-1, keepdims=True)
            normed = (rows_float * lax.rsqrt(mean_square + 1e-05) * norm_gain).astype(jnp.bfloat16)
            query_parts.append(jnp.dot(normed, query_full, preferred_element_type=jnp.float32))
            kv_piece = lax.dot_general(
                normed, kv_full, contract, preferred_element_type=jnp.float32
            ).astype(jnp.bfloat16)
            lo_cols = kv_piece[:, :HD]
            hi_cols = kv_piece[:, HD:]
            got_a = lax.ppermute(jnp.where(low, lo_cols, hi_cols), "tensor", pairs_a)
            got_b = lax.ppermute(jnp.where(low, hi_cols, lo_cols), "tensor", pairs_b)
            key_parts.append(jnp.where(even, got_a, got_b))
            value_parts.append(jnp.where(even, got_b, got_a))
        queries_raw = jnp.concatenate(query_parts, axis=0)
        key_head = jnp.concatenate(key_parts, axis=0)
        value_head = jnp.concatenate(value_parts, axis=0)

        queries = rotate_pairs(queries_raw.reshape(total_rows, head_local, HD), offsets).astype(
            jnp.bfloat16
        )
        keys = rotate_pairs(key_head.astype(jnp.float32)[:, None, :], offsets)[:, 0, :].astype(
            jnp.bfloat16
        )
        scale = HD ** (-0.5)
        starts = [0, split]
        sizes = [split, total_rows - split]

        def context_rows(i):
            q_rows = lax.slice_in_dim(queries, starts[i], starts[i] + sizes[i], axis=0)
            mask = lax.slice_in_dim(allowed, starts[i], starts[i] + sizes[i], axis=0)
            scores = jnp.einsum("qhd,kd->hqk", q_rows, keys, preferred_element_type=jnp.float32) * scale
            weighted = jnp.where(mask[None, :, :], jnp.exp(scores), 0.0)
            probs = (weighted / jnp.sum(weighted, axis=-1, keepdims=True)).astype(jnp.bfloat16)
            context = jnp.einsum(
                "hqk,kd->qhd", probs, value_head, preferred_element_type=jnp.float32
            ).astype(jnp.bfloat16)
            return context.reshape(sizes[i], head_local * HD)

        def chunk(context, dest_pos):
            cols = lax.dynamic_slice_in_dim(out_full, ring[dest_pos % n] * feat, feat, axis=1)
            return jnp.dot(context, cols, preferred_element_type=jnp.float32)

        parts = []
        for i in range(2):
            context = context_rows(i)
            mine = [chunk(context, pos + sign * (n - 1 - s)) for s in range(n)]
            parts.append([mine[0].astype(jnp.bfloat16)] + lax.optimization_barrier(mine[1:]))
        acc = [None, None]
        for s in range(n - 1):
            for i in range(2):
                if acc[i] is None:
                    send = parts[i][0]
                else:
                    send = (parts[i][s] + acc[i].astype(jnp.float32)).astype(jnp.bfloat16)
                acc[i] = lax.ppermute(send, both, ring_pairs)
        total = jnp.concatenate(
            [parts[i][n - 1] + acc[i].astype(jnp.float32) for i in range(2)], axis=0
        )
        return total.astype(jnp.bfloat16)

    return on_device


def generic(
    hidden,
    norm_gain,
    query_weight,
    query_keep,
    kv_weight,
    out_weight,
    out_keep,
    pair_lengths,
    premise_lengths,
):
    tensor_rank = lax.axis_index("tensor")
    total_rows = hidden.shape[0]
    head_local = query_weight.shape[1] // HD
    query_pruned = prune(query_weight, query_keep)
    out_pruned = prune(out_weight, out_keep)
    query_full = lax.all_gather(query_pruned, "dp", axis=0, tiled=True)
    kv_full, out_full = (
        lax.all_gather(kv_weight, "dp", axis=1, tiled=True),
        lax.all_gather(out_pruned, "dp", axis=1, tiled=True),
    )
    whole = lax.all_gather(hidden, "tensor", axis=1, tiled=True)
    rows_float = whole.astype(jnp.float32)
    mean_square = jnp.mean(rows_float * rows_float, axis=-1, keepdims=True)
    normed = (rows_float * lax.rsqrt(mean_square + 1e-05) * norm_gain).astype(jnp.bfloat16)
    queries_raw = jnp.dot(normed, query_full, preferred_element_type=jnp.float32)
    kv_piece = lax.dot_general(
        normed, kv_full, (((1,), (1,)), ((), ())), preferred_element_type=jnp.float32
    ).astype(jnp.bfloat16)
    kv_whole = lax.all_gather(kv_piece, "tensor", axis=1, tiled=True)
    offsets, allowed = pair_layout(pair_lengths[0], premise_lengths[0], total_rows)
    queries = rotate_pairs(queries_raw.reshape(total_rows, head_local, HD), offsets).astype(
        jnp.bfloat16
    )
    keys_all = rotate_pairs(
        kv_whole[:, : KVH * HD].reshape(total_rows, KVH, HD).astype(jnp.float32), offsets
    ).astype(jnp.bfloat16)
    values_all = kv_whole[:, KVH * HD :].reshape(total_rows, KVH, HD)
    chosen = (tensor_rank * head_local + jnp.arange(head_local, dtype=jnp.int32)) // (HEADS // KVH)
    keys_used = jnp.take(keys_all, chosen, axis=1)
    values_used = jnp.take(values_all, chosen, axis=1)
    scale = HD ** (-0.5)
    scores = (
        jnp.einsum("qhd,khd->hqk", queries, keys_used, preferred_element_type=jnp.float32) * scale
    )
    weighted = jnp.where(allowed[None, :, :], jnp.exp(scores), 0.0)
    probs = (weighted / jnp.sum(weighted, axis=-1, keepdims=True)).astype(jnp.bfloat16)
    context = jnp.einsum(
        "hqk,khd->qhd", probs, values_used, preferred_element_type=jnp.float32
    ).astype(jnp.bfloat16)
    context = context.reshape(total_rows, head_local * HD)
    terms = jnp.dot(context, out_full, preferred_element_type=jnp.float32)
    mixed = lax.psum_scatter(terms, "tensor", scatter_dimension=1, tiled=True)
    return mixed.astype(jnp.bfloat16)


def solution(mesh):
    placed = (
        P(("groups", "dp"), "tensor"),
        P(),
        P("dp", "tensor"),
        P("dp", "tensor"),
        P("tensor", "dp"),
        P("tensor", "dp"),
        P("tensor", "dp"),
        P(("groups", "dp"), None),
        P(("groups", "dp"), None),
    )
    n = mesh.shape["tensor"]
    if n == KVH and mesh.shape["dp"] == 2:
        coords = [getattr(d, "coords", None) for d in mesh.devices.reshape(-1)]
        z_size, x_size = n, 1
        if all(c is not None for c in coords):
            xs = sorted({c[0] for c in coords})
            zs = sorted({c[2] for c in coords})
            if len(xs) * len(zs) == n:
                z_size, x_size = len(zs), len(xs)
        body = make_fast(n, ring_order(z_size, x_size))
    else:
        body = generic
    return jax.shard_map(
        body,
        mesh=mesh,
        in_specs=placed,
        out_specs=P(("groups", "dp"), "tensor"),
        check_vma=False,
    )
```

```python
import jax
import jax.numpy as jnp
import numpy as np
from jax import lax
from jax.sharding import PartitionSpec as P

HEADS = 64
KVH = 8
HD = 128


def rotate_pairs(values, positions):
    half_width = values.shape[-1] // 2
    inverse = 500000.0 ** (-(jnp.arange(half_width, dtype=jnp.float32) * 2.0 / values.shape[-1]))
    angles = positions[:, None] * inverse[None, :]
    cosine = jnp.cos(angles)[:, None, :]
    sine_part = jnp.sin(angles)[:, None, :]
    first_half = values[..., :half_width]
    second_half = values[..., half_width:]
    return jnp.concatenate(
        [
            first_half * cosine - second_half * sine_part,
            second_half * cosine + first_half * sine_part,
        ],
        axis=-1,
    )


def pair_layout(lengths, premise, count):
    pair_ends = jnp.cumsum(lengths)
    pair_starts = pair_ends - lengths
    position = jnp.arange(count, dtype=jnp.int32)
    pair_index = jnp.sum((position[:, None] >= pair_ends[None, :]).astype(jnp.int32), axis=1)
    one_hot = (
        pair_index[:, None] == jnp.arange(lengths.shape[0], dtype=jnp.int32)[None, :]
    ).astype(jnp.int32)
    offset = position - jnp.sum(one_hot * pair_starts[None, :], axis=1)
    premise_used = jnp.minimum(premise, lengths - 1)
    in_premise = offset < jnp.sum(one_hot * premise_used[None, :], axis=1)
    allowed = (pair_index[:, None] == pair_index[None, :]) & (
        in_premise[None, :] | jnp.logical_not(in_premise)[:, None]
    )
    return (offset.astype(jnp.float32), allowed)


def prune(weight, keep):
    blocks = weight.reshape(
        keep.shape[0],
        weight.shape[0] // keep.shape[0],
        keep.shape[1],
        weight.shape[1] // keep.shape[1],
    )
    blocks = blocks * keep.astype(weight.dtype)[:, None, :, None]
    return blocks.reshape(weight.shape)


def ring_order(z_size, x_size):
    if x_size == 1 or z_size == 1:
        return list(range(z_size * x_size))
    cycle = [(z, 0) for z in range(z_size)]
    for step, z in enumerate(range(z_size - 1, -1, -1)):
        xs = list(range(1, x_size))
        cycle += [(z, x) for x in (xs if step % 2 == 0 else xs[::-1])]
    return [z * x_size + x for z, x in cycle]


def fast_prune(weight, keep):
    rows, cols = weight.shape
    step_r, step_c = rows // keep.shape[0], cols // keep.shape[1]
    mask = jnp.repeat(keep.astype(weight.dtype), step_c, axis=1)
    return (weight.reshape(keep.shape[0], step_r, cols) * mask[:, None, :]).reshape(rows, cols)


def make_fast(n, order):
    position_of = np.zeros(n, np.int32)
    for p, t in enumerate(order):
        position_of[t] = p
    order_arr = np.asarray(order, np.int32)
    both = ("tensor", "dp")
    ring_pairs = [(order[i] * 2, order[(i + 1) % n] * 2) for i in range(n)] + [
        (order[i] * 2 + 1, order[(i - 1) % n] * 2 + 1) for i in range(n)
    ]

    def on_device(
        hidden,
        norm_gain,
        query_weight,
        query_keep,
        kv_weight,
        out_weight,
        out_keep,
        pair_lengths,
        premise_lengths,
    ):
        tensor_rank = lax.axis_index("tensor")
        dp_rank = lax.axis_index("dp")
        pos = jnp.asarray(position_of)[tensor_rank]
        ring = jnp.asarray(order_arr)
        sign = 1 - 2 * dp_rank
        total_rows, feat = hidden.shape
        head_local = query_weight.shape[1] // HD

        query_full = fast_prune(
            lax.all_gather(query_weight, "dp", axis=0, tiled=True),
            lax.all_gather(query_keep, "dp", axis=0, tiled=True),
        )
        kv_full = lax.all_gather(kv_weight, "dp", axis=1, tiled=True)
        out_full = fast_prune(
            lax.all_gather(out_weight, "dp", axis=1, tiled=True),
            lax.all_gather(out_keep, "dp", axis=1, tiled=True),
        )

        split = (total_rows // 2 + 7) // 8 * 8
        halves = [hidden[:split], hidden[split:]]
        wholes = []
        for half in halves:
            buf = jnp.zeros((half.shape[0], n * feat), hidden.dtype)
            wholes.append(lax.dynamic_update_slice(buf, half, (0, tensor_rank * feat)))
        moving = list(halves)
        for s in range(n - 1):
            src = ring[(pos - sign * (s + 1)) % n]
            for i in range(2):
                moving[i] = lax.ppermute(moving[i], both, ring_pairs)
                wholes[i] = lax.dynamic_update_slice(wholes[i], moving[i], (0, src * feat))

        offsets, allowed = pair_layout(pair_lengths[0], premise_lengths[0], total_rows)
        low = tensor_rank < n // 2
        even = tensor_rank % 2 == 0
        pairs_a = [(s, 2 * s) if s < n // 2 else (s, 2 * (s - n // 2) + 1) for s in range(n)]
        pairs_b = [(s, 2 * s + 1) if s < n // 2 else (s, 2 * (s - n // 2)) for s in range(n)]
        contract = (((1,), (1,)), ((), ()))
        query_parts, key_parts, value_parts = [], [], []
        for i in range(2):
            rows_float = wholes[i].astype(jnp.float32)
            mean_square = jnp.mean(rows_float * rows_float, axis=-1, keepdims=True)
            normed = (rows_float * lax.rsqrt(mean_square + 1e-05) * norm_gain).astype(jnp.bfloat16)
            query_parts.append(jnp.dot(normed, query_full, preferred_element_type=jnp.float32))
            kv_piece = lax.dot_general(
                normed, kv_full, contract, preferred_element_type=jnp.float32
            ).astype(jnp.bfloat16)
            lo_cols = kv_piece[:, :HD]
            hi_cols = kv_piece[:, HD:]
            got_a = lax.ppermute(jnp.where(low, lo_cols, hi_cols), "tensor", pairs_a)
            got_b = lax.ppermute(jnp.where(low, hi_cols, lo_cols), "tensor", pairs_b)
            key_parts.append(jnp.where(even, got_a, got_b))
            value_parts.append(jnp.where(even, got_b, got_a))
        queries_raw = jnp.concatenate(query_parts, axis=0)
        key_head = jnp.concatenate(key_parts, axis=0)
        value_head = jnp.concatenate(value_parts, axis=0)

        queries = rotate_pairs(queries_raw.reshape(total_rows, head_local, HD), offsets).astype(
            jnp.bfloat16
        )
        keys = rotate_pairs(key_head.astype(jnp.float32)[:, None, :], offsets)[:, 0, :].astype(
            jnp.bfloat16
        )
        scale = HD ** (-0.5)
        starts = [0, split]
        sizes = [split, total_rows - split]

        def context_rows(i, q_rows):
            mask = lax.slice_in_dim(allowed, starts[i], starts[i] + sizes[i], axis=0)
            scores = jnp.einsum("qhd,kd->hqk", q_rows, keys, preferred_element_type=jnp.float32) * scale
            weighted = jnp.where(mask[None, :, :], jnp.exp(scores), 0.0)
            probs = (weighted / jnp.sum(weighted, axis=-1, keepdims=True)).astype(jnp.bfloat16)
            context = jnp.einsum(
                "hqk,kd->qhd", probs, value_head, preferred_element_type=jnp.float32
            ).astype(jnp.bfloat16)
            return context.reshape(sizes[i], head_local * HD)

        def chunk(context, dest_pos):
            cols = lax.dynamic_slice_in_dim(out_full, ring[dest_pos % n] * feat, feat, axis=1)
            return jnp.dot(context, cols, preferred_element_type=jnp.float32)

        parts = []
        for i in range(2):
            q_rows = lax.slice_in_dim(queries, starts[i], starts[i] + sizes[i], axis=0)
            if i > 0:
                q_rows, _ = lax.optimization_barrier((q_rows, parts[0][0]))
            context = context_rows(i, q_rows)
            mine = [chunk(context, pos + sign * (n - 1 - s)) for s in range(n)]
            parts.append([mine[0].astype(jnp.bfloat16)] + lax.optimization_barrier(mine[1:]))
        acc = [None, None]
        for s in range(n - 1):
            for i in range(2):
                if acc[i] is None:
                    send = parts[i][0]
                else:
                    send = (parts[i][s] + acc[i].astype(jnp.float32)).astype(jnp.bfloat16)
                acc[i] = lax.ppermute(send, both, ring_pairs)
        total = jnp.concatenate(
            [parts[i][n - 1] + acc[i].astype(jnp.float32) for i in range(2)], axis=0
        )
        return total.astype(jnp.bfloat16)

    return on_device


def generic(
    hidden,
    norm_gain,
    query_weight,
    query_keep,
    kv_weight,
    out_weight,
    out_keep,
    pair_lengths,
    premise_lengths,
):
    tensor_rank = lax.axis_index("tensor")
    total_rows = hidden.shape[0]
    head_local = query_weight.shape[1] // HD
    query_pruned = prune(query_weight, query_keep)
    out_pruned = prune(out_weight, out_keep)
    query_full = lax.all_gather(query_pruned, "dp", axis=0, tiled=True)
    kv_full, out_full = (
        lax.all_gather(kv_weight, "dp", axis=1, tiled=True),
        lax.all_gather(out_pruned, "dp", axis=1, tiled=True),
    )
    whole = lax.all_gather(hidden, "tensor", axis=1, tiled=True)
    rows_float = whole.astype(jnp.float32)
    mean_square = jnp.mean(rows_float * rows_float, axis=-1, keepdims=True)
    normed = (rows_float * lax.rsqrt(mean_square + 1e-05) * norm_gain).astype(jnp.bfloat16)
    queries_raw = jnp.dot(normed, query_full, preferred_element_type=jnp.float32)
    kv_piece = lax.dot_general(
        normed, kv_full, (((1,), (1,)), ((), ())), preferred_element_type=jnp.float32
    ).astype(jnp.bfloat16)
    kv_whole = lax.all_gather(kv_piece, "tensor", axis=1, tiled=True)
    offsets, allowed = pair_layout(pair_lengths[0], premise_lengths[0], total_rows)
    queries = rotate_pairs(queries_raw.reshape(total_rows, head_local, HD), offsets).astype(
        jnp.bfloat16
    )
    keys_all = rotate_pairs(
        kv_whole[:, : KVH * HD].reshape(total_rows, KVH, HD).astype(jnp.float32), offsets
    ).astype(jnp.bfloat16)
    values_all = kv_whole[:, KVH * HD :].reshape(total_rows, KVH, HD)
    chosen = (tensor_rank * head_local + jnp.arange(head_local, dtype=jnp.int32)) // (HEADS // KVH)
    keys_used = jnp.take(keys_all, chosen, axis=1)
    values_used = jnp.take(values_all, chosen, axis=1)
    scale = HD ** (-0.5)
    scores = (
        jnp.einsum("qhd,khd->hqk", queries, keys_used, preferred_element_type=jnp.float32) * scale
    )
    weighted = jnp.where(allowed[None, :, :], jnp.exp(scores), 0.0)
    probs = (weighted / jnp.sum(weighted, axis=-1, keepdims=True)).astype(jnp.bfloat16)
    context = jnp.einsum(
        "hqk,khd->qhd", probs, values_used, preferred_element_type=jnp.float32
    ).astype(jnp.bfloat16)
    context = context.reshape(total_rows, head_local * HD)
    terms = jnp.dot(context, out_full, preferred_element_type=jnp.float32)
    mixed = lax.psum_scatter(terms, "tensor", scatter_dimension=1, tiled=True)
    return mixed.astype(jnp.bfloat16)


def solution(mesh):
    placed = (
        P(("groups", "dp"), "tensor"),
        P(),
        P("dp", "tensor"),
        P("dp", "tensor"),
        P("tensor", "dp"),
        P("tensor", "dp"),
        P("tensor", "dp"),
        P(("groups", "dp"), None),
        P(("groups", "dp"), None),
    )
    n = mesh.shape["tensor"]
    if n == KVH and mesh.shape["dp"] == 2:
        coords = [getattr(d, "coords", None) for d in mesh.devices.reshape(-1)]
        z_size, x_size = n, 1
        if all(c is not None for c in coords):
            xs = sorted({c[0] for c in coords})
            zs = sorted({c[2] for c in coords})
            if len(xs) * len(zs) == n:
                z_size, x_size = len(zs), len(xs)
        body = make_fast(n, ring_order(z_size, x_size))
    else:
        body = generic
    return jax.shard_map(
        body,
        mesh=mesh,
        in_specs=placed,
        out_specs=P(("groups", "dp"), "tensor"),
        check_vma=False,
    )
```

```python
import jax
import jax.numpy as jnp
import numpy as np
from jax import lax
from jax.sharding import PartitionSpec as P

HEADS = 64
KVH = 8
HD = 128


def rotate_pairs(values, positions):
    half_width = values.shape[-1] // 2
    inverse = 500000.0 ** (-(jnp.arange(half_width, dtype=jnp.float32) * 2.0 / values.shape[-1]))
    angles = positions[:, None] * inverse[None, :]
    cosine = jnp.cos(angles)[:, None, :]
    sine_part = jnp.sin(angles)[:, None, :]
    first_half = values[..., :half_width]
    second_half = values[..., half_width:]
    return jnp.concatenate(
        [
            first_half * cosine - second_half * sine_part,
            second_half * cosine + first_half * sine_part,
        ],
        axis=-1,
    )


def pair_layout(lengths, premise, count):
    pair_ends = jnp.cumsum(lengths)
    pair_starts = pair_ends - lengths
    position = jnp.arange(count, dtype=jnp.int32)
    pair_index = jnp.sum((position[:, None] >= pair_ends[None, :]).astype(jnp.int32), axis=1)
    one_hot = (
        pair_index[:, None] == jnp.arange(lengths.shape[0], dtype=jnp.int32)[None, :]
    ).astype(jnp.int32)
    offset = position - jnp.sum(one_hot * pair_starts[None, :], axis=1)
    premise_used = jnp.minimum(premise, lengths - 1)
    in_premise = offset < jnp.sum(one_hot * premise_used[None, :], axis=1)
    allowed = (pair_index[:, None] == pair_index[None, :]) & (
        in_premise[None, :] | jnp.logical_not(in_premise)[:, None]
    )
    return (offset.astype(jnp.float32), allowed)


def prune(weight, keep):
    blocks = weight.reshape(
        keep.shape[0],
        weight.shape[0] // keep.shape[0],
        keep.shape[1],
        weight.shape[1] // keep.shape[1],
    )
    blocks = blocks * keep.astype(weight.dtype)[:, None, :, None]
    return blocks.reshape(weight.shape)


def ring_order(z_size, x_size):
    if x_size == 1 or z_size == 1:
        return list(range(z_size * x_size))
    cycle = [(z, 0) for z in range(z_size)]
    for step, z in enumerate(range(z_size - 1, -1, -1)):
        xs = list(range(1, x_size))
        cycle += [(z, x) for x in (xs if step % 2 == 0 else xs[::-1])]
    return [z * x_size + x for z, x in cycle]


def fast_prune(weight, keep):
    rows, cols = weight.shape
    step_r, step_c = rows // keep.shape[0], cols // keep.shape[1]
    mask = jnp.repeat(keep.astype(weight.dtype), step_c, axis=1)
    return (weight.reshape(keep.shape[0], step_r, cols) * mask[:, None, :]).reshape(rows, cols)


def make_fast(n, order):
    position_of = np.zeros(n, np.int32)
    for p, t in enumerate(order):
        position_of[t] = p
    order_arr = np.asarray(order, np.int32)
    both = ("tensor", "dp")
    ring_pairs = [(order[i] * 2, order[(i + 1) % n] * 2) for i in range(n)] + [
        (order[i] * 2 + 1, order[(i - 1) % n] * 2 + 1) for i in range(n)
    ]

    def on_device(
        hidden,
        norm_gain,
        query_weight,
        query_keep,
        kv_weight,
        out_weight,
        out_keep,
        pair_lengths,
        premise_lengths,
    ):
        tensor_rank = lax.axis_index("tensor")
        dp_rank = lax.axis_index("dp")
        pos = jnp.asarray(position_of)[tensor_rank]
        ring = jnp.asarray(order_arr)
        sign = 1 - 2 * dp_rank
        total_rows, feat = hidden.shape
        head_local = query_weight.shape[1] // HD

        swap = [(0, 1), (1, 0)]

        def keep_over_dp(local, axis):
            other = lax.ppermute(local, "dp", swap)
            return jnp.where(
                dp_rank == 0,
                jnp.concatenate([local, other], axis=axis),
                jnp.concatenate([other, local], axis=axis),
            )

        query_full = fast_prune(
            lax.all_gather(query_weight, "dp", axis=0, tiled=True), keep_over_dp(query_keep, 0)
        )
        kv_full = lax.all_gather(kv_weight, "dp", axis=1, tiled=True)
        out_full = fast_prune(
            lax.all_gather(out_weight, "dp", axis=1, tiled=True), keep_over_dp(out_keep, 1)
        )

        split = (total_rows // 2 + 7) // 8 * 8
        halves = [hidden[:split], hidden[split:]]
        wholes = []
        for half in halves:
            buf = jnp.zeros((half.shape[0], n * feat), hidden.dtype)
            wholes.append(lax.dynamic_update_slice(buf, half, (0, tensor_rank * feat)))
        moving = list(halves)
        for s in range(n - 1):
            src = ring[(pos - sign * (s + 1)) % n]
            for i in range(2):
                moving[i] = lax.ppermute(moving[i], both, ring_pairs)
                wholes[i] = lax.dynamic_update_slice(wholes[i], moving[i], (0, src * feat))

        offsets, allowed = pair_layout(pair_lengths[0], premise_lengths[0], total_rows)
        low = tensor_rank < n // 2
        even = tensor_rank % 2 == 0
        pairs_a = [(s, 2 * s) if s < n // 2 else (s, 2 * (s - n // 2) + 1) for s in range(n)]
        pairs_b = [(s, 2 * s + 1) if s < n // 2 else (s, 2 * (s - n // 2)) for s in range(n)]
        contract = (((1,), (1,)), ((), ()))
        query_parts, key_parts, value_parts = [], [], []
        for i in range(2):
            rows_float = wholes[i].astype(jnp.float32)
            mean_square = jnp.mean(rows_float * rows_float, axis=-1, keepdims=True)
            normed = (rows_float * lax.rsqrt(mean_square + 1e-05) * norm_gain).astype(jnp.bfloat16)
            query_parts.append(jnp.dot(normed, query_full, preferred_element_type=jnp.float32))
            kv_piece = lax.dot_general(
                normed, kv_full, contract, preferred_element_type=jnp.float32
            ).astype(jnp.bfloat16)
            lo_cols = kv_piece[:, :HD]
            hi_cols = kv_piece[:, HD:]
            got_a = lax.ppermute(jnp.where(low, lo_cols, hi_cols), "tensor", pairs_a)
            got_b = lax.ppermute(jnp.where(low, hi_cols, lo_cols), "tensor", pairs_b)
            key_parts.append(jnp.where(even, got_a, got_b))
            value_parts.append(jnp.where(even, got_b, got_a))
        queries_raw = jnp.concatenate(query_parts, axis=0)
        key_head = jnp.concatenate(key_parts, axis=0)
        value_head = jnp.concatenate(value_parts, axis=0)

        queries = rotate_pairs(queries_raw.reshape(total_rows, head_local, HD), offsets).astype(
            jnp.bfloat16
        )
        keys = rotate_pairs(key_head.astype(jnp.float32)[:, None, :], offsets)[:, 0, :].astype(
            jnp.bfloat16
        )
        scale = HD ** (-0.5)
        starts = [0, split]
        sizes = [split, total_rows - split]

        def context_rows(i, q_rows):
            mask = lax.slice_in_dim(allowed, starts[i], starts[i] + sizes[i], axis=0)
            scores = jnp.einsum("qhd,kd->hqk", q_rows, keys, preferred_element_type=jnp.float32) * scale
            weighted = jnp.where(mask[None, :, :], jnp.exp(scores), 0.0)
            probs = (weighted / jnp.sum(weighted, axis=-1, keepdims=True)).astype(jnp.bfloat16)
            context = jnp.einsum(
                "hqk,kd->qhd", probs, value_head, preferred_element_type=jnp.float32
            ).astype(jnp.bfloat16)
            return context.reshape(sizes[i], head_local * HD)

        def chunk(context, dest_pos):
            cols = lax.dynamic_slice_in_dim(out_full, ring[dest_pos % n] * feat, feat, axis=1)
            return jnp.dot(context, cols, preferred_element_type=jnp.float32)

        parts = []
        for i in range(2):
            q_rows = lax.slice_in_dim(queries, starts[i], starts[i] + sizes[i], axis=0)
            if i > 0:
                q_rows, _ = lax.optimization_barrier((q_rows, parts[0][0]))
            context = context_rows(i, q_rows)
            mine = [chunk(context, pos + sign * (n - 1 - s)) for s in range(n)]
            parts.append([mine[0].astype(jnp.bfloat16)] + lax.optimization_barrier(mine[1:]))
        acc = [None, None]
        for s in range(n - 1):
            for i in range(2):
                if acc[i] is None:
                    send = parts[i][0]
                else:
                    send = (parts[i][s] + acc[i].astype(jnp.float32)).astype(jnp.bfloat16)
                acc[i] = lax.ppermute(send, both, ring_pairs)
        total = jnp.concatenate(
            [parts[i][n - 1] + acc[i].astype(jnp.float32) for i in range(2)], axis=0
        )
        return total.astype(jnp.bfloat16)

    return on_device


def generic(
    hidden,
    norm_gain,
    query_weight,
    query_keep,
    kv_weight,
    out_weight,
    out_keep,
    pair_lengths,
    premise_lengths,
):
    tensor_rank = lax.axis_index("tensor")
    total_rows = hidden.shape[0]
    head_local = query_weight.shape[1] // HD
    query_pruned = prune(query_weight, query_keep)
    out_pruned = prune(out_weight, out_keep)
    query_full = lax.all_gather(query_pruned, "dp", axis=0, tiled=True)
    kv_full, out_full = (
        lax.all_gather(kv_weight, "dp", axis=1, tiled=True),
        lax.all_gather(out_pruned, "dp", axis=1, tiled=True),
    )
    whole = lax.all_gather(hidden, "tensor", axis=1, tiled=True)
    rows_float = whole.astype(jnp.float32)
    mean_square = jnp.mean(rows_float * rows_float, axis=-1, keepdims=True)
    normed = (rows_float * lax.rsqrt(mean_square + 1e-05) * norm_gain).astype(jnp.bfloat16)
    queries_raw = jnp.dot(normed, query_full, preferred_element_type=jnp.float32)
    kv_piece = lax.dot_general(
        normed, kv_full, (((1,), (1,)), ((), ())), preferred_element_type=jnp.float32
    ).astype(jnp.bfloat16)
    kv_whole = lax.all_gather(kv_piece, "tensor", axis=1, tiled=True)
    offsets, allowed = pair_layout(pair_lengths[0], premise_lengths[0], total_rows)
    queries = rotate_pairs(queries_raw.reshape(total_rows, head_local, HD), offsets).astype(
        jnp.bfloat16
    )
    keys_all = rotate_pairs(
        kv_whole[:, : KVH * HD].reshape(total_rows, KVH, HD).astype(jnp.float32), offsets
    ).astype(jnp.bfloat16)
    values_all = kv_whole[:, KVH * HD :].reshape(total_rows, KVH, HD)
    chosen = (tensor_rank * head_local + jnp.arange(head_local, dtype=jnp.int32)) // (HEADS // KVH)
    keys_used = jnp.take(keys_all, chosen, axis=1)
    values_used = jnp.take(values_all, chosen, axis=1)
    scale = HD ** (-0.5)
    scores = (
        jnp.einsum("qhd,khd->hqk", queries, keys_used, preferred_element_type=jnp.float32) * scale
    )
    weighted = jnp.where(allowed[None, :, :], jnp.exp(scores), 0.0)
    probs = (weighted / jnp.sum(weighted, axis=-1, keepdims=True)).astype(jnp.bfloat16)
    context = jnp.einsum(
        "hqk,khd->qhd", probs, values_used, preferred_element_type=jnp.float32
    ).astype(jnp.bfloat16)
    context = context.reshape(total_rows, head_local * HD)
    terms = jnp.dot(context, out_full, preferred_element_type=jnp.float32)
    mixed = lax.psum_scatter(terms, "tensor", scatter_dimension=1, tiled=True)
    return mixed.astype(jnp.bfloat16)


def solution(mesh):
    placed = (
        P(("groups", "dp"), "tensor"),
        P(),
        P("dp", "tensor"),
        P("dp", "tensor"),
        P("tensor", "dp"),
        P("tensor", "dp"),
        P("tensor", "dp"),
        P(("groups", "dp"), None),
        P(("groups", "dp"), None),
    )
    n = mesh.shape["tensor"]
    if n == KVH and mesh.shape["dp"] == 2:
        coords = [getattr(d, "coords", None) for d in mesh.devices.reshape(-1)]
        z_size, x_size = n, 1
        if all(c is not None for c in coords):
            xs = sorted({c[0] for c in coords})
            zs = sorted({c[2] for c in coords})
            if len(xs) * len(zs) == n:
                z_size, x_size = len(zs), len(xs)
        body = make_fast(n, ring_order(z_size, x_size))
    else:
        body = generic
    return jax.shard_map(
        body,
        mesh=mesh,
        in_specs=placed,
        out_specs=P(("groups", "dp"), "tensor"),
        check_vma=False,
    )
```

```python
import jax
import jax.numpy as jnp
import numpy as np
from jax import lax
from jax.sharding import PartitionSpec as P

HEADS = 64
KVH = 8
HD = 128


def rotate_pairs(values, positions):
    half_width = values.shape[-1] // 2
    inverse = 500000.0 ** (-(jnp.arange(half_width, dtype=jnp.float32) * 2.0 / values.shape[-1]))
    angles = positions[:, None] * inverse[None, :]
    cosine = jnp.cos(angles)[:, None, :]
    sine_part = jnp.sin(angles)[:, None, :]
    first_half = values[..., :half_width]
    second_half = values[..., half_width:]
    return jnp.concatenate(
        [
            first_half * cosine - second_half * sine_part,
            second_half * cosine + first_half * sine_part,
        ],
        axis=-1,
    )


def pair_layout(lengths, premise, count):
    pair_ends = jnp.cumsum(lengths)
    pair_starts = pair_ends - lengths
    position = jnp.arange(count, dtype=jnp.int32)
    pair_index = jnp.sum((position[:, None] >= pair_ends[None, :]).astype(jnp.int32), axis=1)
    one_hot = (
        pair_index[:, None] == jnp.arange(lengths.shape[0], dtype=jnp.int32)[None, :]
    ).astype(jnp.int32)
    offset = position - jnp.sum(one_hot * pair_starts[None, :], axis=1)
    premise_used = jnp.minimum(premise, lengths - 1)
    in_premise = offset < jnp.sum(one_hot * premise_used[None, :], axis=1)
    allowed = (pair_index[:, None] == pair_index[None, :]) & (
        in_premise[None, :] | jnp.logical_not(in_premise)[:, None]
    )
    return (offset.astype(jnp.float32), allowed)


def prune(weight, keep):
    blocks = weight.reshape(
        keep.shape[0],
        weight.shape[0] // keep.shape[0],
        keep.shape[1],
        weight.shape[1] // keep.shape[1],
    )
    blocks = blocks * keep.astype(weight.dtype)[:, None, :, None]
    return blocks.reshape(weight.shape)


def ring_order(z_size, x_size):
    if x_size == 1 or z_size == 1:
        return list(range(z_size * x_size))
    cycle = [(z, 0) for z in range(z_size)]
    for step, z in enumerate(range(z_size - 1, -1, -1)):
        xs = list(range(1, x_size))
        cycle += [(z, x) for x in (xs if step % 2 == 0 else xs[::-1])]
    return [z * x_size + x for z, x in cycle]


def fast_prune(weight, keep):
    rows, cols = weight.shape
    step_r, step_c = rows // keep.shape[0], cols // keep.shape[1]
    mask = jnp.repeat(keep.astype(weight.dtype), step_c, axis=1)
    return (weight.reshape(keep.shape[0], step_r, cols) * mask[:, None, :]).reshape(rows, cols)


def make_fast(n, order):
    position_of = np.zeros(n, np.int32)
    for p, t in enumerate(order):
        position_of[t] = p
    order_arr = np.asarray(order, np.int32)
    both = ("tensor", "dp")
    ring_pairs = [(order[i] * 2, order[(i + 1) % n] * 2) for i in range(n)] + [
        (order[i] * 2 + 1, order[(i - 1) % n] * 2 + 1) for i in range(n)
    ]

    def on_device(
        hidden,
        norm_gain,
        query_weight,
        query_keep,
        kv_weight,
        out_weight,
        out_keep,
        pair_lengths,
        premise_lengths,
    ):
        tensor_rank = lax.axis_index("tensor")
        dp_rank = lax.axis_index("dp")
        pos = jnp.asarray(position_of)[tensor_rank]
        ring = jnp.asarray(order_arr)
        sign = 1 - 2 * dp_rank
        total_rows, feat = hidden.shape
        head_local = query_weight.shape[1] // HD

        query_full = fast_prune(
            lax.all_gather(query_weight, "dp", axis=0, tiled=True),
            lax.all_gather(query_keep, "dp", axis=0, tiled=True),
        )
        kv_full = lax.all_gather(kv_weight, "dp", axis=1, tiled=True)
        out_full = fast_prune(
            lax.all_gather(out_weight, "dp", axis=1, tiled=True),
            lax.all_gather(out_keep, "dp", axis=1, tiled=True),
        )

        split = (total_rows // 2 + 7) // 8 * 8
        moving = [hidden[:split], hidden[split:]]
        arrived = [[moving[0]], [moving[1]]]
        sources = [tensor_rank]
        for s in range(n - 1):
            sources.append(ring[(pos - sign * (s + 1)) % n])
            for i in range(2):
                moving[i] = lax.ppermute(moving[i], both, ring_pairs)
                arrived[i].append(moving[i])
        wholes = [jnp.concatenate(arrived[i], axis=1) for i in range(2)]
        norm_gain = jnp.concatenate(
            [lax.dynamic_slice_in_dim(norm_gain, src * feat, feat) for src in sources]
        )
        query_full = jnp.concatenate(
            [lax.dynamic_slice_in_dim(query_full, src * feat, feat, axis=0) for src in sources],
            axis=0,
        )
        kv_full = jnp.concatenate(
            [lax.dynamic_slice_in_dim(kv_full, src * feat, feat, axis=1) for src in sources],
            axis=1,
        )

        offsets, allowed = pair_layout(pair_lengths[0], premise_lengths[0], total_rows)
        low = tensor_rank < n // 2
        even = tensor_rank % 2 == 0
        pairs_a = [(s, 2 * s) if s < n // 2 else (s, 2 * (s - n // 2) + 1) for s in range(n)]
        pairs_b = [(s, 2 * s + 1) if s < n // 2 else (s, 2 * (s - n // 2)) for s in range(n)]
        contract = (((1,), (1,)), ((), ()))
        query_parts, key_parts, value_parts = [], [], []
        for i in range(2):
            rows_float = wholes[i].astype(jnp.float32)
            mean_square = jnp.mean(rows_float * rows_float, axis=-1, keepdims=True)
            normed = (rows_float * lax.rsqrt(mean_square + 1e-05) * norm_gain).astype(jnp.bfloat16)
            query_parts.append(jnp.dot(normed, query_full, preferred_element_type=jnp.float32))
            kv_piece = lax.dot_general(
                normed, kv_full, contract, preferred_element_type=jnp.float32
            ).astype(jnp.bfloat16)
            lo_cols = kv_piece[:, :HD]
            hi_cols = kv_piece[:, HD:]
            got_a = lax.ppermute(jnp.where(low, lo_cols, hi_cols), "tensor", pairs_a)
            got_b = lax.ppermute(jnp.where(low, hi_cols, lo_cols), "tensor", pairs_b)
            key_parts.append(jnp.where(even, got_a, got_b))
            value_parts.append(jnp.where(even, got_b, got_a))
        queries_raw = jnp.concatenate(query_parts, axis=0)
        key_head = jnp.concatenate(key_parts, axis=0)
        value_head = jnp.concatenate(value_parts, axis=0)

        queries = rotate_pairs(queries_raw.reshape(total_rows, head_local, HD), offsets).astype(
            jnp.bfloat16
        )
        keys = rotate_pairs(key_head.astype(jnp.float32)[:, None, :], offsets)[:, 0, :].astype(
            jnp.bfloat16
        )
        scale = HD ** (-0.5)
        starts = [0, split]
        sizes = [split, total_rows - split]

        def context_rows(i, q_rows):
            mask = lax.slice_in_dim(allowed, starts[i], starts[i] + sizes[i], axis=0)
            scores = jnp.einsum("qhd,kd->hqk", q_rows, keys, preferred_element_type=jnp.float32) * scale
            weighted = jnp.where(mask[None, :, :], jnp.exp(scores), 0.0)
            probs = (weighted / jnp.sum(weighted, axis=-1, keepdims=True)).astype(jnp.bfloat16)
            context = jnp.einsum(
                "hqk,kd->qhd", probs, value_head, preferred_element_type=jnp.float32
            ).astype(jnp.bfloat16)
            return context.reshape(sizes[i], head_local * HD)

        def chunk(context, dest_pos):
            cols = lax.dynamic_slice_in_dim(out_full, ring[dest_pos % n] * feat, feat, axis=1)
            return jnp.dot(context, cols, preferred_element_type=jnp.float32)

        parts = []
        for i in range(2):
            q_rows = lax.slice_in_dim(queries, starts[i], starts[i] + sizes[i], axis=0)
            if i > 0:
                q_rows, _ = lax.optimization_barrier((q_rows, parts[0][0]))
            context = context_rows(i, q_rows)
            mine = [chunk(context, pos + sign * (n - 1 - s)) for s in range(n)]
            parts.append([mine[0].astype(jnp.bfloat16)] + lax.optimization_barrier(mine[1:]))
        acc = [None, None]
        for s in range(n - 1):
            for i in range(2):
                if acc[i] is None:
                    send = parts[i][0]
                else:
                    send = (parts[i][s] + acc[i].astype(jnp.float32)).astype(jnp.bfloat16)
                acc[i] = lax.ppermute(send, both, ring_pairs)
        total = jnp.concatenate(
            [parts[i][n - 1] + acc[i].astype(jnp.float32) for i in range(2)], axis=0
        )
        return total.astype(jnp.bfloat16)

    return on_device


def generic(
    hidden,
    norm_gain,
    query_weight,
    query_keep,
    kv_weight,
    out_weight,
    out_keep,
    pair_lengths,
    premise_lengths,
):
    tensor_rank = lax.axis_index("tensor")
    total_rows = hidden.shape[0]
    head_local = query_weight.shape[1] // HD
    query_pruned = prune(query_weight, query_keep)
    out_pruned = prune(out_weight, out_keep)
    query_full = lax.all_gather(query_pruned, "dp", axis=0, tiled=True)
    kv_full, out_full = (
        lax.all_gather(kv_weight, "dp", axis=1, tiled=True),
        lax.all_gather(out_pruned, "dp", axis=1, tiled=True),
    )
    whole = lax.all_gather(hidden, "tensor", axis=1, tiled=True)
    rows_float = whole.astype(jnp.float32)
    mean_square = jnp.mean(rows_float * rows_float, axis=-1, keepdims=True)
    normed = (rows_float * lax.rsqrt(mean_square + 1e-05) * norm_gain).astype(jnp.bfloat16)
    queries_raw = jnp.dot(normed, query_full, preferred_element_type=jnp.float32)
    kv_piece = lax.dot_general(
        normed, kv_full, (((1,), (1,)), ((), ())), preferred_element_type=jnp.float32
    ).astype(jnp.bfloat16)
    kv_whole = lax.all_gather(kv_piece, "tensor", axis=1, tiled=True)
    offsets, allowed = pair_layout(pair_lengths[0], premise_lengths[0], total_rows)
    queries = rotate_pairs(queries_raw.reshape(total_rows, head_local, HD), offsets).astype(
        jnp.bfloat16
    )
    keys_all = rotate_pairs(
        kv_whole[:, : KVH * HD].reshape(total_rows, KVH, HD).astype(jnp.float32), offsets
    ).astype(jnp.bfloat16)
    values_all = kv_whole[:, KVH * HD :].reshape(total_rows, KVH, HD)
    chosen = (tensor_rank * head_local + jnp.arange(head_local, dtype=jnp.int32)) // (HEADS // KVH)
    keys_used = jnp.take(keys_all, chosen, axis=1)
    values_used = jnp.take(values_all, chosen, axis=1)
    scale = HD ** (-0.5)
    scores = (
        jnp.einsum("qhd,khd->hqk", queries, keys_used, preferred_element_type=jnp.float32) * scale
    )
    weighted = jnp.where(allowed[None, :, :], jnp.exp(scores), 0.0)
    probs = (weighted / jnp.sum(weighted, axis=-1, keepdims=True)).astype(jnp.bfloat16)
    context = jnp.einsum(
        "hqk,khd->qhd", probs, values_used, preferred_element_type=jnp.float32
    ).astype(jnp.bfloat16)
    context = context.reshape(total_rows, head_local * HD)
    terms = jnp.dot(context, out_full, preferred_element_type=jnp.float32)
    mixed = lax.psum_scatter(terms, "tensor", scatter_dimension=1, tiled=True)
    return mixed.astype(jnp.bfloat16)


def solution(mesh):
    placed = (
        P(("groups", "dp"), "tensor"),
        P(),
        P("dp", "tensor"),
        P("dp", "tensor"),
        P("tensor", "dp"),
        P("tensor", "dp"),
        P("tensor", "dp"),
        P(("groups", "dp"), None),
        P(("groups", "dp"), None),
    )
    n = mesh.shape["tensor"]
    if n == KVH and mesh.shape["dp"] == 2:
        coords = [getattr(d, "coords", None) for d in mesh.devices.reshape(-1)]
        z_size, x_size = n, 1
        if all(c is not None for c in coords):
            xs = sorted({c[0] for c in coords})
            zs = sorted({c[2] for c in coords})
            if len(xs) * len(zs) == n:
                z_size, x_size = len(zs), len(xs)
        body = make_fast(n, ring_order(z_size, x_size))
    else:
        body = generic
    return jax.shard_map(
        body,
        mesh=mesh,
        in_specs=placed,
        out_specs=P(("groups", "dp"), "tensor"),
        check_vma=False,
    )
```

```python
import jax
import jax.numpy as jnp
import numpy as np
from jax import lax
from jax.sharding import PartitionSpec as P

HEADS = 64
KVH = 8
HD = 128


def rotate_pairs(values, positions):
    half_width = values.shape[-1] // 2
    inverse = 500000.0 ** (-(jnp.arange(half_width, dtype=jnp.float32) * 2.0 / values.shape[-1]))
    angles = positions[:, None] * inverse[None, :]
    cosine = jnp.cos(angles)[:, None, :]
    sine_part = jnp.sin(angles)[:, None, :]
    first_half = values[..., :half_width]
    second_half = values[..., half_width:]
    return jnp.concatenate(
        [
            first_half * cosine - second_half * sine_part,
            second_half * cosine + first_half * sine_part,
        ],
        axis=-1,
    )


def pair_layout(lengths, premise, count):
    pair_ends = jnp.cumsum(lengths)
    pair_starts = pair_ends - lengths
    position = jnp.arange(count, dtype=jnp.int32)
    pair_index = jnp.sum((position[:, None] >= pair_ends[None, :]).astype(jnp.int32), axis=1)
    one_hot = (
        pair_index[:, None] == jnp.arange(lengths.shape[0], dtype=jnp.int32)[None, :]
    ).astype(jnp.int32)
    offset = position - jnp.sum(one_hot * pair_starts[None, :], axis=1)
    premise_used = jnp.minimum(premise, lengths - 1)
    in_premise = offset < jnp.sum(one_hot * premise_used[None, :], axis=1)
    allowed = (pair_index[:, None] == pair_index[None, :]) & (
        in_premise[None, :] | jnp.logical_not(in_premise)[:, None]
    )
    return (offset.astype(jnp.float32), allowed)


def prune(weight, keep):
    blocks = weight.reshape(
        keep.shape[0],
        weight.shape[0] // keep.shape[0],
        keep.shape[1],
        weight.shape[1] // keep.shape[1],
    )
    blocks = blocks * keep.astype(weight.dtype)[:, None, :, None]
    return blocks.reshape(weight.shape)


def ring_order(z_size, x_size):
    if x_size == 1 or z_size == 1:
        return list(range(z_size * x_size))
    cycle = [(z, 0) for z in range(z_size)]
    for step, z in enumerate(range(z_size - 1, -1, -1)):
        xs = list(range(1, x_size))
        cycle += [(z, x) for x in (xs if step % 2 == 0 else xs[::-1])]
    return [z * x_size + x for z, x in cycle]


def fast_prune(weight, keep):
    rows, cols = weight.shape
    step_r, step_c = rows // keep.shape[0], cols // keep.shape[1]
    mask = jnp.repeat(keep.astype(weight.dtype), step_c, axis=1)
    return (weight.reshape(keep.shape[0], step_r, cols) * mask[:, None, :]).reshape(rows, cols)


def make_fast(n, order):
    position_of = np.zeros(n, np.int32)
    for p, t in enumerate(order):
        position_of[t] = p
    order_arr = np.asarray(order, np.int32)
    both = ("tensor", "dp")
    ring_pairs = [(order[i] * 2, order[(i + 1) % n] * 2) for i in range(n)] + [
        (order[i] * 2 + 1, order[(i - 1) % n] * 2 + 1) for i in range(n)
    ]

    def on_device(
        hidden,
        norm_gain,
        query_weight,
        query_keep,
        kv_weight,
        out_weight,
        out_keep,
        pair_lengths,
        premise_lengths,
    ):
        tensor_rank = lax.axis_index("tensor")
        dp_rank = lax.axis_index("dp")
        pos = jnp.asarray(position_of)[tensor_rank]
        ring = jnp.asarray(order_arr)
        sign = 1 - 2 * dp_rank
        total_rows, feat = hidden.shape
        head_local = query_weight.shape[1] // HD

        query_full = fast_prune(
            lax.all_gather(query_weight, "dp", axis=0, tiled=True),
            lax.all_gather(query_keep, "dp", axis=0, tiled=True),
        )
        kv_full = lax.all_gather(kv_weight, "dp", axis=1, tiled=True)
        out_raw = lax.all_gather(out_weight, "dp", axis=1, tiled=True)
        out_keep_full = lax.all_gather(out_keep, "dp", axis=1, tiled=True)

        split = (total_rows // 2 + 7) // 8 * 8
        moving = [hidden[:split], hidden[split:]]
        arrived = [[moving[0]], [moving[1]]]
        sources = [tensor_rank]
        for s in range(n - 1):
            sources.append(ring[(pos - sign * (s + 1)) % n])
            for i in range(2):
                moving[i] = lax.ppermute(moving[i], both, ring_pairs)
                arrived[i].append(moving[i])
        wholes = [jnp.concatenate(arrived[i], axis=1) for i in range(2)]
        norm_gain = jnp.concatenate(
            [lax.dynamic_slice_in_dim(norm_gain, src * feat, feat) for src in sources]
        )
        query_full = jnp.concatenate(
            [lax.dynamic_slice_in_dim(query_full, src * feat, feat, axis=0) for src in sources],
            axis=0,
        )
        kv_full = jnp.concatenate(
            [lax.dynamic_slice_in_dim(kv_full, src * feat, feat, axis=1) for src in sources],
            axis=1,
        )

        offsets, allowed = pair_layout(pair_lengths[0], premise_lengths[0], total_rows)
        low = tensor_rank < n // 2
        even = tensor_rank % 2 == 0
        pairs_a = [(s, 2 * s) if s < n // 2 else (s, 2 * (s - n // 2) + 1) for s in range(n)]
        pairs_b = [(s, 2 * s + 1) if s < n // 2 else (s, 2 * (s - n // 2)) for s in range(n)]
        contract = (((1,), (1,)), ((), ()))
        query_parts, key_parts, value_parts = [], [], []
        for i in range(2):
            rows_float = wholes[i].astype(jnp.float32)
            mean_square = jnp.mean(rows_float * rows_float, axis=-1, keepdims=True)
            normed = (rows_float * lax.rsqrt(mean_square + 1e-05) * norm_gain).astype(jnp.bfloat16)
            query_parts.append(jnp.dot(normed, query_full, preferred_element_type=jnp.float32))
            kv_piece = lax.dot_general(
                normed, kv_full, contract, preferred_element_type=jnp.float32
            ).astype(jnp.bfloat16)
            lo_cols = kv_piece[:, :HD]
            hi_cols = kv_piece[:, HD:]
            got_a = lax.ppermute(jnp.where(low, lo_cols, hi_cols), "tensor", pairs_a)
            got_b = lax.ppermute(jnp.where(low, hi_cols, lo_cols), "tensor", pairs_b)
            key_parts.append(jnp.where(even, got_a, got_b))
            value_parts.append(jnp.where(even, got_b, got_a))
        queries_raw = jnp.concatenate(query_parts, axis=0)
        key_head = jnp.concatenate(key_parts, axis=0)
        value_head = jnp.concatenate(value_parts, axis=0)

        queries = rotate_pairs(queries_raw.reshape(total_rows, head_local, HD), offsets).astype(
            jnp.bfloat16
        )
        keys = rotate_pairs(key_head.astype(jnp.float32)[:, None, :], offsets)[:, 0, :].astype(
            jnp.bfloat16
        )
        scale = HD ** (-0.5)
        starts = [0, split]
        sizes = [split, total_rows - split]

        def context_rows(i, q_rows):
            mask = lax.slice_in_dim(allowed, starts[i], starts[i] + sizes[i], axis=0)
            scores = jnp.einsum("qhd,kd->hqk", q_rows, keys, preferred_element_type=jnp.float32) * scale
            weighted = jnp.where(mask[None, :, :], jnp.exp(scores), 0.0)
            probs = (weighted / jnp.sum(weighted, axis=-1, keepdims=True)).astype(jnp.bfloat16)
            context = jnp.einsum(
                "hqk,kd->qhd", probs, value_head, preferred_element_type=jnp.float32
            ).astype(jnp.bfloat16)
            return context.reshape(sizes[i], head_local * HD)

        keep_step = out_raw.shape[1] // out_keep_full.shape[1]

        def chunk_weight(dest_pos):
            col = ring[dest_pos % n] * feat
            cols = lax.dynamic_slice_in_dim(out_raw, col, feat, axis=1)
            keep = lax.dynamic_slice_in_dim(out_keep_full, col // keep_step, feat // keep_step, axis=1)
            return fast_prune(cols, keep)

        weights_by_step = [chunk_weight(pos + sign * (n - 1 - s)) for s in range(n)]
        parts = []
        for i in range(2):
            q_rows = lax.slice_in_dim(queries, starts[i], starts[i] + sizes[i], axis=0)
            if i > 0:
                q_rows, _ = lax.optimization_barrier((q_rows, parts[0][0]))
            context = context_rows(i, q_rows)
            mine = [
                jnp.dot(context, weights_by_step[s], preferred_element_type=jnp.float32)
                for s in range(n)
            ]
            parts.append([mine[0].astype(jnp.bfloat16)] + lax.optimization_barrier(mine[1:]))
        acc = [None, None]
        for s in range(n - 1):
            for i in range(2):
                if acc[i] is None:
                    send = parts[i][0]
                else:
                    send = (parts[i][s] + acc[i].astype(jnp.float32)).astype(jnp.bfloat16)
                acc[i] = lax.ppermute(send, both, ring_pairs)
        total = jnp.concatenate(
            [parts[i][n - 1] + acc[i].astype(jnp.float32) for i in range(2)], axis=0
        )
        return total.astype(jnp.bfloat16)

    return on_device


def generic(
    hidden,
    norm_gain,
    query_weight,
    query_keep,
    kv_weight,
    out_weight,
    out_keep,
    pair_lengths,
    premise_lengths,
):
    tensor_rank = lax.axis_index("tensor")
    total_rows = hidden.shape[0]
    head_local = query_weight.shape[1] // HD
    query_pruned = prune(query_weight, query_keep)
    out_pruned = prune(out_weight, out_keep)
    query_full = lax.all_gather(query_pruned, "dp", axis=0, tiled=True)
    kv_full, out_full = (
        lax.all_gather(kv_weight, "dp", axis=1, tiled=True),
        lax.all_gather(out_pruned, "dp", axis=1, tiled=True),
    )
    whole = lax.all_gather(hidden, "tensor", axis=1, tiled=True)
    rows_float = whole.astype(jnp.float32)
    mean_square = jnp.mean(rows_float * rows_float, axis=-1, keepdims=True)
    normed = (rows_float * lax.rsqrt(mean_square + 1e-05) * norm_gain).astype(jnp.bfloat16)
    queries_raw = jnp.dot(normed, query_full, preferred_element_type=jnp.float32)
    kv_piece = lax.dot_general(
        normed, kv_full, (((1,), (1,)), ((), ())), preferred_element_type=jnp.float32
    ).astype(jnp.bfloat16)
    kv_whole = lax.all_gather(kv_piece, "tensor", axis=1, tiled=True)
    offsets, allowed = pair_layout(pair_lengths[0], premise_lengths[0], total_rows)
    queries = rotate_pairs(queries_raw.reshape(total_rows, head_local, HD), offsets).astype(
        jnp.bfloat16
    )
    keys_all = rotate_pairs(
        kv_whole[:, : KVH * HD].reshape(total_rows, KVH, HD).astype(jnp.float32), offsets
    ).astype(jnp.bfloat16)
    values_all = kv_whole[:, KVH * HD :].reshape(total_rows, KVH, HD)
    chosen = (tensor_rank * head_local + jnp.arange(head_local, dtype=jnp.int32)) // (HEADS // KVH)
    keys_used = jnp.take(keys_all, chosen, axis=1)
    values_used = jnp.take(values_all, chosen, axis=1)
    scale = HD ** (-0.5)
    scores = (
        jnp.einsum("qhd,khd->hqk", queries, keys_used, preferred_element_type=jnp.float32) * scale
    )
    weighted = jnp.where(allowed[None, :, :], jnp.exp(scores), 0.0)
    probs = (weighted / jnp.sum(weighted, axis=-1, keepdims=True)).astype(jnp.bfloat16)
    context = jnp.einsum(
        "hqk,khd->qhd", probs, values_used, preferred_element_type=jnp.float32
    ).astype(jnp.bfloat16)
    context = context.reshape(total_rows, head_local * HD)
    terms = jnp.dot(context, out_full, preferred_element_type=jnp.float32)
    mixed = lax.psum_scatter(terms, "tensor", scatter_dimension=1, tiled=True)
    return mixed.astype(jnp.bfloat16)


def solution(mesh):
    placed = (
        P(("groups", "dp"), "tensor"),
        P(),
        P("dp", "tensor"),
        P("dp", "tensor"),
        P("tensor", "dp"),
        P("tensor", "dp"),
        P("tensor", "dp"),
        P(("groups", "dp"), None),
        P(("groups", "dp"), None),
    )
    n = mesh.shape["tensor"]
    if n == KVH and mesh.shape["dp"] == 2:
        coords = [getattr(d, "coords", None) for d in mesh.devices.reshape(-1)]
        z_size, x_size = n, 1
        if all(c is not None for c in coords):
            xs = sorted({c[0] for c in coords})
            zs = sorted({c[2] for c in coords})
            if len(xs) * len(zs) == n:
                z_size, x_size = len(zs), len(xs)
        body = make_fast(n, ring_order(z_size, x_size))
    else:
        body = generic
    return jax.shard_map(
        body,
        mesh=mesh,
        in_specs=placed,
        out_specs=P(("groups", "dp"), "tensor"),
        check_vma=False,
    )
```

```python
import jax
import jax.numpy as jnp
import numpy as np
from jax import lax
from jax.sharding import PartitionSpec as P

HEADS = 64
KVH = 8
HD = 128


def rotate_pairs(values, positions):
    half_width = values.shape[-1] // 2
    inverse = 500000.0 ** (-(jnp.arange(half_width, dtype=jnp.float32) * 2.0 / values.shape[-1]))
    angles = positions[:, None] * inverse[None, :]
    cosine = jnp.cos(angles)[:, None, :]
    sine_part = jnp.sin(angles)[:, None, :]
    first_half = values[..., :half_width]
    second_half = values[..., half_width:]
    return jnp.concatenate(
        [
            first_half * cosine - second_half * sine_part,
            second_half * cosine + first_half * sine_part,
        ],
        axis=-1,
    )


def pair_layout(lengths, premise, count):
    pair_ends = jnp.cumsum(lengths)
    pair_starts = pair_ends - lengths
    position = jnp.arange(count, dtype=jnp.int32)
    pair_index = jnp.sum((position[:, None] >= pair_ends[None, :]).astype(jnp.int32), axis=1)
    one_hot = (
        pair_index[:, None] == jnp.arange(lengths.shape[0], dtype=jnp.int32)[None, :]
    ).astype(jnp.int32)
    offset = position - jnp.sum(one_hot * pair_starts[None, :], axis=1)
    premise_used = jnp.minimum(premise, lengths - 1)
    in_premise = offset < jnp.sum(one_hot * premise_used[None, :], axis=1)
    allowed = (pair_index[:, None] == pair_index[None, :]) & (
        in_premise[None, :] | jnp.logical_not(in_premise)[:, None]
    )
    return (offset.astype(jnp.float32), allowed)


def prune(weight, keep):
    blocks = weight.reshape(
        keep.shape[0],
        weight.shape[0] // keep.shape[0],
        keep.shape[1],
        weight.shape[1] // keep.shape[1],
    )
    blocks = blocks * keep.astype(weight.dtype)[:, None, :, None]
    return blocks.reshape(weight.shape)


def ring_order(z_size, x_size):
    if x_size == 1 or z_size == 1:
        return list(range(z_size * x_size))
    cycle = [(z, 0) for z in range(z_size)]
    for step, z in enumerate(range(z_size - 1, -1, -1)):
        xs = list(range(1, x_size))
        cycle += [(z, x) for x in (xs if step % 2 == 0 else xs[::-1])]
    return [z * x_size + x for z, x in cycle]


def fast_prune(weight, keep):
    rows, cols = weight.shape
    step_r, step_c = rows // keep.shape[0], cols // keep.shape[1]
    mask = jnp.repeat(keep.astype(weight.dtype), step_c, axis=1)
    return (weight.reshape(keep.shape[0], step_r, cols) * mask[:, None, :]).reshape(rows, cols)


def make_fast(n, order):
    position_of = np.zeros(n, np.int32)
    for p, t in enumerate(order):
        position_of[t] = p
    order_arr = np.asarray(order, np.int32)
    both = ("tensor", "dp")
    ring_pairs = [(order[i] * 2, order[(i + 1) % n] * 2) for i in range(n)] + [
        (order[i] * 2 + 1, order[(i - 1) % n] * 2 + 1) for i in range(n)
    ]

    def on_device(
        hidden,
        norm_gain,
        query_weight,
        query_keep,
        kv_weight,
        out_weight,
        out_keep,
        pair_lengths,
        premise_lengths,
    ):
        tensor_rank = lax.axis_index("tensor")
        dp_rank = lax.axis_index("dp")
        pos = jnp.asarray(position_of)[tensor_rank]
        ring = jnp.asarray(order_arr)
        sign = 1 - 2 * dp_rank
        total_rows, feat = hidden.shape
        head_local = query_weight.shape[1] // HD

        swap = [(0, 1), (1, 0)]

        def full_over_dp(local, axis):
            other = lax.ppermute(local, "dp", swap)
            return jnp.where(
                dp_rank == 0,
                jnp.concatenate([local, other], axis=axis),
                jnp.concatenate([other, local], axis=axis),
            )

        query_full = fast_prune(full_over_dp(query_weight, 0), full_over_dp(query_keep, 0))
        kv_full = lax.all_gather(kv_weight, "dp", axis=1, tiled=True)
        out_full = fast_prune(
            lax.all_gather(out_weight, "dp", axis=1, tiled=True),
            lax.all_gather(out_keep, "dp", axis=1, tiled=True),
        )

        split = (total_rows // 2 + 7) // 8 * 8
        halves = [hidden[:split], hidden[split:]]
        wholes = []
        for half in halves:
            buf = jnp.zeros((half.shape[0], n * feat), hidden.dtype)
            wholes.append(lax.dynamic_update_slice(buf, half, (0, tensor_rank * feat)))
        moving = list(halves)
        for s in range(n - 1):
            src = ring[(pos - sign * (s + 1)) % n]
            for i in range(2):
                moving[i] = lax.ppermute(moving[i], both, ring_pairs)
                wholes[i] = lax.dynamic_update_slice(wholes[i], moving[i], (0, src * feat))

        offsets, allowed = pair_layout(pair_lengths[0], premise_lengths[0], total_rows)
        low = tensor_rank < n // 2
        even = tensor_rank % 2 == 0
        pairs_a = [(s, 2 * s) if s < n // 2 else (s, 2 * (s - n // 2) + 1) for s in range(n)]
        pairs_b = [(s, 2 * s + 1) if s < n // 2 else (s, 2 * (s - n // 2)) for s in range(n)]
        contract = (((1,), (1,)), ((), ()))
        query_parts, key_parts, value_parts = [], [], []
        for i in range(2):
            rows_float = wholes[i].astype(jnp.float32)
            mean_square = jnp.mean(rows_float * rows_float, axis=-1, keepdims=True)
            normed = (rows_float * lax.rsqrt(mean_square + 1e-05) * norm_gain).astype(jnp.bfloat16)
            query_parts.append(jnp.dot(normed, query_full, preferred_element_type=jnp.float32))
            kv_piece = lax.dot_general(
                normed, kv_full, contract, preferred_element_type=jnp.float32
            ).astype(jnp.bfloat16)
            lo_cols = kv_piece[:, :HD]
            hi_cols = kv_piece[:, HD:]
            got_a = lax.ppermute(jnp.where(low, lo_cols, hi_cols), "tensor", pairs_a)
            got_b = lax.ppermute(jnp.where(low, hi_cols, lo_cols), "tensor", pairs_b)
            key_parts.append(jnp.where(even, got_a, got_b))
            value_parts.append(jnp.where(even, got_b, got_a))
        queries_raw = jnp.concatenate(query_parts, axis=0)
        key_head = jnp.concatenate(key_parts, axis=0)
        value_head = jnp.concatenate(value_parts, axis=0)

        queries = rotate_pairs(queries_raw.reshape(total_rows, head_local, HD), offsets).astype(
            jnp.bfloat16
        )
        keys = rotate_pairs(key_head.astype(jnp.float32)[:, None, :], offsets)[:, 0, :].astype(
            jnp.bfloat16
        )
        scale = HD ** (-0.5)
        starts = [0, split]
        sizes = [split, total_rows - split]

        def context_rows(i, q_rows):
            mask = lax.slice_in_dim(allowed, starts[i], starts[i] + sizes[i], axis=0)
            scores = jnp.einsum("qhd,kd->hqk", q_rows, keys, preferred_element_type=jnp.float32) * scale
            weighted = jnp.where(mask[None, :, :], jnp.exp(scores), 0.0)
            probs = (weighted / jnp.sum(weighted, axis=-1, keepdims=True)).astype(jnp.bfloat16)
            context = jnp.einsum(
                "hqk,kd->qhd", probs, value_head, preferred_element_type=jnp.float32
            ).astype(jnp.bfloat16)
            return context.reshape(sizes[i], head_local * HD)

        def chunk(context, dest_pos):
            cols = lax.dynamic_slice_in_dim(out_full, ring[dest_pos % n] * feat, feat, axis=1)
            return jnp.dot(context, cols, preferred_element_type=jnp.float32)

        parts = []
        for i in range(2):
            q_rows = lax.slice_in_dim(queries, starts[i], starts[i] + sizes[i], axis=0)
            if i > 0:
                q_rows, _ = lax.optimization_barrier((q_rows, parts[0][0]))
            context = context_rows(i, q_rows)
            mine = [chunk(context, pos + sign * (n - 1 - s)) for s in range(n)]
            parts.append([mine[0].astype(jnp.bfloat16)] + lax.optimization_barrier(mine[1:]))
        acc = [None, None]
        for s in range(n - 1):
            for i in range(2):
                if acc[i] is None:
                    send = parts[i][0]
                else:
                    send = (parts[i][s] + acc[i].astype(jnp.float32)).astype(jnp.bfloat16)
                acc[i] = lax.ppermute(send, both, ring_pairs)
        total = jnp.concatenate(
            [parts[i][n - 1] + acc[i].astype(jnp.float32) for i in range(2)], axis=0
        )
        return total.astype(jnp.bfloat16)

    return on_device


def generic(
    hidden,
    norm_gain,
    query_weight,
    query_keep,
    kv_weight,
    out_weight,
    out_keep,
    pair_lengths,
    premise_lengths,
):
    tensor_rank = lax.axis_index("tensor")
    total_rows = hidden.shape[0]
    head_local = query_weight.shape[1] // HD
    query_pruned = prune(query_weight, query_keep)
    out_pruned = prune(out_weight, out_keep)
    query_full = lax.all_gather(query_pruned, "dp", axis=0, tiled=True)
    kv_full, out_full = (
        lax.all_gather(kv_weight, "dp", axis=1, tiled=True),
        lax.all_gather(out_pruned, "dp", axis=1, tiled=True),
    )
    whole = lax.all_gather(hidden, "tensor", axis=1, tiled=True)
    rows_float = whole.astype(jnp.float32)
    mean_square = jnp.mean(rows_float * rows_float, axis=-1, keepdims=True)
    normed = (rows_float * lax.rsqrt(mean_square + 1e-05) * norm_gain).astype(jnp.bfloat16)
    queries_raw = jnp.dot(normed, query_full, preferred_element_type=jnp.float32)
    kv_piece = lax.dot_general(
        normed, kv_full, (((1,), (1,)), ((), ())), preferred_element_type=jnp.float32
    ).astype(jnp.bfloat16)
    kv_whole = lax.all_gather(kv_piece, "tensor", axis=1, tiled=True)
    offsets, allowed = pair_layout(pair_lengths[0], premise_lengths[0], total_rows)
    queries = rotate_pairs(queries_raw.reshape(total_rows, head_local, HD), offsets).astype(
        jnp.bfloat16
    )
    keys_all = rotate_pairs(
        kv_whole[:, : KVH * HD].reshape(total_rows, KVH, HD).astype(jnp.float32), offsets
    ).astype(jnp.bfloat16)
    values_all = kv_whole[:, KVH * HD :].reshape(total_rows, KVH, HD)
    chosen = (tensor_rank * head_local + jnp.arange(head_local, dtype=jnp.int32)) // (HEADS // KVH)
    keys_used = jnp.take(keys_all, chosen, axis=1)
    values_used = jnp.take(values_all, chosen, axis=1)
    scale = HD ** (-0.5)
    scores = (
        jnp.einsum("qhd,khd->hqk", queries, keys_used, preferred_element_type=jnp.float32) * scale
    )
    weighted = jnp.where(allowed[None, :, :], jnp.exp(scores), 0.0)
    probs = (weighted / jnp.sum(weighted, axis=-1, keepdims=True)).astype(jnp.bfloat16)
    context = jnp.einsum(
        "hqk,khd->qhd", probs, values_used, preferred_element_type=jnp.float32
    ).astype(jnp.bfloat16)
    context = context.reshape(total_rows, head_local * HD)
    terms = jnp.dot(context, out_full, preferred_element_type=jnp.float32)
    mixed = lax.psum_scatter(terms, "tensor", scatter_dimension=1, tiled=True)
    return mixed.astype(jnp.bfloat16)


def solution(mesh):
    placed = (
        P(("groups", "dp"), "tensor"),
        P(),
        P("dp", "tensor"),
        P("dp", "tensor"),
        P("tensor", "dp"),
        P("tensor", "dp"),
        P("tensor", "dp"),
        P(("groups", "dp"), None),
        P(("groups", "dp"), None),
    )
    n = mesh.shape["tensor"]
    if n == KVH and mesh.shape["dp"] == 2:
        coords = [getattr(d, "coords", None) for d in mesh.devices.reshape(-1)]
        z_size, x_size = n, 1
        if all(c is not None for c in coords):
            xs = sorted({c[0] for c in coords})
            zs = sorted({c[2] for c in coords})
            if len(xs) * len(zs) == n:
                z_size, x_size = len(zs), len(xs)
        body = make_fast(n, ring_order(z_size, x_size))
    else:
        body = generic
    return jax.shard_map(
        body,
        mesh=mesh,
        in_specs=placed,
        out_specs=P(("groups", "dp"), "tensor"),
        check_vma=False,
    )
```

```python
import jax
import jax.numpy as jnp
import numpy as np
from jax import lax
from jax.sharding import PartitionSpec as P

HEADS = 64
KVH = 8
HD = 128


def rotate_pairs(values, positions):
    half_width = values.shape[-1] // 2
    inverse = 500000.0 ** (-(jnp.arange(half_width, dtype=jnp.float32) * 2.0 / values.shape[-1]))
    angles = positions[:, None] * inverse[None, :]
    cosine = jnp.cos(angles)[:, None, :]
    sine_part = jnp.sin(angles)[:, None, :]
    first_half = values[..., :half_width]
    second_half = values[..., half_width:]
    return jnp.concatenate(
        [
            first_half * cosine - second_half * sine_part,
            second_half * cosine + first_half * sine_part,
        ],
        axis=-1,
    )


def pair_layout(lengths, premise, count):
    pair_ends = jnp.cumsum(lengths)
    pair_starts = pair_ends - lengths
    position = jnp.arange(count, dtype=jnp.int32)
    pair_index = jnp.sum((position[:, None] >= pair_ends[None, :]).astype(jnp.int32), axis=1)
    one_hot = (
        pair_index[:, None] == jnp.arange(lengths.shape[0], dtype=jnp.int32)[None, :]
    ).astype(jnp.int32)
    offset = position - jnp.sum(one_hot * pair_starts[None, :], axis=1)
    premise_used = jnp.minimum(premise, lengths - 1)
    in_premise = offset < jnp.sum(one_hot * premise_used[None, :], axis=1)
    allowed = (pair_index[:, None] == pair_index[None, :]) & (
        in_premise[None, :] | jnp.logical_not(in_premise)[:, None]
    )
    return (offset.astype(jnp.float32), allowed)


def prune(weight, keep):
    blocks = weight.reshape(
        keep.shape[0],
        weight.shape[0] // keep.shape[0],
        keep.shape[1],
        weight.shape[1] // keep.shape[1],
    )
    blocks = blocks * keep.astype(weight.dtype)[:, None, :, None]
    return blocks.reshape(weight.shape)


def ring_order(z_size, x_size):
    if x_size == 1 or z_size == 1:
        return list(range(z_size * x_size))
    cycle = [(z, 0) for z in range(z_size)]
    for step, z in enumerate(range(z_size - 1, -1, -1)):
        xs = list(range(1, x_size))
        cycle += [(z, x) for x in (xs if step % 2 == 0 else xs[::-1])]
    return [z * x_size + x for z, x in cycle]


def fast_prune(weight, keep):
    rows, cols = weight.shape
    step_r, step_c = rows // keep.shape[0], cols // keep.shape[1]
    mask = jnp.repeat(keep.astype(weight.dtype), step_c, axis=1)
    return (weight.reshape(keep.shape[0], step_r, cols) * mask[:, None, :]).reshape(rows, cols)


def make_fast(n, order):
    position_of = np.zeros(n, np.int32)
    for p, t in enumerate(order):
        position_of[t] = p
    order_arr = np.asarray(order, np.int32)
    both = ("tensor", "dp")
    ring_pairs = [(order[i] * 2, order[(i + 1) % n] * 2) for i in range(n)] + [
        (order[i] * 2 + 1, order[(i - 1) % n] * 2 + 1) for i in range(n)
    ]

    def on_device(
        hidden,
        norm_gain,
        query_weight,
        query_keep,
        kv_weight,
        out_weight,
        out_keep,
        pair_lengths,
        premise_lengths,
    ):
        tensor_rank = lax.axis_index("tensor")
        dp_rank = lax.axis_index("dp")
        pos = jnp.asarray(position_of)[tensor_rank]
        ring = jnp.asarray(order_arr)
        sign = 1 - 2 * dp_rank
        total_rows, feat = hidden.shape
        head_local = query_weight.shape[1] // HD

        swap = [(0, 1), (1, 0)]

        def full_over_dp(local, axis):
            other = lax.ppermute(local, "dp", swap)
            return jnp.where(
                dp_rank == 0,
                jnp.concatenate([local, other], axis=axis),
                jnp.concatenate([other, local], axis=axis),
            )

        query_full = fast_prune(full_over_dp(query_weight, 0), full_over_dp(query_keep, 0))
        kv_full = lax.all_gather(kv_weight, "dp", axis=1, tiled=True)
        out_full = fast_prune(full_over_dp(out_weight, 1), full_over_dp(out_keep, 1))

        split = (total_rows // 2 + 7) // 8 * 8
        halves = [hidden[:split], hidden[split:]]
        wholes = []
        for half in halves:
            buf = jnp.zeros((half.shape[0], n * feat), hidden.dtype)
            wholes.append(lax.dynamic_update_slice(buf, half, (0, tensor_rank * feat)))
        moving = list(halves)
        for s in range(n - 1):
            src = ring[(pos - sign * (s + 1)) % n]
            for i in range(2):
                moving[i] = lax.ppermute(moving[i], both, ring_pairs)
                wholes[i] = lax.dynamic_update_slice(wholes[i], moving[i], (0, src * feat))

        offsets, allowed = pair_layout(pair_lengths[0], premise_lengths[0], total_rows)
        low = tensor_rank < n // 2
        even = tensor_rank % 2 == 0
        pairs_a = [(s, 2 * s) if s < n // 2 else (s, 2 * (s - n // 2) + 1) for s in range(n)]
        pairs_b = [(s, 2 * s + 1) if s < n // 2 else (s, 2 * (s - n // 2)) for s in range(n)]
        contract = (((1,), (1,)), ((), ()))
        query_parts, key_parts, value_parts = [], [], []
        for i in range(2):
            rows_float = wholes[i].astype(jnp.float32)
            mean_square = jnp.mean(rows_float * rows_float, axis=-1, keepdims=True)
            normed = (rows_float * lax.rsqrt(mean_square + 1e-05) * norm_gain).astype(jnp.bfloat16)
            query_parts.append(jnp.dot(normed, query_full, preferred_element_type=jnp.float32))
            kv_piece = lax.dot_general(
                normed, kv_full, contract, preferred_element_type=jnp.float32
            ).astype(jnp.bfloat16)
            lo_cols = kv_piece[:, :HD]
            hi_cols = kv_piece[:, HD:]
            got_a = lax.ppermute(jnp.where(low, lo_cols, hi_cols), "tensor", pairs_a)
            got_b = lax.ppermute(jnp.where(low, hi_cols, lo_cols), "tensor", pairs_b)
            key_parts.append(jnp.where(even, got_a, got_b))
            value_parts.append(jnp.where(even, got_b, got_a))
        queries_raw = jnp.concatenate(query_parts, axis=0)
        key_head = jnp.concatenate(key_parts, axis=0)
        value_head = jnp.concatenate(value_parts, axis=0)

        queries = rotate_pairs(queries_raw.reshape(total_rows, head_local, HD), offsets).astype(
            jnp.bfloat16
        )
        keys = rotate_pairs(key_head.astype(jnp.float32)[:, None, :], offsets)[:, 0, :].astype(
            jnp.bfloat16
        )
        scale = HD ** (-0.5)
        starts = [0, split]
        sizes = [split, total_rows - split]

        def context_rows(i, q_rows):
            mask = lax.slice_in_dim(allowed, starts[i], starts[i] + sizes[i], axis=0)
            scores = jnp.einsum("qhd,kd->hqk", q_rows, keys, preferred_element_type=jnp.float32) * scale
            weighted = jnp.where(mask[None, :, :], jnp.exp(scores), 0.0)
            probs = (weighted / jnp.sum(weighted, axis=-1, keepdims=True)).astype(jnp.bfloat16)
            context = jnp.einsum(
                "hqk,kd->qhd", probs, value_head, preferred_element_type=jnp.float32
            ).astype(jnp.bfloat16)
            return context.reshape(sizes[i], head_local * HD)

        def chunk(context, dest_pos):
            cols = lax.dynamic_slice_in_dim(out_full, ring[dest_pos % n] * feat, feat, axis=1)
            return jnp.dot(context, cols, preferred_element_type=jnp.float32)

        parts = []
        for i in range(2):
            q_rows = lax.slice_in_dim(queries, starts[i], starts[i] + sizes[i], axis=0)
            if i > 0:
                q_rows, _ = lax.optimization_barrier((q_rows, parts[0][0]))
            context = context_rows(i, q_rows)
            mine = [chunk(context, pos + sign * (n - 1 - s)) for s in range(n)]
            parts.append([mine[0].astype(jnp.bfloat16)] + lax.optimization_barrier(mine[1:]))
        acc = [None, None]
        for s in range(n - 1):
            for i in range(2):
                if acc[i] is None:
                    send = parts[i][0]
                else:
                    send = (parts[i][s] + acc[i].astype(jnp.float32)).astype(jnp.bfloat16)
                acc[i] = lax.ppermute(send, both, ring_pairs)
        total = jnp.concatenate(
            [parts[i][n - 1] + acc[i].astype(jnp.float32) for i in range(2)], axis=0
        )
        return total.astype(jnp.bfloat16)

    return on_device


def generic(
    hidden,
    norm_gain,
    query_weight,
    query_keep,
    kv_weight,
    out_weight,
    out_keep,
    pair_lengths,
    premise_lengths,
):
    tensor_rank = lax.axis_index("tensor")
    total_rows = hidden.shape[0]
    head_local = query_weight.shape[1] // HD
    query_pruned = prune(query_weight, query_keep)
    out_pruned = prune(out_weight, out_keep)
    query_full = lax.all_gather(query_pruned, "dp", axis=0, tiled=True)
    kv_full, out_full = (
        lax.all_gather(kv_weight, "dp", axis=1, tiled=True),
        lax.all_gather(out_pruned, "dp", axis=1, tiled=True),
    )
    whole = lax.all_gather(hidden, "tensor", axis=1, tiled=True)
    rows_float = whole.astype(jnp.float32)
    mean_square = jnp.mean(rows_float * rows_float, axis=-1, keepdims=True)
    normed = (rows_float * lax.rsqrt(mean_square + 1e-05) * norm_gain).astype(jnp.bfloat16)
    queries_raw = jnp.dot(normed, query_full, preferred_element_type=jnp.float32)
    kv_piece = lax.dot_general(
        normed, kv_full, (((1,), (1,)), ((), ())), preferred_element_type=jnp.float32
    ).astype(jnp.bfloat16)
    kv_whole = lax.all_gather(kv_piece, "tensor", axis=1, tiled=True)
    offsets, allowed = pair_layout(pair_lengths[0], premise_lengths[0], total_rows)
    queries = rotate_pairs(queries_raw.reshape(total_rows, head_local, HD), offsets).astype(
        jnp.bfloat16
    )
    keys_all = rotate_pairs(
        kv_whole[:, : KVH * HD].reshape(total_rows, KVH, HD).astype(jnp.float32), offsets
    ).astype(jnp.bfloat16)
    values_all = kv_whole[:, KVH * HD :].reshape(total_rows, KVH, HD)
    chosen = (tensor_rank * head_local + jnp.arange(head_local, dtype=jnp.int32)) // (HEADS // KVH)
    keys_used = jnp.take(keys_all, chosen, axis=1)
    values_used = jnp.take(values_all, chosen, axis=1)
    scale = HD ** (-0.5)
    scores = (
        jnp.einsum("qhd,khd->hqk", queries, keys_used, preferred_element_type=jnp.float32) * scale
    )
    weighted = jnp.where(allowed[None, :, :], jnp.exp(scores), 0.0)
    probs = (weighted / jnp.sum(weighted, axis=-1, keepdims=True)).astype(jnp.bfloat16)
    context = jnp.einsum(
        "hqk,khd->qhd", probs, values_used, preferred_element_type=jnp.float32
    ).astype(jnp.bfloat16)
    context = context.reshape(total_rows, head_local * HD)
    terms = jnp.dot(context, out_full, preferred_element_type=jnp.float32)
    mixed = lax.psum_scatter(terms, "tensor", scatter_dimension=1, tiled=True)
    return mixed.astype(jnp.bfloat16)


def solution(mesh):
    placed = (
        P(("groups", "dp"), "tensor"),
        P(),
        P("dp", "tensor"),
        P("dp", "tensor"),
        P("tensor", "dp"),
        P("tensor", "dp"),
        P("tensor", "dp"),
        P(("groups", "dp"), None),
        P(("groups", "dp"), None),
    )
    n = mesh.shape["tensor"]
    if n == KVH and mesh.shape["dp"] == 2:
        coords = [getattr(d, "coords", None) for d in mesh.devices.reshape(-1)]
        z_size, x_size = n, 1
        if all(c is not None for c in coords):
            xs = sorted({c[0] for c in coords})
            zs = sorted({c[2] for c in coords})
            if len(xs) * len(zs) == n:
                z_size, x_size = len(zs), len(xs)
        body = make_fast(n, ring_order(z_size, x_size))
    else:
        body = generic
    return jax.shard_map(
        body,
        mesh=mesh,
        in_specs=placed,
        out_specs=P(("groups", "dp"), "tensor"),
        check_vma=False,
    )
```

```python
import jax
import jax.numpy as jnp
import numpy as np
from jax import lax
from jax.sharding import PartitionSpec as P

HEADS = 64
KVH = 8
HD = 128


def rotate_pairs(values, positions):
    half_width = values.shape[-1] // 2
    inverse = 500000.0 ** (-(jnp.arange(half_width, dtype=jnp.float32) * 2.0 / values.shape[-1]))
    angles = positions[:, None] * inverse[None, :]
    cosine = jnp.cos(angles)[:, None, :]
    sine_part = jnp.sin(angles)[:, None, :]
    first_half = values[..., :half_width]
    second_half = values[..., half_width:]
    return jnp.concatenate(
        [
            first_half * cosine - second_half * sine_part,
            second_half * cosine + first_half * sine_part,
        ],
        axis=-1,
    )


def pair_layout(lengths, premise, count):
    pair_ends = jnp.cumsum(lengths)
    pair_starts = pair_ends - lengths
    position = jnp.arange(count, dtype=jnp.int32)
    pair_index = jnp.sum((position[:, None] >= pair_ends[None, :]).astype(jnp.int32), axis=1)
    one_hot = (
        pair_index[:, None] == jnp.arange(lengths.shape[0], dtype=jnp.int32)[None, :]
    ).astype(jnp.int32)
    offset = position - jnp.sum(one_hot * pair_starts[None, :], axis=1)
    premise_used = jnp.minimum(premise, lengths - 1)
    in_premise = offset < jnp.sum(one_hot * premise_used[None, :], axis=1)
    allowed = (pair_index[:, None] == pair_index[None, :]) & (
        in_premise[None, :] | jnp.logical_not(in_premise)[:, None]
    )
    return (offset.astype(jnp.float32), allowed)


def prune(weight, keep):
    blocks = weight.reshape(
        keep.shape[0],
        weight.shape[0] // keep.shape[0],
        keep.shape[1],
        weight.shape[1] // keep.shape[1],
    )
    blocks = blocks * keep.astype(weight.dtype)[:, None, :, None]
    return blocks.reshape(weight.shape)


def ring_order(z_size, x_size):
    if x_size == 1 or z_size == 1:
        return list(range(z_size * x_size))
    cycle = [(z, 0) for z in range(z_size)]
    for step, z in enumerate(range(z_size - 1, -1, -1)):
        xs = list(range(1, x_size))
        cycle += [(z, x) for x in (xs if step % 2 == 0 else xs[::-1])]
    return [z * x_size + x for z, x in cycle]


def fast_prune(weight, keep):
    rows, cols = weight.shape
    step_r, step_c = rows // keep.shape[0], cols // keep.shape[1]
    mask = jnp.repeat(keep.astype(weight.dtype), step_c, axis=1)
    return (weight.reshape(keep.shape[0], step_r, cols) * mask[:, None, :]).reshape(rows, cols)


def make_fast(n, order):
    position_of = np.zeros(n, np.int32)
    for p, t in enumerate(order):
        position_of[t] = p
    order_arr = np.asarray(order, np.int32)
    both = ("tensor", "dp")
    ring_pairs = [(order[i] * 2, order[(i + 1) % n] * 2) for i in range(n)] + [
        (order[i] * 2 + 1, order[(i - 1) % n] * 2 + 1) for i in range(n)
    ]

    def on_device(
        hidden,
        norm_gain,
        query_weight,
        query_keep,
        kv_weight,
        out_weight,
        out_keep,
        pair_lengths,
        premise_lengths,
    ):
        tensor_rank = lax.axis_index("tensor")
        dp_rank = lax.axis_index("dp")
        pos = jnp.asarray(position_of)[tensor_rank]
        ring = jnp.asarray(order_arr)
        sign = 1 - 2 * dp_rank
        total_rows, feat = hidden.shape
        head_local = query_weight.shape[1] // HD

        swap = [(0, 1), (1, 0)]

        def full_over_dp(local, axis):
            other = lax.ppermute(local, "dp", swap)
            return jnp.where(
                dp_rank == 0,
                jnp.concatenate([local, other], axis=axis),
                jnp.concatenate([other, local], axis=axis),
            )

        query_full = fast_prune(full_over_dp(query_weight, 0), full_over_dp(query_keep, 0))
        kv_full = lax.all_gather(kv_weight, "dp", axis=1, tiled=True)

        split = (total_rows // 2 + 7) // 8 * 8
        halves = [hidden[:split], hidden[split:]]
        wholes = []
        for half in halves:
            buf = jnp.zeros((half.shape[0], n * feat), hidden.dtype)
            wholes.append(lax.dynamic_update_slice(buf, half, (0, tensor_rank * feat)))
        moving = list(halves)
        for s in range(n - 1):
            src = ring[(pos - sign * (s + 1)) % n]
            for i in range(2):
                moving[i] = lax.ppermute(moving[i], both, ring_pairs)
                wholes[i] = lax.dynamic_update_slice(wholes[i], moving[i], (0, src * feat))

        wholes[1], out_weight, out_keep = lax.optimization_barrier((wholes[1], out_weight, out_keep))
        out_full = fast_prune(
            lax.all_gather(out_weight, "dp", axis=1, tiled=True),
            lax.all_gather(out_keep, "dp", axis=1, tiled=True),
        )

        offsets, allowed = pair_layout(pair_lengths[0], premise_lengths[0], total_rows)
        low = tensor_rank < n // 2
        even = tensor_rank % 2 == 0
        pairs_a = [(s, 2 * s) if s < n // 2 else (s, 2 * (s - n // 2) + 1) for s in range(n)]
        pairs_b = [(s, 2 * s + 1) if s < n // 2 else (s, 2 * (s - n // 2)) for s in range(n)]
        contract = (((1,), (1,)), ((), ()))
        query_parts, key_parts, value_parts = [], [], []
        for i in range(2):
            rows_float = wholes[i].astype(jnp.float32)
            mean_square = jnp.mean(rows_float * rows_float, axis=-1, keepdims=True)
            normed = (rows_float * lax.rsqrt(mean_square + 1e-05) * norm_gain).astype(jnp.bfloat16)
            query_parts.append(jnp.dot(normed, query_full, preferred_element_type=jnp.float32))
            kv_piece = lax.dot_general(
                normed, kv_full, contract, preferred_element_type=jnp.float32
            ).astype(jnp.bfloat16)
            lo_cols = kv_piece[:, :HD]
            hi_cols = kv_piece[:, HD:]
            got_a = lax.ppermute(jnp.where(low, lo_cols, hi_cols), "tensor", pairs_a)
            got_b = lax.ppermute(jnp.where(low, hi_cols, lo_cols), "tensor", pairs_b)
            key_parts.append(jnp.where(even, got_a, got_b))
            value_parts.append(jnp.where(even, got_b, got_a))
        queries_raw = jnp.concatenate(query_parts, axis=0)
        key_head = jnp.concatenate(key_parts, axis=0)
        value_head = jnp.concatenate(value_parts, axis=0)

        queries = rotate_pairs(queries_raw.reshape(total_rows, head_local, HD), offsets).astype(
            jnp.bfloat16
        )
        keys = rotate_pairs(key_head.astype(jnp.float32)[:, None, :], offsets)[:, 0, :].astype(
            jnp.bfloat16
        )
        scale = HD ** (-0.5)
        starts = [0, split]
        sizes = [split, total_rows - split]

        def context_rows(i, q_rows):
            mask = lax.slice_in_dim(allowed, starts[i], starts[i] + sizes[i], axis=0)
            scores = jnp.einsum("qhd,kd->hqk", q_rows, keys, preferred_element_type=jnp.float32) * scale
            weighted = jnp.where(mask[None, :, :], jnp.exp(scores), 0.0)
            probs = (weighted / jnp.sum(weighted, axis=-1, keepdims=True)).astype(jnp.bfloat16)
            context = jnp.einsum(
                "hqk,kd->qhd", probs, value_head, preferred_element_type=jnp.float32
            ).astype(jnp.bfloat16)
            return context.reshape(sizes[i], head_local * HD)

        def chunk(context, dest_pos):
            cols = lax.dynamic_slice_in_dim(out_full, ring[dest_pos % n] * feat, feat, axis=1)
            return jnp.dot(context, cols, preferred_element_type=jnp.float32)

        parts = []
        for i in range(2):
            q_rows = lax.slice_in_dim(queries, starts[i], starts[i] + sizes[i], axis=0)
            if i > 0:
                q_rows, _ = lax.optimization_barrier((q_rows, parts[0][0]))
            context = context_rows(i, q_rows)
            mine = [chunk(context, pos + sign * (n - 1 - s)) for s in range(n)]
            parts.append([mine[0].astype(jnp.bfloat16)] + lax.optimization_barrier(mine[1:]))
        acc = [None, None]
        for s in range(n - 1):
            for i in range(2):
                if acc[i] is None:
                    send = parts[i][0]
                else:
                    send = (parts[i][s] + acc[i].astype(jnp.float32)).astype(jnp.bfloat16)
                acc[i] = lax.ppermute(send, both, ring_pairs)
        total = jnp.concatenate(
            [parts[i][n - 1] + acc[i].astype(jnp.float32) for i in range(2)], axis=0
        )
        return total.astype(jnp.bfloat16)

    return on_device


def generic(
    hidden,
    norm_gain,
    query_weight,
    query_keep,
    kv_weight,
    out_weight,
    out_keep,
    pair_lengths,
    premise_lengths,
):
    tensor_rank = lax.axis_index("tensor")
    total_rows = hidden.shape[0]
    head_local = query_weight.shape[1] // HD
    query_pruned = prune(query_weight, query_keep)
    out_pruned = prune(out_weight, out_keep)
    query_full = lax.all_gather(query_pruned, "dp", axis=0, tiled=True)
    kv_full, out_full = (
        lax.all_gather(kv_weight, "dp", axis=1, tiled=True),
        lax.all_gather(out_pruned, "dp", axis=1, tiled=True),
    )
    whole = lax.all_gather(hidden, "tensor", axis=1, tiled=True)
    rows_float = whole.astype(jnp.float32)
    mean_square = jnp.mean(rows_float * rows_float, axis=-1, keepdims=True)
    normed = (rows_float * lax.rsqrt(mean_square + 1e-05) * norm_gain).astype(jnp.bfloat16)
    queries_raw = jnp.dot(normed, query_full, preferred_element_type=jnp.float32)
    kv_piece = lax.dot_general(
        normed, kv_full, (((1,), (1,)), ((), ())), preferred_element_type=jnp.float32
    ).astype(jnp.bfloat16)
    kv_whole = lax.all_gather(kv_piece, "tensor", axis=1, tiled=True)
    offsets, allowed = pair_layout(pair_lengths[0], premise_lengths[0], total_rows)
    queries = rotate_pairs(queries_raw.reshape(total_rows, head_local, HD), offsets).astype(
        jnp.bfloat16
    )
    keys_all = rotate_pairs(
        kv_whole[:, : KVH * HD].reshape(total_rows, KVH, HD).astype(jnp.float32), offsets
    ).astype(jnp.bfloat16)
    values_all = kv_whole[:, KVH * HD :].reshape(total_rows, KVH, HD)
    chosen = (tensor_rank * head_local + jnp.arange(head_local, dtype=jnp.int32)) // (HEADS // KVH)
    keys_used = jnp.take(keys_all, chosen, axis=1)
    values_used = jnp.take(values_all, chosen, axis=1)
    scale = HD ** (-0.5)
    scores = (
        jnp.einsum("qhd,khd->hqk", queries, keys_used, preferred_element_type=jnp.float32) * scale
    )
    weighted = jnp.where(allowed[None, :, :], jnp.exp(scores), 0.0)
    probs = (weighted / jnp.sum(weighted, axis=-1, keepdims=True)).astype(jnp.bfloat16)
    context = jnp.einsum(
        "hqk,khd->qhd", probs, values_used, preferred_element_type=jnp.float32
    ).astype(jnp.bfloat16)
    context = context.reshape(total_rows, head_local * HD)
    terms = jnp.dot(context, out_full, preferred_element_type=jnp.float32)
    mixed = lax.psum_scatter(terms, "tensor", scatter_dimension=1, tiled=True)
    return mixed.astype(jnp.bfloat16)


def solution(mesh):
    placed = (
        P(("groups", "dp"), "tensor"),
        P(),
        P("dp", "tensor"),
        P("dp", "tensor"),
        P("tensor", "dp"),
        P("tensor", "dp"),
        P("tensor", "dp"),
        P(("groups", "dp"), None),
        P(("groups", "dp"), None),
    )
    n = mesh.shape["tensor"]
    if n == KVH and mesh.shape["dp"] == 2:
        coords = [getattr(d, "coords", None) for d in mesh.devices.reshape(-1)]
        z_size, x_size = n, 1
        if all(c is not None for c in coords):
            xs = sorted({c[0] for c in coords})
            zs = sorted({c[2] for c in coords})
            if len(xs) * len(zs) == n:
                z_size, x_size = len(zs), len(xs)
        body = make_fast(n, ring_order(z_size, x_size))
    else:
        body = generic
    return jax.shard_map(
        body,
        mesh=mesh,
        in_specs=placed,
        out_specs=P(("groups", "dp"), "tensor"),
        check_vma=False,
    )
```

```python
import jax
import jax.numpy as jnp
import numpy as np
from jax import lax
from jax.sharding import PartitionSpec as P

HEADS = 64
KVH = 8
HD = 128


def rotate_pairs(values, positions):
    half_width = values.shape[-1] // 2
    inverse = 500000.0 ** (-(jnp.arange(half_width, dtype=jnp.float32) * 2.0 / values.shape[-1]))
    angles = positions[:, None] * inverse[None, :]
    cosine = jnp.cos(angles)[:, None, :]
    sine_part = jnp.sin(angles)[:, None, :]
    first_half = values[..., :half_width]
    second_half = values[..., half_width:]
    return jnp.concatenate(
        [
            first_half * cosine - second_half * sine_part,
            second_half * cosine + first_half * sine_part,
        ],
        axis=-1,
    )


def pair_layout(lengths, premise, count):
    pair_ends = jnp.cumsum(lengths)
    pair_starts = pair_ends - lengths
    position = jnp.arange(count, dtype=jnp.int32)
    pair_index = jnp.sum((position[:, None] >= pair_ends[None, :]).astype(jnp.int32), axis=1)
    one_hot = (
        pair_index[:, None] == jnp.arange(lengths.shape[0], dtype=jnp.int32)[None, :]
    ).astype(jnp.int32)
    offset = position - jnp.sum(one_hot * pair_starts[None, :], axis=1)
    premise_used = jnp.minimum(premise, lengths - 1)
    in_premise = offset < jnp.sum(one_hot * premise_used[None, :], axis=1)
    allowed = (pair_index[:, None] == pair_index[None, :]) & (
        in_premise[None, :] | jnp.logical_not(in_premise)[:, None]
    )
    return (offset.astype(jnp.float32), allowed)


def prune(weight, keep):
    blocks = weight.reshape(
        keep.shape[0],
        weight.shape[0] // keep.shape[0],
        keep.shape[1],
        weight.shape[1] // keep.shape[1],
    )
    blocks = blocks * keep.astype(weight.dtype)[:, None, :, None]
    return blocks.reshape(weight.shape)


def ring_order(z_size, x_size):
    if x_size == 1 or z_size == 1:
        return list(range(z_size * x_size))
    cycle = [(z, 0) for z in range(z_size)]
    for step, z in enumerate(range(z_size - 1, -1, -1)):
        xs = list(range(1, x_size))
        cycle += [(z, x) for x in (xs if step % 2 == 0 else xs[::-1])]
    return [z * x_size + x for z, x in cycle]


def fast_prune(weight, keep):
    rows, cols = weight.shape
    step_r, step_c = rows // keep.shape[0], cols // keep.shape[1]
    mask = jnp.repeat(keep.astype(weight.dtype), step_c, axis=1)
    return (weight.reshape(keep.shape[0], step_r, cols) * mask[:, None, :]).reshape(rows, cols)


def make_fast(n, order):
    position_of = np.zeros(n, np.int32)
    for p, t in enumerate(order):
        position_of[t] = p
    order_arr = np.asarray(order, np.int32)
    both = ("tensor", "dp")
    ring_pairs = [(order[i] * 2, order[(i + 1) % n] * 2) for i in range(n)] + [
        (order[i] * 2 + 1, order[(i - 1) % n] * 2 + 1) for i in range(n)
    ]

    def on_device(
        hidden,
        norm_gain,
        query_weight,
        query_keep,
        kv_weight,
        out_weight,
        out_keep,
        pair_lengths,
        premise_lengths,
    ):
        tensor_rank = lax.axis_index("tensor")
        dp_rank = lax.axis_index("dp")
        pos = jnp.asarray(position_of)[tensor_rank]
        ring = jnp.asarray(order_arr)
        sign = 1 - 2 * dp_rank
        total_rows, feat = hidden.shape
        head_local = query_weight.shape[1] // HD

        swap = [(0, 1), (1, 0)]

        def full_over_dp(local, axis):
            other = lax.ppermute(local, "dp", swap)
            return jnp.where(
                dp_rank == 0,
                jnp.concatenate([local, other], axis=axis),
                jnp.concatenate([other, local], axis=axis),
            )

        query_full = full_over_dp(fast_prune(query_weight, query_keep), 0)
        kv_full = lax.all_gather(kv_weight, "dp", axis=1, tiled=True)
        out_full = fast_prune(
            lax.all_gather(out_weight, "dp", axis=1, tiled=True),
            lax.all_gather(out_keep, "dp", axis=1, tiled=True),
        )

        split = (total_rows // 2 + 7) // 8 * 8
        halves = [hidden[:split], hidden[split:]]
        wholes = []
        for half in halves:
            buf = jnp.zeros((half.shape[0], n * feat), hidden.dtype)
            wholes.append(lax.dynamic_update_slice(buf, half, (0, tensor_rank * feat)))
        moving = list(halves)
        for s in range(n - 1):
            src = ring[(pos - sign * (s + 1)) % n]
            for i in range(2):
                moving[i] = lax.ppermute(moving[i], both, ring_pairs)
                wholes[i] = lax.dynamic_update_slice(wholes[i], moving[i], (0, src * feat))

        offsets, allowed = pair_layout(pair_lengths[0], premise_lengths[0], total_rows)
        low = tensor_rank < n // 2
        even = tensor_rank % 2 == 0
        pairs_a = [(s, 2 * s) if s < n // 2 else (s, 2 * (s - n // 2) + 1) for s in range(n)]
        pairs_b = [(s, 2 * s + 1) if s < n // 2 else (s, 2 * (s - n // 2)) for s in range(n)]
        contract = (((1,), (1,)), ((), ()))
        query_parts, key_parts, value_parts = [], [], []
        for i in range(2):
            rows_float = wholes[i].astype(jnp.float32)
            mean_square = jnp.mean(rows_float * rows_float, axis=-1, keepdims=True)
            normed = (rows_float * lax.rsqrt(mean_square + 1e-05) * norm_gain).astype(jnp.bfloat16)
            query_parts.append(jnp.dot(normed, query_full, preferred_element_type=jnp.float32))
            kv_piece = lax.dot_general(
                normed, kv_full, contract, preferred_element_type=jnp.float32
            ).astype(jnp.bfloat16)
            lo_cols = kv_piece[:, :HD]
            hi_cols = kv_piece[:, HD:]
            got_a = lax.ppermute(jnp.where(low, lo_cols, hi_cols), "tensor", pairs_a)
            got_b = lax.ppermute(jnp.where(low, hi_cols, lo_cols), "tensor", pairs_b)
            key_parts.append(jnp.where(even, got_a, got_b))
            value_parts.append(jnp.where(even, got_b, got_a))
        queries_raw = jnp.concatenate(query_parts, axis=0)
        key_head = jnp.concatenate(key_parts, axis=0)
        value_head = jnp.concatenate(value_parts, axis=0)

        queries = rotate_pairs(queries_raw.reshape(total_rows, head_local, HD), offsets).astype(
            jnp.bfloat16
        )
        keys = rotate_pairs(key_head.astype(jnp.float32)[:, None, :], offsets)[:, 0, :].astype(
            jnp.bfloat16
        )
        scale = HD ** (-0.5)
        starts = [0, split]
        sizes = [split, total_rows - split]

        def context_rows(i, q_rows):
            mask = lax.slice_in_dim(allowed, starts[i], starts[i] + sizes[i], axis=0)
            scores = jnp.einsum("qhd,kd->hqk", q_rows, keys, preferred_element_type=jnp.float32) * scale
            weighted = jnp.where(mask[None, :, :], jnp.exp(scores), 0.0)
            probs = (weighted / jnp.sum(weighted, axis=-1, keepdims=True)).astype(jnp.bfloat16)
            context = jnp.einsum(
                "hqk,kd->qhd", probs, value_head, preferred_element_type=jnp.float32
            ).astype(jnp.bfloat16)
            return context.reshape(sizes[i], head_local * HD)

        def chunk(context, dest_pos):
            cols = lax.dynamic_slice_in_dim(out_full, ring[dest_pos % n] * feat, feat, axis=1)
            return jnp.dot(context, cols, preferred_element_type=jnp.float32)

        parts = []
        for i in range(2):
            q_rows = lax.slice_in_dim(queries, starts[i], starts[i] + sizes[i], axis=0)
            if i > 0:
                q_rows, _ = lax.optimization_barrier((q_rows, parts[0][0]))
            context = context_rows(i, q_rows)
            mine = [chunk(context, pos + sign * (n - 1 - s)) for s in range(n)]
            parts.append([mine[0].astype(jnp.bfloat16)] + lax.optimization_barrier(mine[1:]))
        acc = [None, None]
        for s in range(n - 1):
            for i in range(2):
                if acc[i] is None:
                    send = parts[i][0]
                else:
                    send = (parts[i][s] + acc[i].astype(jnp.float32)).astype(jnp.bfloat16)
                acc[i] = lax.ppermute(send, both, ring_pairs)
        total = jnp.concatenate(
            [parts[i][n - 1] + acc[i].astype(jnp.float32) for i in range(2)], axis=0
        )
        return total.astype(jnp.bfloat16)

    return on_device


def generic(
    hidden,
    norm_gain,
    query_weight,
    query_keep,
    kv_weight,
    out_weight,
    out_keep,
    pair_lengths,
    premise_lengths,
):
    tensor_rank = lax.axis_index("tensor")
    total_rows = hidden.shape[0]
    head_local = query_weight.shape[1] // HD
    query_pruned = prune(query_weight, query_keep)
    out_pruned = prune(out_weight, out_keep)
    query_full = lax.all_gather(query_pruned, "dp", axis=0, tiled=True)
    kv_full, out_full = (
        lax.all_gather(kv_weight, "dp", axis=1, tiled=True),
        lax.all_gather(out_pruned, "dp", axis=1, tiled=True),
    )
    whole = lax.all_gather(hidden, "tensor", axis=1, tiled=True)
    rows_float = whole.astype(jnp.float32)
    mean_square = jnp.mean(rows_float * rows_float, axis=-1, keepdims=True)
    normed = (rows_float * lax.rsqrt(mean_square + 1e-05) * norm_gain).astype(jnp.bfloat16)
    queries_raw = jnp.dot(normed, query_full, preferred_element_type=jnp.float32)
    kv_piece = lax.dot_general(
        normed, kv_full, (((1,), (1,)), ((), ())), preferred_element_type=jnp.float32
    ).astype(jnp.bfloat16)
    kv_whole = lax.all_gather(kv_piece, "tensor", axis=1, tiled=True)
    offsets, allowed = pair_layout(pair_lengths[0], premise_lengths[0], total_rows)
    queries = rotate_pairs(queries_raw.reshape(total_rows, head_local, HD), offsets).astype(
        jnp.bfloat16
    )
    keys_all = rotate_pairs(
        kv_whole[:, : KVH * HD].reshape(total_rows, KVH, HD).astype(jnp.float32), offsets
    ).astype(jnp.bfloat16)
    values_all = kv_whole[:, KVH * HD :].reshape(total_rows, KVH, HD)
    chosen = (tensor_rank * head_local + jnp.arange(head_local, dtype=jnp.int32)) // (HEADS // KVH)
    keys_used = jnp.take(keys_all, chosen, axis=1)
    values_used = jnp.take(values_all, chosen, axis=1)
    scale = HD ** (-0.5)
    scores = (
        jnp.einsum("qhd,khd->hqk", queries, keys_used, preferred_element_type=jnp.float32) * scale
    )
    weighted = jnp.where(allowed[None, :, :], jnp.exp(scores), 0.0)
    probs = (weighted / jnp.sum(weighted, axis=-1, keepdims=True)).astype(jnp.bfloat16)
    context = jnp.einsum(
        "hqk,khd->qhd", probs, values_used, preferred_element_type=jnp.float32
    ).astype(jnp.bfloat16)
    context = context.reshape(total_rows, head_local * HD)
    terms = jnp.dot(context, out_full, preferred_element_type=jnp.float32)
    mixed = lax.psum_scatter(terms, "tensor", scatter_dimension=1, tiled=True)
    return mixed.astype(jnp.bfloat16)


def solution(mesh):
    placed = (
        P(("groups", "dp"), "tensor"),
        P(),
        P("dp", "tensor"),
        P("dp", "tensor"),
        P("tensor", "dp"),
        P("tensor", "dp"),
        P("tensor", "dp"),
        P(("groups", "dp"), None),
        P(("groups", "dp"), None),
    )
    n = mesh.shape["tensor"]
    if n == KVH and mesh.shape["dp"] == 2:
        coords = [getattr(d, "coords", None) for d in mesh.devices.reshape(-1)]
        z_size, x_size = n, 1
        if all(c is not None for c in coords):
            xs = sorted({c[0] for c in coords})
            zs = sorted({c[2] for c in coords})
            if len(xs) * len(zs) == n:
                z_size, x_size = len(zs), len(xs)
        body = make_fast(n, ring_order(z_size, x_size))
    else:
        body = generic
    return jax.shard_map(
        body,
        mesh=mesh,
        in_specs=placed,
        out_specs=P(("groups", "dp"), "tensor"),
        check_vma=False,
    )
```

```python
import jax
import jax.numpy as jnp
import numpy as np
from jax import lax
from jax.sharding import PartitionSpec as P

HEADS = 64
KVH = 8
HD = 128


def rotate_pairs(values, positions):
    half_width = values.shape[-1] // 2
    inverse = 500000.0 ** (-(jnp.arange(half_width, dtype=jnp.float32) * 2.0 / values.shape[-1]))
    angles = positions[:, None] * inverse[None, :]
    cosine = jnp.cos(angles)[:, None, :]
    sine_part = jnp.sin(angles)[:, None, :]
    first_half = values[..., :half_width]
    second_half = values[..., half_width:]
    return jnp.concatenate(
        [
            first_half * cosine - second_half * sine_part,
            second_half * cosine + first_half * sine_part,
        ],
        axis=-1,
    )


def pair_layout(lengths, premise, count):
    pair_ends = jnp.cumsum(lengths)
    pair_starts = pair_ends - lengths
    position = jnp.arange(count, dtype=jnp.int32)
    pair_index = jnp.sum((position[:, None] >= pair_ends[None, :]).astype(jnp.int32), axis=1)
    one_hot = (
        pair_index[:, None] == jnp.arange(lengths.shape[0], dtype=jnp.int32)[None, :]
    ).astype(jnp.int32)
    offset = position - jnp.sum(one_hot * pair_starts[None, :], axis=1)
    premise_used = jnp.minimum(premise, lengths - 1)
    in_premise = offset < jnp.sum(one_hot * premise_used[None, :], axis=1)
    allowed = (pair_index[:, None] == pair_index[None, :]) & (
        in_premise[None, :] | jnp.logical_not(in_premise)[:, None]
    )
    return (offset.astype(jnp.float32), allowed)


def prune(weight, keep):
    blocks = weight.reshape(
        keep.shape[0],
        weight.shape[0] // keep.shape[0],
        keep.shape[1],
        weight.shape[1] // keep.shape[1],
    )
    blocks = blocks * keep.astype(weight.dtype)[:, None, :, None]
    return blocks.reshape(weight.shape)


def ring_order(z_size, x_size):
    if x_size == 1 or z_size == 1:
        return list(range(z_size * x_size))
    cycle = [(z, 0) for z in range(z_size)]
    for step, z in enumerate(range(z_size - 1, -1, -1)):
        xs = list(range(1, x_size))
        cycle += [(z, x) for x in (xs if step % 2 == 0 else xs[::-1])]
    return [z * x_size + x for z, x in cycle]


def fast_prune(weight, keep):
    rows, cols = weight.shape
    step_r, step_c = rows // keep.shape[0], cols // keep.shape[1]
    mask = jnp.repeat(keep.astype(weight.dtype), step_c, axis=1)
    return (weight.reshape(keep.shape[0], step_r, cols) * mask[:, None, :]).reshape(rows, cols)


def make_fast(n, order):
    position_of = np.zeros(n, np.int32)
    for p, t in enumerate(order):
        position_of[t] = p
    order_arr = np.asarray(order, np.int32)
    both = ("tensor", "dp")
    ring_pairs = [(order[i] * 2, order[(i + 1) % n] * 2) for i in range(n)] + [
        (order[i] * 2 + 1, order[(i - 1) % n] * 2 + 1) for i in range(n)
    ]

    def on_device(
        hidden,
        norm_gain,
        query_weight,
        query_keep,
        kv_weight,
        out_weight,
        out_keep,
        pair_lengths,
        premise_lengths,
    ):
        tensor_rank = lax.axis_index("tensor")
        dp_rank = lax.axis_index("dp")
        pos = jnp.asarray(position_of)[tensor_rank]
        ring = jnp.asarray(order_arr)
        sign = 1 - 2 * dp_rank
        total_rows, feat = hidden.shape
        head_local = query_weight.shape[1] // HD

        swap = [(0, 1), (1, 0)]

        def full_over_dp(local, axis):
            other = lax.ppermute(local, "dp", swap)
            return jnp.where(
                dp_rank == 0,
                jnp.concatenate([local, other], axis=axis),
                jnp.concatenate([other, local], axis=axis),
            )

        query_full = fast_prune(full_over_dp(query_weight, 0), full_over_dp(query_keep, 0))
        kv_full = lax.all_gather(kv_weight, "dp", axis=1, tiled=True)
        out_full = fast_prune(
            lax.all_gather(out_weight, "dp", axis=1, tiled=True),
            lax.all_gather(out_keep, "dp", axis=1, tiled=True),
        )

        split = (total_rows // 2 + 7) // 8 * 8
        moving = [hidden[:split], hidden[split:]]
        arrived = [[moving[0]], [moving[1]]]
        sources = [tensor_rank]
        for s in range(n - 1):
            sources.append(ring[(pos - sign * (s + 1)) % n])
            for i in range(2):
                moving[i] = lax.ppermute(moving[i], both, ring_pairs)
                arrived[i].append(moving[i])
        wholes = [jnp.concatenate(arrived[i], axis=1) for i in range(2)]
        norm_gain = jnp.concatenate(
            [lax.dynamic_slice_in_dim(norm_gain, src * feat, feat) for src in sources]
        )
        query_full = jnp.concatenate(
            [lax.dynamic_slice_in_dim(query_full, src * feat, feat, axis=0) for src in sources],
            axis=0,
        )
        kv_full = jnp.concatenate(
            [lax.dynamic_slice_in_dim(kv_full, src * feat, feat, axis=1) for src in sources],
            axis=1,
        )

        offsets, allowed = pair_layout(pair_lengths[0], premise_lengths[0], total_rows)
        low = tensor_rank < n // 2
        even = tensor_rank % 2 == 0
        pairs_a = [(s, 2 * s) if s < n // 2 else (s, 2 * (s - n // 2) + 1) for s in range(n)]
        pairs_b = [(s, 2 * s + 1) if s < n // 2 else (s, 2 * (s - n // 2)) for s in range(n)]
        contract = (((1,), (1,)), ((), ()))
        query_parts, key_parts, value_parts = [], [], []
        for i in range(2):
            rows_float = wholes[i].astype(jnp.float32)
            mean_square = jnp.mean(rows_float * rows_float, axis=-1, keepdims=True)
            normed = (rows_float * lax.rsqrt(mean_square + 1e-05) * norm_gain).astype(jnp.bfloat16)
            query_parts.append(jnp.dot(normed, query_full, preferred_element_type=jnp.float32))
            kv_piece = lax.dot_general(
                normed, kv_full, contract, preferred_element_type=jnp.float32
            ).astype(jnp.bfloat16)
            lo_cols = kv_piece[:, :HD]
            hi_cols = kv_piece[:, HD:]
            got_a = lax.ppermute(jnp.where(low, lo_cols, hi_cols), "tensor", pairs_a)
            got_b = lax.ppermute(jnp.where(low, hi_cols, lo_cols), "tensor", pairs_b)
            key_parts.append(jnp.where(even, got_a, got_b))
            value_parts.append(jnp.where(even, got_b, got_a))
        queries_raw = jnp.concatenate(query_parts, axis=0)
        key_head = jnp.concatenate(key_parts, axis=0)
        value_head = jnp.concatenate(value_parts, axis=0)

        queries = rotate_pairs(queries_raw.reshape(total_rows, head_local, HD), offsets).astype(
            jnp.bfloat16
        )
        keys = rotate_pairs(key_head.astype(jnp.float32)[:, None, :], offsets)[:, 0, :].astype(
            jnp.bfloat16
        )
        scale = HD ** (-0.5)
        starts = [0, split]
        sizes = [split, total_rows - split]

        def context_rows(i, q_rows):
            mask = lax.slice_in_dim(allowed, starts[i], starts[i] + sizes[i], axis=0)
            scores = jnp.einsum("qhd,kd->hqk", q_rows, keys, preferred_element_type=jnp.float32) * scale
            weighted = jnp.where(mask[None, :, :], jnp.exp(scores), 0.0)
            probs = (weighted / jnp.sum(weighted, axis=-1, keepdims=True)).astype(jnp.bfloat16)
            context = jnp.einsum(
                "hqk,kd->qhd", probs, value_head, preferred_element_type=jnp.float32
            ).astype(jnp.bfloat16)
            return context.reshape(sizes[i], head_local * HD)

        def chunk(context, dest_pos):
            cols = lax.dynamic_slice_in_dim(out_full, ring[dest_pos % n] * feat, feat, axis=1)
            return jnp.dot(context, cols, preferred_element_type=jnp.float32)

        parts = []
        for i in range(2):
            q_rows = lax.slice_in_dim(queries, starts[i], starts[i] + sizes[i], axis=0)
            if i > 0:
                q_rows, _ = lax.optimization_barrier((q_rows, parts[0][0]))
            context = context_rows(i, q_rows)
            mine = [chunk(context, pos + sign * (n - 1 - s)) for s in range(n)]
            parts.append([mine[0].astype(jnp.bfloat16)] + lax.optimization_barrier(mine[1:]))
        acc = [None, None]
        for s in range(n - 1):
            for i in range(2):
                if acc[i] is None:
                    send = parts[i][0]
                else:
                    send = (parts[i][s] + acc[i].astype(jnp.float32)).astype(jnp.bfloat16)
                acc[i] = lax.ppermute(send, both, ring_pairs)
        total = jnp.concatenate(
            [parts[i][n - 1] + acc[i].astype(jnp.float32) for i in range(2)], axis=0
        )
        return total.astype(jnp.bfloat16)

    return on_device


def generic(
    hidden,
    norm_gain,
    query_weight,
    query_keep,
    kv_weight,
    out_weight,
    out_keep,
    pair_lengths,
    premise_lengths,
):
    tensor_rank = lax.axis_index("tensor")
    total_rows = hidden.shape[0]
    head_local = query_weight.shape[1] // HD
    query_pruned = prune(query_weight, query_keep)
    out_pruned = prune(out_weight, out_keep)
    query_full = lax.all_gather(query_pruned, "dp", axis=0, tiled=True)
    kv_full, out_full = (
        lax.all_gather(kv_weight, "dp", axis=1, tiled=True),
        lax.all_gather(out_pruned, "dp", axis=1, tiled=True),
    )
    whole = lax.all_gather(hidden, "tensor", axis=1, tiled=True)
    rows_float = whole.astype(jnp.float32)
    mean_square = jnp.mean(rows_float * rows_float, axis=-1, keepdims=True)
    normed = (rows_float * lax.rsqrt(mean_square + 1e-05) * norm_gain).astype(jnp.bfloat16)
    queries_raw = jnp.dot(normed, query_full, preferred_element_type=jnp.float32)
    kv_piece = lax.dot_general(
        normed, kv_full, (((1,), (1,)), ((), ())), preferred_element_type=jnp.float32
    ).astype(jnp.bfloat16)
    kv_whole = lax.all_gather(kv_piece, "tensor", axis=1, tiled=True)
    offsets, allowed = pair_layout(pair_lengths[0], premise_lengths[0], total_rows)
    queries = rotate_pairs(queries_raw.reshape(total_rows, head_local, HD), offsets).astype(
        jnp.bfloat16
    )
    keys_all = rotate_pairs(
        kv_whole[:, : KVH * HD].reshape(total_rows, KVH, HD).astype(jnp.float32), offsets
    ).astype(jnp.bfloat16)
    values_all = kv_whole[:, KVH * HD :].reshape(total_rows, KVH, HD)
    chosen = (tensor_rank * head_local + jnp.arange(head_local, dtype=jnp.int32)) // (HEADS // KVH)
    keys_used = jnp.take(keys_all, chosen, axis=1)
    values_used = jnp.take(values_all, chosen, axis=1)
    scale = HD ** (-0.5)
    scores = (
        jnp.einsum("qhd,khd->hqk", queries, keys_used, preferred_element_type=jnp.float32) * scale
    )
    weighted = jnp.where(allowed[None, :, :], jnp.exp(scores), 0.0)
    probs = (weighted / jnp.sum(weighted, axis=-1, keepdims=True)).astype(jnp.bfloat16)
    context = jnp.einsum(
        "hqk,khd->qhd", probs, values_used, preferred_element_type=jnp.float32
    ).astype(jnp.bfloat16)
    context = context.reshape(total_rows, head_local * HD)
    terms = jnp.dot(context, out_full, preferred_element_type=jnp.float32)
    mixed = lax.psum_scatter(terms, "tensor", scatter_dimension=1, tiled=True)
    return mixed.astype(jnp.bfloat16)


def solution(mesh):
    placed = (
        P(("groups", "dp"), "tensor"),
        P(),
        P("dp", "tensor"),
        P("dp", "tensor"),
        P("tensor", "dp"),
        P("tensor", "dp"),
        P("tensor", "dp"),
        P(("groups", "dp"), None),
        P(("groups", "dp"), None),
    )
    n = mesh.shape["tensor"]
    if n == KVH and mesh.shape["dp"] == 2:
        coords = [getattr(d, "coords", None) for d in mesh.devices.reshape(-1)]
        z_size, x_size = n, 1
        if all(c is not None for c in coords):
            xs = sorted({c[0] for c in coords})
            zs = sorted({c[2] for c in coords})
            if len(xs) * len(zs) == n:
                z_size, x_size = len(zs), len(xs)
        body = make_fast(n, ring_order(z_size, x_size))
    else:
        body = generic
    return jax.shard_map(
        body,
        mesh=mesh,
        in_specs=placed,
        out_specs=P(("groups", "dp"), "tensor"),
        check_vma=False,
    )
```

```python
import jax
import jax.numpy as jnp
import numpy as np
from jax import lax
from jax.sharding import PartitionSpec as P

HEADS = 64
KVH = 8
HD = 128


def rotate_pairs(values, positions):
    half_width = values.shape[-1] // 2
    inverse = 500000.0 ** (-(jnp.arange(half_width, dtype=jnp.float32) * 2.0 / values.shape[-1]))
    angles = positions[:, None] * inverse[None, :]
    cosine = jnp.cos(angles)[:, None, :]
    sine_part = jnp.sin(angles)[:, None, :]
    first_half = values[..., :half_width]
    second_half = values[..., half_width:]
    return jnp.concatenate(
        [
            first_half * cosine - second_half * sine_part,
            second_half * cosine + first_half * sine_part,
        ],
        axis=-1,
    )


def pair_layout(lengths, premise, count):
    pair_ends = jnp.cumsum(lengths)
    pair_starts = pair_ends - lengths
    position = jnp.arange(count, dtype=jnp.int32)
    pair_index = jnp.sum((position[:, None] >= pair_ends[None, :]).astype(jnp.int32), axis=1)
    one_hot = (
        pair_index[:, None] == jnp.arange(lengths.shape[0], dtype=jnp.int32)[None, :]
    ).astype(jnp.int32)
    offset = position - jnp.sum(one_hot * pair_starts[None, :], axis=1)
    premise_used = jnp.minimum(premise, lengths - 1)
    in_premise = offset < jnp.sum(one_hot * premise_used[None, :], axis=1)
    allowed = (pair_index[:, None] == pair_index[None, :]) & (
        in_premise[None, :] | jnp.logical_not(in_premise)[:, None]
    )
    return (offset.astype(jnp.float32), allowed)


def prune(weight, keep):
    blocks = weight.reshape(
        keep.shape[0],
        weight.shape[0] // keep.shape[0],
        keep.shape[1],
        weight.shape[1] // keep.shape[1],
    )
    blocks = blocks * keep.astype(weight.dtype)[:, None, :, None]
    return blocks.reshape(weight.shape)


def ring_order(z_size, x_size):
    if x_size == 1 or z_size == 1:
        return list(range(z_size * x_size))
    cycle = [(z, 0) for z in range(z_size)]
    for step, z in enumerate(range(z_size - 1, -1, -1)):
        xs = list(range(1, x_size))
        cycle += [(z, x) for x in (xs if step % 2 == 0 else xs[::-1])]
    return [z * x_size + x for z, x in cycle]


def fast_prune(weight, keep):
    rows, cols = weight.shape
    step_r, step_c = rows // keep.shape[0], cols // keep.shape[1]
    mask = jnp.repeat(keep.astype(weight.dtype), step_c, axis=1)
    return (weight.reshape(keep.shape[0], step_r, cols) * mask[:, None, :]).reshape(rows, cols)


def make_fast(n, order):
    position_of = np.zeros(n, np.int32)
    for p, t in enumerate(order):
        position_of[t] = p
    order_arr = np.asarray(order, np.int32)
    both = ("tensor", "dp")
    ring_pairs = [(order[i] * 2, order[(i + 1) % n] * 2) for i in range(n)] + [
        (order[i] * 2 + 1, order[(i - 1) % n] * 2 + 1) for i in range(n)
    ]

    def on_device(
        hidden,
        norm_gain,
        query_weight,
        query_keep,
        kv_weight,
        out_weight,
        out_keep,
        pair_lengths,
        premise_lengths,
    ):
        tensor_rank = lax.axis_index("tensor")
        dp_rank = lax.axis_index("dp")
        pos = jnp.asarray(position_of)[tensor_rank]
        ring = jnp.asarray(order_arr)
        sign = 1 - 2 * dp_rank
        total_rows, feat = hidden.shape
        head_local = query_weight.shape[1] // HD

        swap = [(0, 1), (1, 0)]

        def full_over_dp(local, axis):
            other = lax.ppermute(local, "dp", swap)
            return jnp.where(
                dp_rank == 0,
                jnp.concatenate([local, other], axis=axis),
                jnp.concatenate([other, local], axis=axis),
            )

        query_full = fast_prune(full_over_dp(query_weight, 0), full_over_dp(query_keep, 0))
        kv_full = lax.all_gather(kv_weight, "dp", axis=1, tiled=True)
        out_full = fast_prune(
            lax.all_gather(out_weight, "dp", axis=1, tiled=True),
            full_over_dp(out_keep, 1),
        )

        split = (total_rows // 2 + 7) // 8 * 8
        halves = [hidden[:split], hidden[split:]]
        wholes = []
        for half in halves:
            buf = jnp.zeros((half.shape[0], n * feat), hidden.dtype)
            wholes.append(lax.dynamic_update_slice(buf, half, (0, tensor_rank * feat)))
        moving = list(halves)
        for s in range(n - 1):
            src = ring[(pos - sign * (s + 1)) % n]
            for i in range(2):
                moving[i] = lax.ppermute(moving[i], both, ring_pairs)
                wholes[i] = lax.dynamic_update_slice(wholes[i], moving[i], (0, src * feat))

        offsets, allowed = pair_layout(pair_lengths[0], premise_lengths[0], total_rows)
        low = tensor_rank < n // 2
        even = tensor_rank % 2 == 0
        pairs_a = [(s, 2 * s) if s < n // 2 else (s, 2 * (s - n // 2) + 1) for s in range(n)]
        pairs_b = [(s, 2 * s + 1) if s < n // 2 else (s, 2 * (s - n // 2)) for s in range(n)]
        contract = (((1,), (1,)), ((), ()))
        query_parts, key_parts, value_parts = [], [], []
        for i in range(2):
            rows_float = wholes[i].astype(jnp.float32)
            mean_square = jnp.mean(rows_float * rows_float, axis=-1, keepdims=True)
            normed = (rows_float * lax.rsqrt(mean_square + 1e-05) * norm_gain).astype(jnp.bfloat16)
            query_parts.append(jnp.dot(normed, query_full, preferred_element_type=jnp.float32))
            kv_piece = lax.dot_general(
                normed, kv_full, contract, preferred_element_type=jnp.float32
            ).astype(jnp.bfloat16)
            lo_cols = kv_piece[:, :HD]
            hi_cols = kv_piece[:, HD:]
            got_a = lax.ppermute(jnp.where(low, lo_cols, hi_cols), "tensor", pairs_a)
            got_b = lax.ppermute(jnp.where(low, hi_cols, lo_cols), "tensor", pairs_b)
            key_parts.append(jnp.where(even, got_a, got_b))
            value_parts.append(jnp.where(even, got_b, got_a))
        queries_raw = jnp.concatenate(query_parts, axis=0)
        key_head = jnp.concatenate(key_parts, axis=0)
        value_head = jnp.concatenate(value_parts, axis=0)

        queries = rotate_pairs(queries_raw.reshape(total_rows, head_local, HD), offsets).astype(
            jnp.bfloat16
        )
        keys = rotate_pairs(key_head.astype(jnp.float32)[:, None, :], offsets)[:, 0, :].astype(
            jnp.bfloat16
        )
        scale = HD ** (-0.5)
        starts = [0, split]
        sizes = [split, total_rows - split]

        def context_rows(i, q_rows):
            mask = lax.slice_in_dim(allowed, starts[i], starts[i] + sizes[i], axis=0)
            scores = jnp.einsum("qhd,kd->hqk", q_rows, keys, preferred_element_type=jnp.float32) * scale
            weighted = jnp.where(mask[None, :, :], jnp.exp(scores), 0.0)
            probs = (weighted / jnp.sum(weighted, axis=-1, keepdims=True)).astype(jnp.bfloat16)
            context = jnp.einsum(
                "hqk,kd->qhd", probs, value_head, preferred_element_type=jnp.float32
            ).astype(jnp.bfloat16)
            return context.reshape(sizes[i], head_local * HD)

        def chunk(context, dest_pos):
            cols = lax.dynamic_slice_in_dim(out_full, ring[dest_pos % n] * feat, feat, axis=1)
            return jnp.dot(context, cols, preferred_element_type=jnp.float32)

        parts = []
        for i in range(2):
            q_rows = lax.slice_in_dim(queries, starts[i], starts[i] + sizes[i], axis=0)
            if i > 0:
                q_rows, _ = lax.optimization_barrier((q_rows, parts[0][0]))
            context = context_rows(i, q_rows)
            mine = [chunk(context, pos + sign * (n - 1 - s)) for s in range(n)]
            parts.append([mine[0].astype(jnp.bfloat16)] + lax.optimization_barrier(mine[1:]))
        acc = [None, None]
        for s in range(n - 1):
            for i in range(2):
                if acc[i] is None:
                    send = parts[i][0]
                else:
                    send = (parts[i][s] + acc[i].astype(jnp.float32)).astype(jnp.bfloat16)
                acc[i] = lax.ppermute(send, both, ring_pairs)
        total = jnp.concatenate(
            [parts[i][n - 1] + acc[i].astype(jnp.float32) for i in range(2)], axis=0
        )
        return total.astype(jnp.bfloat16)

    return on_device


def generic(
    hidden,
    norm_gain,
    query_weight,
    query_keep,
    kv_weight,
    out_weight,
    out_keep,
    pair_lengths,
    premise_lengths,
):
    tensor_rank = lax.axis_index("tensor")
    total_rows = hidden.shape[0]
    head_local = query_weight.shape[1] // HD
    query_pruned = prune(query_weight, query_keep)
    out_pruned = prune(out_weight, out_keep)
    query_full = lax.all_gather(query_pruned, "dp", axis=0, tiled=True)
    kv_full, out_full = (
        lax.all_gather(kv_weight, "dp", axis=1, tiled=True),
        lax.all_gather(out_pruned, "dp", axis=1, tiled=True),
    )
    whole = lax.all_gather(hidden, "tensor", axis=1, tiled=True)
    rows_float = whole.astype(jnp.float32)
    mean_square = jnp.mean(rows_float * rows_float, axis=-1, keepdims=True)
    normed = (rows_float * lax.rsqrt(mean_square + 1e-05) * norm_gain).astype(jnp.bfloat16)
    queries_raw = jnp.dot(normed, query_full, preferred_element_type=jnp.float32)
    kv_piece = lax.dot_general(
        normed, kv_full, (((1,), (1,)), ((), ())), preferred_element_type=jnp.float32
    ).astype(jnp.bfloat16)
    kv_whole = lax.all_gather(kv_piece, "tensor", axis=1, tiled=True)
    offsets, allowed = pair_layout(pair_lengths[0], premise_lengths[0], total_rows)
    queries = rotate_pairs(queries_raw.reshape(total_rows, head_local, HD), offsets).astype(
        jnp.bfloat16
    )
    keys_all = rotate_pairs(
        kv_whole[:, : KVH * HD].reshape(total_rows, KVH, HD).astype(jnp.float32), offsets
    ).astype(jnp.bfloat16)
    values_all = kv_whole[:, KVH * HD :].reshape(total_rows, KVH, HD)
    chosen = (tensor_rank * head_local + jnp.arange(head_local, dtype=jnp.int32)) // (HEADS // KVH)
    keys_used = jnp.take(keys_all, chosen, axis=1)
    values_used = jnp.take(values_all, chosen, axis=1)
    scale = HD ** (-0.5)
    scores = (
        jnp.einsum("qhd,khd->hqk", queries, keys_used, preferred_element_type=jnp.float32) * scale
    )
    weighted = jnp.where(allowed[None, :, :], jnp.exp(scores), 0.0)
    probs = (weighted / jnp.sum(weighted, axis=-1, keepdims=True)).astype(jnp.bfloat16)
    context = jnp.einsum(
        "hqk,khd->qhd", probs, values_used, preferred_element_type=jnp.float32
    ).astype(jnp.bfloat16)
    context = context.reshape(total_rows, head_local * HD)
    terms = jnp.dot(context, out_full, preferred_element_type=jnp.float32)
    mixed = lax.psum_scatter(terms, "tensor", scatter_dimension=1, tiled=True)
    return mixed.astype(jnp.bfloat16)


def solution(mesh):
    placed = (
        P(("groups", "dp"), "tensor"),
        P(),
        P("dp", "tensor"),
        P("dp", "tensor"),
        P("tensor", "dp"),
        P("tensor", "dp"),
        P("tensor", "dp"),
        P(("groups", "dp"), None),
        P(("groups", "dp"), None),
    )
    n = mesh.shape["tensor"]
    if n == KVH and mesh.shape["dp"] == 2:
        coords = [getattr(d, "coords", None) for d in mesh.devices.reshape(-1)]
        z_size, x_size = n, 1
        if all(c is not None for c in coords):
            xs = sorted({c[0] for c in coords})
            zs = sorted({c[2] for c in coords})
            if len(xs) * len(zs) == n:
                z_size, x_size = len(zs), len(xs)
        body = make_fast(n, ring_order(z_size, x_size))
    else:
        body = generic
    return jax.shard_map(
        body,
        mesh=mesh,
        in_specs=placed,
        out_specs=P(("groups", "dp"), "tensor"),
        check_vma=False,
    )
```

```python
import jax
import jax.numpy as jnp
import numpy as np
from jax import lax
from jax.sharding import PartitionSpec as P

HEADS = 64
KVH = 8
HD = 128


def rotate_pairs(values, positions):
    half_width = values.shape[-1] // 2
    inverse = 500000.0 ** (-(jnp.arange(half_width, dtype=jnp.float32) * 2.0 / values.shape[-1]))
    angles = positions[:, None] * inverse[None, :]
    cosine = jnp.cos(angles)[:, None, :]
    sine_part = jnp.sin(angles)[:, None, :]
    first_half = values[..., :half_width]
    second_half = values[..., half_width:]
    return jnp.concatenate(
        [
            first_half * cosine - second_half * sine_part,
            second_half * cosine + first_half * sine_part,
        ],
        axis=-1,
    )


def pair_layout(lengths, premise, count):
    pair_ends = jnp.cumsum(lengths)
    pair_starts = pair_ends - lengths
    position = jnp.arange(count, dtype=jnp.int32)
    pair_index = jnp.sum((position[:, None] >= pair_ends[None, :]).astype(jnp.int32), axis=1)
    one_hot = (
        pair_index[:, None] == jnp.arange(lengths.shape[0], dtype=jnp.int32)[None, :]
    ).astype(jnp.int32)
    offset = position - jnp.sum(one_hot * pair_starts[None, :], axis=1)
    premise_used = jnp.minimum(premise, lengths - 1)
    in_premise = offset < jnp.sum(one_hot * premise_used[None, :], axis=1)
    allowed = (pair_index[:, None] == pair_index[None, :]) & (
        in_premise[None, :] | jnp.logical_not(in_premise)[:, None]
    )
    return (offset.astype(jnp.float32), allowed)


def prune(weight, keep):
    blocks = weight.reshape(
        keep.shape[0],
        weight.shape[0] // keep.shape[0],
        keep.shape[1],
        weight.shape[1] // keep.shape[1],
    )
    blocks = blocks * keep.astype(weight.dtype)[:, None, :, None]
    return blocks.reshape(weight.shape)


def ring_order(z_size, x_size):
    if x_size == 1 or z_size == 1:
        return list(range(z_size * x_size))
    cycle = [(z, 0) for z in range(z_size)]
    for step, z in enumerate(range(z_size - 1, -1, -1)):
        xs = list(range(1, x_size))
        cycle += [(z, x) for x in (xs if step % 2 == 0 else xs[::-1])]
    return [z * x_size + x for z, x in cycle]


def fast_prune(weight, keep):
    rows, cols = weight.shape
    step_r, step_c = rows // keep.shape[0], cols // keep.shape[1]
    mask = jnp.repeat(keep.astype(weight.dtype), step_c, axis=1)
    return (weight.reshape(keep.shape[0], step_r, cols) * mask[:, None, :]).reshape(rows, cols)


def make_fast(n, order):
    position_of = np.zeros(n, np.int32)
    for p, t in enumerate(order):
        position_of[t] = p
    order_arr = np.asarray(order, np.int32)
    both = ("tensor", "dp")
    ring_pairs = [(order[i] * 2, order[(i + 1) % n] * 2) for i in range(n)] + [
        (order[i] * 2 + 1, order[(i - 1) % n] * 2 + 1) for i in range(n)
    ]

    def on_device(
        hidden,
        norm_gain,
        query_weight,
        query_keep,
        kv_weight,
        out_weight,
        out_keep,
        pair_lengths,
        premise_lengths,
    ):
        tensor_rank = lax.axis_index("tensor")
        dp_rank = lax.axis_index("dp")
        pos = jnp.asarray(position_of)[tensor_rank]
        ring = jnp.asarray(order_arr)
        sign = 1 - 2 * dp_rank
        total_rows, feat = hidden.shape
        head_local = query_weight.shape[1] // HD

        swap = [(0, 1), (1, 0)]

        def full_over_dp(local, axis):
            other = lax.ppermute(local, "dp", swap)
            return jnp.where(
                dp_rank == 0,
                jnp.concatenate([local, other], axis=axis),
                jnp.concatenate([other, local], axis=axis),
            )

        query_full = fast_prune(full_over_dp(query_weight, 0), full_over_dp(query_keep, 0))
        kv_full = lax.all_gather(kv_weight, "dp", axis=1, tiled=True)
        out_full = lax.all_gather(fast_prune(out_weight, out_keep), "dp", axis=1, tiled=True)

        split = (total_rows // 2 + 7) // 8 * 8
        halves = [hidden[:split], hidden[split:]]
        wholes = []
        for half in halves:
            buf = jnp.zeros((half.shape[0], n * feat), hidden.dtype)
            wholes.append(lax.dynamic_update_slice(buf, half, (0, tensor_rank * feat)))
        moving = list(halves)
        for s in range(n - 1):
            src = ring[(pos - sign * (s + 1)) % n]
            for i in range(2):
                moving[i] = lax.ppermute(moving[i], both, ring_pairs)
                wholes[i] = lax.dynamic_update_slice(wholes[i], moving[i], (0, src * feat))

        offsets, allowed = pair_layout(pair_lengths[0], premise_lengths[0], total_rows)
        low = tensor_rank < n // 2
        even = tensor_rank % 2 == 0
        pairs_a = [(s, 2 * s) if s < n // 2 else (s, 2 * (s - n // 2) + 1) for s in range(n)]
        pairs_b = [(s, 2 * s + 1) if s < n // 2 else (s, 2 * (s - n // 2)) for s in range(n)]
        contract = (((1,), (1,)), ((), ()))
        query_parts, key_parts, value_parts = [], [], []
        for i in range(2):
            rows_float = wholes[i].astype(jnp.float32)
            mean_square = jnp.mean(rows_float * rows_float, axis=-1, keepdims=True)
            normed = (rows_float * lax.rsqrt(mean_square + 1e-05) * norm_gain).astype(jnp.bfloat16)
            query_parts.append(jnp.dot(normed, query_full, preferred_element_type=jnp.float32))
            kv_piece = lax.dot_general(
                normed, kv_full, contract, preferred_element_type=jnp.float32
            ).astype(jnp.bfloat16)
            lo_cols = kv_piece[:, :HD]
            hi_cols = kv_piece[:, HD:]
            got_a = lax.ppermute(jnp.where(low, lo_cols, hi_cols), "tensor", pairs_a)
            got_b = lax.ppermute(jnp.where(low, hi_cols, lo_cols), "tensor", pairs_b)
            key_parts.append(jnp.where(even, got_a, got_b))
            value_parts.append(jnp.where(even, got_b, got_a))
        queries_raw = jnp.concatenate(query_parts, axis=0)
        key_head = jnp.concatenate(key_parts, axis=0)
        value_head = jnp.concatenate(value_parts, axis=0)

        queries = rotate_pairs(queries_raw.reshape(total_rows, head_local, HD), offsets).astype(
            jnp.bfloat16
        )
        keys = rotate_pairs(key_head.astype(jnp.float32)[:, None, :], offsets)[:, 0, :].astype(
            jnp.bfloat16
        )
        scale = HD ** (-0.5)
        starts = [0, split]
        sizes = [split, total_rows - split]

        def context_rows(i, q_rows):
            mask = lax.slice_in_dim(allowed, starts[i], starts[i] + sizes[i], axis=0)
            scores = jnp.einsum("qhd,kd->hqk", q_rows, keys, preferred_element_type=jnp.float32) * scale
            weighted = jnp.where(mask[None, :, :], jnp.exp(scores), 0.0)
            probs = (weighted / jnp.sum(weighted, axis=-1, keepdims=True)).astype(jnp.bfloat16)
            context = jnp.einsum(
                "hqk,kd->qhd", probs, value_head, preferred_element_type=jnp.float32
            ).astype(jnp.bfloat16)
            return context.reshape(sizes[i], head_local * HD)

        def chunk(context, dest_pos):
            cols = lax.dynamic_slice_in_dim(out_full, ring[dest_pos % n] * feat, feat, axis=1)
            return jnp.dot(context, cols, preferred_element_type=jnp.float32)

        parts = []
        for i in range(2):
            q_rows = lax.slice_in_dim(queries, starts[i], starts[i] + sizes[i], axis=0)
            if i > 0:
                q_rows, _ = lax.optimization_barrier((q_rows, parts[0][0]))
            context = context_rows(i, q_rows)
            mine = [chunk(context, pos + sign * (n - 1 - s)) for s in range(n)]
            parts.append([mine[0].astype(jnp.bfloat16)] + lax.optimization_barrier(mine[1:]))
        acc = [None, None]
        for s in range(n - 1):
            for i in range(2):
                if acc[i] is None:
                    send = parts[i][0]
                else:
                    send = (parts[i][s] + acc[i].astype(jnp.float32)).astype(jnp.bfloat16)
                acc[i] = lax.ppermute(send, both, ring_pairs)
        total = jnp.concatenate(
            [parts[i][n - 1] + acc[i].astype(jnp.float32) for i in range(2)], axis=0
        )
        return total.astype(jnp.bfloat16)

    return on_device


def generic(
    hidden,
    norm_gain,
    query_weight,
    query_keep,
    kv_weight,
    out_weight,
    out_keep,
    pair_lengths,
    premise_lengths,
):
    tensor_rank = lax.axis_index("tensor")
    total_rows = hidden.shape[0]
    head_local = query_weight.shape[1] // HD
    query_pruned = prune(query_weight, query_keep)
    out_pruned = prune(out_weight, out_keep)
    query_full = lax.all_gather(query_pruned, "dp", axis=0, tiled=True)
    kv_full, out_full = (
        lax.all_gather(kv_weight, "dp", axis=1, tiled=True),
        lax.all_gather(out_pruned, "dp", axis=1, tiled=True),
    )
    whole = lax.all_gather(hidden, "tensor", axis=1, tiled=True)
    rows_float = whole.astype(jnp.float32)
    mean_square = jnp.mean(rows_float * rows_float, axis=-1, keepdims=True)
    normed = (rows_float * lax.rsqrt(mean_square + 1e-05) * norm_gain).astype(jnp.bfloat16)
    queries_raw = jnp.dot(normed, query_full, preferred_element_type=jnp.float32)
    kv_piece = lax.dot_general(
        normed, kv_full, (((1,), (1,)), ((), ())), preferred_element_type=jnp.float32
    ).astype(jnp.bfloat16)
    kv_whole = lax.all_gather(kv_piece, "tensor", axis=1, tiled=True)
    offsets, allowed = pair_layout(pair_lengths[0], premise_lengths[0], total_rows)
    queries = rotate_pairs(queries_raw.reshape(total_rows, head_local, HD), offsets).astype(
        jnp.bfloat16
    )
    keys_all = rotate_pairs(
        kv_whole[:, : KVH * HD].reshape(total_rows, KVH, HD).astype(jnp.float32), offsets
    ).astype(jnp.bfloat16)
    values_all = kv_whole[:, KVH * HD :].reshape(total_rows, KVH, HD)
    chosen = (tensor_rank * head_local + jnp.arange(head_local, dtype=jnp.int32)) // (HEADS // KVH)
    keys_used = jnp.take(keys_all, chosen, axis=1)
    values_used = jnp.take(values_all, chosen, axis=1)
    scale = HD ** (-0.5)
    scores = (
        jnp.einsum("qhd,khd->hqk", queries, keys_used, preferred_element_type=jnp.float32) * scale
    )
    weighted = jnp.where(allowed[None, :, :], jnp.exp(scores), 0.0)
    probs = (weighted / jnp.sum(weighted, axis=-1, keepdims=True)).astype(jnp.bfloat16)
    context = jnp.einsum(
        "hqk,khd->qhd", probs, values_used, preferred_element_type=jnp.float32
    ).astype(jnp.bfloat16)
    context = context.reshape(total_rows, head_local * HD)
    terms = jnp.dot(context, out_full, preferred_element_type=jnp.float32)
    mixed = lax.psum_scatter(terms, "tensor", scatter_dimension=1, tiled=True)
    return mixed.astype(jnp.bfloat16)


def solution(mesh):
    placed = (
        P(("groups", "dp"), "tensor"),
        P(),
        P("dp", "tensor"),
        P("dp", "tensor"),
        P("tensor", "dp"),
        P("tensor", "dp"),
        P("tensor", "dp"),
        P(("groups", "dp"), None),
        P(("groups", "dp"), None),
    )
    n = mesh.shape["tensor"]
    if n == KVH and mesh.shape["dp"] == 2:
        coords = [getattr(d, "coords", None) for d in mesh.devices.reshape(-1)]
        z_size, x_size = n, 1
        if all(c is not None for c in coords):
            xs = sorted({c[0] for c in coords})
            zs = sorted({c[2] for c in coords})
            if len(xs) * len(zs) == n:
                z_size, x_size = len(zs), len(xs)
        body = make_fast(n, ring_order(z_size, x_size))
    else:
        body = generic
    return jax.shard_map(
        body,
        mesh=mesh,
        in_specs=placed,
        out_specs=P(("groups", "dp"), "tensor"),
        check_vma=False,
    )
```
